32 devices in a mesh: gx: 4 (over y, x), gy: 2 (over core), gz: 4 (over z).
Axes of the slice: x: 2, y: 2, z: 4, core: 2. Of those that a mesh axis runs over, the one named last changes fastest.
Arguments:
- features: bfloat16 [8, 32, 65536], P('gz', 'gy', 'gx'), may hold values from -6 to 6
- depth_weight: bfloat16 [27, 64], replicated, may hold values from -1.25 to 1.25
- expand_weight: bfloat16 [64, 256], replicated, may hold values from -0.75 to 0.75
- project_weight: bfloat16 [256, 64], replicated, may hold values from -0.375 to 0.375
- spec_real: bfloat16 [32, 64, 64], replicated, may hold values from -2 to 2
- spec_imag: bfloat16 [32, 64, 64], replicated, may hold values from -2 to 2
- cotangent: bfloat16 [8, 32, 65536], P('gz', 'gy', 'gx'), may hold values from -6 to 6
Outputs:
- output: bfloat16 [8, 32, 65536], P('gz', 'gy', 'gx')
- grad_features: bfloat16 [8, 32, 65536], P('gz', 'gy', 'gx')
- grad_spec: float32 [2, 32, 64, 64], P(None, 'gx')
The draws below stay inside these ranges and needn't reach their ends.
All inputs are finite; a program needn't handle non-finite values.
Results may differ from the reference program's by a relative error of at most 0.018.
Values may be sent and summed in bfloat16 or wider, within the bound.
No kernel may reach another device: no remote copies, remote signals or barrier semaphores. Data moves between devices by JAX's collectives and lax.ppermute only.
A program may use at most 64 MiB of HBM per device.

```python
import math
import jax
import jax.numpy as jnp
from jax import lax

C = 64
HID = 256
KX = 32
NX = 1024
NY = 32
NZ = 8


def steps_of(own_key, shape, cuts, least, high):
    def one(dim, shards_of):
        draws = jax.random.uniform(jax.random.fold_in(jax.random.fold_in(own_key, 6), dim), (shards_of,), jnp.float32, least / len(cuts), high / len(cuts))
        return jnp.repeat(jnp.exp(draws), shape[dim] // shards_of).reshape((-1,) + (1,) * (len(shape) - dim - 1))

    gain = one(*cuts[0])
    for cut in cuts[1:]:
        gain = gain * one(*cut)
    return gain


def noise(own_key, dims, width, bound, pieces=(), kind=jnp.bfloat16):
    values = jax.random.normal(own_key, dims, jnp.float32) * width
    if len(pieces) > 0:
        values = steps_of(own_key, dims, pieces, -0.22, 0.18) * values
    return jnp.clip(values, min=-bound, max=bound).astype(kind)


def setup_inputs(seed: int = 0) -> dict:
    key_list = jax.random.split(jax.random.key(seed), 8)
    features = noise(key_list[0], (NZ, NY, NX * C), 1.0, 6.0, ((0, 4), (1, 2), (2, 4)))
    depth_weight = noise(key_list[1], (27, C), 27 ** -0.5, 1.25)
    expand_weight = noise(key_list[2], (C, HID), C ** -0.5, 0.75)
    project_weight = noise(key_list[3], (HID, C), HID ** -0.5, 0.375)
    spec_real = noise(key_list[4], (KX, C, C), 0.35, 2.0)
    spec_imag = noise(key_list[5], (KX, C, C), 0.35, 2.0)
    cotangent = noise(key_list[6], (NZ, NY, NX * C), 1.0, 6.0, ((0, 4), (1, 2), (2, 4)))
    return {"features": features, "depth_weight": depth_weight, "expand_weight": expand_weight, "project_weight": project_weight, "spec_real": spec_real, "spec_imag": spec_imag, "cotangent": cotangent}


def gelu_parts(values):
    normal_cdf = 0.5 * (1.0 + jax.scipy.special.erf(values * (1.0 / math.sqrt(2.0))))
    density = jnp.exp(-0.5 * values * values) * (1.0 / math.sqrt(2.0 * math.pi))
    return (values * normal_cdf, normal_cdf + values * density)

def dft_tables(offset, cells, x_length, mode_count):
    position = offset + jnp.arange(cells, dtype=jnp.int32)
    frequency = jnp.arange(mode_count, dtype=jnp.int32)
    phase_int = position[:, None] * frequency[None, :] % x_length
    angles = phase_int.astype(jnp.float32) * (2.0 * math.pi / x_length)
    return (jnp.cos(angles).astype(jnp.bfloat16), (-jnp.sin(angles)).astype(jnp.bfloat16))

def scaled_table(table, mode_count, x_length):
    frequency = jnp.arange(mode_count, dtype=jnp.int32)
    mode_scale = jnp.where(frequency == 0, 1.0, 2.0).astype(jnp.float32) / x_length
    return (table.astype(jnp.float32) * mode_scale[None, :]).astype(jnp.bfloat16)

def block_weights(spec_real, spec_imag):
    upper_row = jnp.concatenate([spec_real, spec_imag], axis=2)
    lower_row = jnp.concatenate([-spec_imag, spec_real], axis=2)
    return jnp.concatenate([upper_row, lower_row], axis=1)

def pad_field(grid4):
    wrapped = jnp.concatenate([grid4[:, :, -1:], grid4, grid4[:, :, :1]], axis=2)
    return jnp.pad(wrapped, ((1, 1), (1, 1), (0, 0), (0, 0)))

def stencil(window, taps, flipped):
    y_cells = window.shape[1] - 2
    x_cells = window.shape[2] - 2
    running = jnp.zeros((y_cells, x_cells, window.shape[3]), jnp.float32)
    direction = -1 if flipped else 1
    for step_z in (-1, 0, 1):
        for step_y in (-1, 0, 1):
            for step_x in (-1, 0, 1):
                tap_gain = taps[(step_z + 1) * 9 + (step_y + 1) * 3 + (step_x + 1)].astype(jnp.float32)
                z_offset = 1 + direction * step_z
                y_offset = 1 + direction * step_y
                x_offset = 1 + direction * step_x
                cut = window[z_offset, y_offset:y_offset + y_cells, x_offset:x_offset + x_cells]
                running = running + cut.astype(jnp.float32) * tap_gain
    return running

def reference(features, depth_weight, expand_weight, project_weight, spec_real, spec_imag, cotangent):
    grid = features.reshape(NZ, NY, NX, C)
    cot_grid = cotangent.reshape(NZ, NY, NX, C)
    padded = pad_field(grid)
    cos_b, sin_b = dft_tables(0, NX, NX, KX)
    cos_f = cos_b.astype(jnp.float32)
    sin_f = sin_b.astype(jnp.float32)
    cos_sf = scaled_table(cos_b, KX, NX).astype(jnp.float32)
    sin_sf = scaled_table(sin_b, KX, NX).astype(jnp.float32)
    blocks = block_weights(spec_real, spec_imag).astype(jnp.float32)

    def plane_pass(running, plane_index):
        window = lax.dynamic_slice_in_dim(padded, plane_index, 3, 0)
        plane = lax.dynamic_index_in_dim(grid, plane_index, 0, keepdims=False).astype(jnp.float32)
        cot_plane = lax.dynamic_index_in_dim(cot_grid, plane_index, 0, keepdims=False).astype(jnp.float32)
        activation = stencil(window, depth_weight, False).astype(jnp.bfloat16).reshape(NY * NX, C)
        hidden_pre = jnp.dot(activation, expand_weight, preferred_element_type=jnp.float32)
        hidden, hidden_slope = gelu_parts(hidden_pre)
        local_branch = jnp.dot(hidden.astype(jnp.bfloat16), project_weight, preferred_element_type=jnp.float32).reshape(NY, NX, C)
        coeffs = jnp.concatenate([jnp.einsum('yxc,xk->kyc', plane, cos_f), jnp.einsum('yxc,xk->kyc', plane, sin_f)], axis=2).astype(jnp.bfloat16)
        coeffs_f = coeffs.astype(jnp.float32)
        mixed_modes = jnp.einsum('kyc,kco->kyo', coeffs_f, blocks).astype(jnp.bfloat16)
        mixed_f = mixed_modes.astype(jnp.float32)
        spectral = jnp.einsum('kyo,xk->yxo', mixed_f[:, :, :C], cos_sf) + jnp.einsum('kyo,xk->yxo', mixed_f[:, :, C:], sin_sf)
        result, slopes = gelu_parts(local_branch + spectral)
        grad_pre = (cot_plane * slopes).astype(jnp.bfloat16)
        hidden_grad = jnp.dot(grad_pre.reshape(NY * NX, C), project_weight.T, preferred_element_type=jnp.float32)
        grad_hidden = (hidden_grad * hidden_slope).astype(jnp.bfloat16)
        grad_act = jnp.dot(grad_hidden, expand_weight.T, preferred_element_type=jnp.float32).astype(jnp.bfloat16).reshape(NY, NX, C)
        grad_pre_f = grad_pre.astype(jnp.float32)
        dcoef = jnp.concatenate([jnp.einsum('yxc,xk->kyc', grad_pre_f, cos_sf), jnp.einsum('yxc,xk->kyc', grad_pre_f, sin_sf)], axis=2).astype(jnp.bfloat16)
        dcoef_f = dcoef.astype(jnp.float32)
        dmode = jnp.einsum('kyo,kco->kyc', dcoef_f, blocks).astype(jnp.bfloat16)
        running = running + jnp.einsum('kyc,kyo->kco', coeffs_f, dcoef_f)
        return (running, (result.astype(jnp.bfloat16), grad_act, dmode))
    zeros_init = jnp.zeros((KX, 2 * C, 2 * C), jnp.float32)
    plane_ids = jnp.arange(NZ, dtype=jnp.int32)
    dblock, (results, grad_acts, dmodes) = lax.scan(plane_pass, zeros_init, plane_ids)
    padded_grad = pad_field(grad_acts)

    def input_pass(plane_index):
        window = lax.dynamic_slice_in_dim(padded_grad, plane_index, 3, 0)
        dmode = lax.dynamic_index_in_dim(dmodes, plane_index, 0, keepdims=False).astype(jnp.float32)
        spectral_grad = jnp.einsum('kyc,xk->yxc', dmode[:, :, :C], cos_f) + jnp.einsum('kyc,xk->yxc', dmode[:, :, C:], sin_f)
        return (stencil(window, depth_weight, True) + spectral_grad).astype(jnp.bfloat16)
    grad_grid = lax.map(input_pass, plane_ids)
    grad_real = dblock[:, :C, :C] + dblock[:, C:, C:]
    grad_imag = dblock[:, :C, C:] - dblock[:, C:, :C]
    return (results.reshape(NZ, NY, NX * C), grad_grid.reshape(NZ, NY, NX * C), jnp.stack([grad_real, grad_imag]))
```

```python
import functools
import math

import jax
import jax.numpy as jnp
from jax import lax
from jax.experimental import pallas as pl
from jax.experimental.pallas import tpu as pltpu
from jax.sharding import PartitionSpec as P


def padded_2(value, sides, width, wrap):
    for axis, dim in sides:
        size, length = (lax.axis_size(axis), value.shape[dim])
        up = [(i, (i + 1) % size) for i in range(size if wrap else size - 1)]
        down = [(j, i) for i, j in up]
        last = lax.slice_in_dim(value, length - width, length, axis=dim)
        leading = lax.slice_in_dim(value, 0, width, axis=dim)
        before = lax.ppermute(last, axis, up)
        after = lax.ppermute(leading, axis, down)
        value = jnp.concatenate([before, value, after], axis=dim)
    return value


def gelu_parts(values):
    normal_cdf = 0.5 * (1.0 + jax.scipy.special.erf(values * (1.0 / math.sqrt(2.0))))
    density = jnp.exp(-0.5 * values * values) * (1.0 / math.sqrt(2.0 * math.pi))
    return (values * normal_cdf, normal_cdf + values * density)


def dft_tables(offset, cells, x_length, mode_count):
    position = offset + jnp.arange(cells, dtype=jnp.int32)
    frequency = jnp.arange(mode_count, dtype=jnp.int32)
    phase_int = position[:, None] * frequency[None, :] % x_length
    angles = phase_int.astype(jnp.float32) * (2.0 * math.pi / x_length)
    return (jnp.cos(angles).astype(jnp.bfloat16), (-jnp.sin(angles)).astype(jnp.bfloat16))


def scaled_table(table, mode_count, x_length):
    frequency = jnp.arange(mode_count, dtype=jnp.int32)
    mode_scale = jnp.where(frequency == 0, 1.0, 2.0).astype(jnp.float32) / x_length
    return (table.astype(jnp.float32) * mode_scale[None, :]).astype(jnp.bfloat16)


def block_weights(spec_real, spec_imag):
    upper_row = jnp.concatenate([spec_real, spec_imag], axis=2)
    lower_row = jnp.concatenate([-spec_imag, spec_real], axis=2)
    return jnp.concatenate([upper_row, lower_row], axis=1)


def spatial_rims(field_block, channels):
    x_wide = padded_2(field_block, (("gx", 2),), 2 * channels, True)
    return padded_2(x_wide, (("gy", 1), ("gz", 0)), 1, False)


def stencil_kernel(chunk, x_pad, planes, y_cells, p_ref, w_ref, o_ref, s_ref):
    s_ref[...] = p_ref[...].astype(jnp.float32)
    width = chunk + 2 * x_pad
    count = o_ref.shape[2] // chunk

    def body(index, carry):
        base = pl.multiple_of(index * chunk, chunk)
        for plane in range(planes):
            left = jnp.zeros((y_cells, chunk + x_pad), jnp.float32)
            centre = jnp.zeros((y_cells, chunk), jnp.float32)
            right = jnp.zeros((y_cells, chunk + x_pad), jnp.float32)
            for step_z in range(3):
                for step_y in range(3):
                    window = s_ref[plane + step_z, pl.ds(step_y, y_cells), pl.ds(base, width)]
                    tap = 9 * step_z + 3 * step_y
                    left = left + window[:, : chunk + x_pad] * w_ref[tap : tap + 1, : chunk + x_pad]
                    centre = centre + window[:, x_pad : x_pad + chunk] * w_ref[
                        tap + 1 : tap + 2, :chunk
                    ]
                    right = right + window[:, x_pad:] * w_ref[tap + 2 : tap + 3, : chunk + x_pad]
            shift = chunk + x_pad - x_pad // 2
            total = (
                centre
                + pltpu.roll(left, shift, 1)[:, :chunk]
                + pltpu.roll(right, shift, 1)[:, :chunk]
            )
            o_ref[plane, :, pl.ds(base, chunk)] = total.astype(o_ref.dtype)
        return carry

    lax.fori_loop(0, count, body, 0)


def depthwise(padded, taps, flipped, x_cells, channels, out_dtype=jnp.float32):
    planes = padded.shape[0] - 2
    y_cells = padded.shape[1] - 2
    x_pad = 2 * channels
    lanes = x_cells * channels
    chunk = min(512, lanes)
    if flipped:
        taps = taps[::-1]
    gains = jnp.tile(taps.astype(jnp.float32), (1, (chunk + x_pad) // channels))
    kernel = functools.partial(stencil_kernel, chunk, x_pad, planes, y_cells)
    return pl.pallas_call(
        kernel,
        out_shape=jax.ShapeDtypeStruct((planes, y_cells, lanes), out_dtype),
        scratch_shapes=[pltpu.VMEM(padded.shape, jnp.float32)],
    )(padded, gains)


def share_terms(field3, cos_table, sin_table):
    real_part = jnp.einsum("rxc,xk->krc", field3, cos_table, preferred_element_type=jnp.float32)
    imag_part = jnp.einsum("rxc,xk->krc", field3, sin_table, preferred_element_type=jnp.float32)
    return lax.psum_scatter(
        jnp.concatenate([real_part, imag_part], axis=2), "gx", scatter_dimension=0, tiled=True
    )


def share_inverse(modes_share, cos_table, sin_table, channels):
    segment = lax.all_gather(modes_share, "gx", axis=0, tiled=True)
    running = jnp.einsum(
        "krc,xk->rxc", segment[:, :, :channels], cos_table, preferred_element_type=jnp.float32
    )
    return running + jnp.einsum(
        "krc,xk->rxc", segment[:, :, channels:], sin_table, preferred_element_type=jnp.float32
    )


def split_gradients(dblock, channels):
    grad_real = dblock[:, :channels, :channels] + dblock[:, channels:, channels:]
    grad_imag = dblock[:, :channels, channels:] - dblock[:, channels:, :channels]
    return jnp.stack([grad_real, grad_imag])


def sum_gradients(local_grads):
    return lax.psum(local_grads.astype(jnp.bfloat16), ("gy", "gz")).astype(jnp.float32)


def per_device(
    features, depth_weight, expand_weight, project_weight, spec_real, spec_imag, cotangent
):
    planes, y_cells, merged = features.shape
    channels = depth_weight.shape[1]
    x_cells = merged // channels
    row_count = planes * y_cells
    mode_count = spec_real.shape[0]
    group_size = lax.axis_size("gx")
    x_length = x_cells * group_size
    x_start = lax.axis_index("gx") * x_cells
    cos_part, sin_part = dft_tables(x_start, x_cells, x_length, mode_count)
    cos_scaled = scaled_table(cos_part, mode_count, x_length)
    sin_scaled = scaled_table(sin_part, mode_count, x_length)
    blocks = block_weights(spec_real, spec_imag)
    padded = spatial_rims(features, channels)
    activation = depthwise(padded, depth_weight, False, x_cells, channels, jnp.bfloat16)
    activation = activation.reshape(row_count * x_cells, channels)
    hidden_pre = jnp.dot(activation, expand_weight, preferred_element_type=jnp.float32)
    hidden, hidden_slope = gelu_parts(hidden_pre)
    local_branch = jnp.dot(
        hidden.astype(jnp.bfloat16), project_weight, preferred_element_type=jnp.float32
    )
    local_branch = local_branch.reshape(row_count, x_cells, channels)
    field3 = features.reshape(row_count, x_cells, channels)
    share_size = mode_count // group_size
    owned_blocks = lax.dynamic_slice_in_dim(
        blocks, lax.axis_index("gx") * share_size, share_size, 0
    )
    coeffs = share_terms(field3, cos_part, sin_part).astype(jnp.bfloat16)
    mixed_modes = jnp.einsum(
        "krc,kco->kro", coeffs, owned_blocks, preferred_element_type=jnp.float32
    ).astype(jnp.bfloat16)
    spectral = share_inverse(mixed_modes, cos_scaled, sin_scaled, channels)
    result, slopes = gelu_parts(local_branch + spectral)
    output = result.astype(jnp.bfloat16).reshape(planes, y_cells, merged)
    grad_pre = (
        cotangent.reshape(row_count, x_cells, channels).astype(jnp.float32) * slopes
    ).astype(jnp.bfloat16)
    hidden_grad = jnp.dot(
        grad_pre.reshape(row_count * x_cells, channels),
        project_weight.T,
        preferred_element_type=jnp.float32,
    )
    grad_hidden = (hidden_grad * hidden_slope).astype(jnp.bfloat16)
    grad_act = jnp.dot(grad_hidden, expand_weight.T, preferred_element_type=jnp.float32).astype(
        jnp.bfloat16
    )
    grad_act = grad_act.reshape(planes, y_cells, merged)
    dcoef = share_terms(grad_pre, cos_scaled, sin_scaled).astype(jnp.bfloat16)
    dmode = jnp.einsum(
        "kro,kco->krc", dcoef, owned_blocks, preferred_element_type=jnp.float32
    ).astype(jnp.bfloat16)
    spectral_grad = share_inverse(dmode, cos_part, sin_part, channels)
    dblock = jnp.einsum("krc,kro->kco", coeffs, dcoef, preferred_element_type=jnp.float32)
    grad_spec = sum_gradients(split_gradients(dblock, channels))
    padded_grad = spatial_rims(grad_act, channels)
    grad_local = depthwise(padded_grad, depth_weight, True, x_cells, channels)
    grad_features = (grad_local + spectral_grad.reshape(planes, y_cells, merged)).astype(
        jnp.bfloat16
    )
    return (output, grad_features, grad_spec)


def solution(mesh):
    placed = (P("gz", "gy", "gx"), P(), P(), P(), P(), P(), P("gz", "gy", "gx"))
    return jax.shard_map(
        per_device,
        mesh=mesh,
        in_specs=placed,
        out_specs=(P("gz", "gy", "gx"), P("gz", "gy", "gx"), P(None, "gx", None, None)),
        check_vma=False,
    )
```

```python
import functools
import math

import jax
import jax.numpy as jnp
from jax import lax
from jax.experimental import pallas as pl
from jax.experimental.pallas import tpu as pltpu
from jax.sharding import PartitionSpec as P


def padded_2(value, sides, width, wrap):
    for axis, dim in sides:
        size, length = (lax.axis_size(axis), value.shape[dim])
        up = [(i, (i + 1) % size) for i in range(size if wrap else size - 1)]
        down = [(j, i) for i, j in up]
        last = lax.slice_in_dim(value, length - width, length, axis=dim)
        leading = lax.slice_in_dim(value, 0, width, axis=dim)
        before = lax.ppermute(last, axis, up)
        after = lax.ppermute(leading, axis, down)
        value = jnp.concatenate([before, value, after], axis=dim)
    return value


def gelu_parts(values):
    normal_cdf = 0.5 * (1.0 + jax.scipy.special.erf(values * (1.0 / math.sqrt(2.0))))
    density = jnp.exp(-0.5 * values * values) * (1.0 / math.sqrt(2.0 * math.pi))
    return (values * normal_cdf, normal_cdf + values * density)


def dft_tables(offset, cells, x_length, frequency):
    position = offset + jnp.arange(cells, dtype=jnp.int32)
    phase_int = position[:, None] * frequency[None, :] % x_length
    angles = phase_int.astype(jnp.float32) * (2.0 * math.pi / x_length)
    return (jnp.cos(angles).astype(jnp.bfloat16), (-jnp.sin(angles)).astype(jnp.bfloat16))


def scaled_table(table, frequency, x_length):
    mode_scale = jnp.where(frequency == 0, 1.0, 2.0).astype(jnp.float32) / x_length
    return (table.astype(jnp.float32) * mode_scale[None, :]).astype(jnp.bfloat16)


def gathered_order(axis, share_size):
    size = lax.axis_size(axis)
    shifts = jnp.arange(size, dtype=jnp.int32)
    sources = (lax.axis_index(axis) - shifts) % size
    local = jnp.arange(share_size, dtype=jnp.int32)
    return (sources[:, None] * share_size + local[None, :]).reshape(-1)


def ring_gather(block, axis):
    size = lax.axis_size(axis)
    pieces = [block]
    for shift in range(1, size):
        pieces.append(lax.ppermute(block, axis, [(i, (i + shift) % size) for i in range(size)]))
    return jnp.concatenate(pieces, axis=0)


def butterfly_sum(value, axis):
    size = lax.axis_size(axis)
    if size & (size - 1):
        return lax.psum(value, axis)
    step = 1
    while step < size:
        value = value + lax.ppermute(value, axis, [(i, i ^ step) for i in range(size)])
        step *= 2
    return value


def block_weights(spec_real, spec_imag):
    upper_row = jnp.concatenate([spec_real, spec_imag], axis=2)
    lower_row = jnp.concatenate([-spec_imag, spec_real], axis=2)
    return jnp.concatenate([upper_row, lower_row], axis=1)


def spatial_rims(field_block, channels):
    x_wide = padded_2(field_block, (("gx", 2),), 2 * channels, True)
    return padded_2(x_wide, (("gy", 1), ("gz", 0)), 1, False)


def stencil_kernel(chunk, x_pad, planes, y_cells, p_ref, w_ref, o_ref, s_ref):
    s_ref[...] = p_ref[...].astype(jnp.float32)
    width = chunk + 2 * x_pad
    count = o_ref.shape[2] // chunk

    def body(index, carry):
        base = pl.multiple_of(index * chunk, chunk)
        for plane in range(planes):
            left = jnp.zeros((y_cells, chunk + x_pad), jnp.float32)
            centre = jnp.zeros((y_cells, chunk), jnp.float32)
            right = jnp.zeros((y_cells, chunk + x_pad), jnp.float32)
            for step_z in range(3):
                for step_y in range(3):
                    window = s_ref[plane + step_z, pl.ds(step_y, y_cells), pl.ds(base, width)]
                    tap = 9 * step_z + 3 * step_y
                    left = left + window[:, : chunk + x_pad] * w_ref[tap : tap + 1, : chunk + x_pad]
                    centre = centre + window[:, x_pad : x_pad + chunk] * w_ref[
                        tap + 1 : tap + 2, :chunk
                    ]
                    right = right + window[:, x_pad:] * w_ref[tap + 2 : tap + 3, : chunk + x_pad]
            shift = chunk + x_pad - x_pad // 2
            total = (
                centre
                + pltpu.roll(left, shift, 1)[:, :chunk]
                + pltpu.roll(right, shift, 1)[:, :chunk]
            )
            o_ref[plane, :, pl.ds(base, chunk)] = total.astype(o_ref.dtype)
        return carry

    lax.fori_loop(0, count, body, 0)


def depthwise(padded, taps, flipped, x_cells, channels, out_dtype=jnp.float32):
    planes = padded.shape[0] - 2
    y_cells = padded.shape[1] - 2
    x_pad = 2 * channels
    lanes = x_cells * channels
    chunk = min(512, lanes)
    if flipped:
        taps = taps[::-1]
    gains = jnp.tile(taps.astype(jnp.float32), (1, (chunk + x_pad) // channels))
    kernel = functools.partial(stencil_kernel, chunk, x_pad, planes, y_cells)
    return pl.pallas_call(
        kernel,
        out_shape=jax.ShapeDtypeStruct((planes, y_cells, lanes), out_dtype),
        scratch_shapes=[pltpu.VMEM(padded.shape, jnp.float32)],
    )(padded, gains)


def share_terms(field3, cos_table, sin_table):
    real_part = jnp.einsum("rxc,xk->krc", field3, cos_table, preferred_element_type=jnp.float32)
    imag_part = jnp.einsum("rxc,xk->krc", field3, sin_table, preferred_element_type=jnp.float32)
    return lax.psum_scatter(
        jnp.concatenate([real_part, imag_part], axis=2), "gx", scatter_dimension=0, tiled=True
    )


def share_inverse(modes_share, cos_table, sin_table, channels):
    segment = ring_gather(modes_share, "gx")
    running = jnp.einsum(
        "krc,xk->rxc", segment[:, :, :channels], cos_table, preferred_element_type=jnp.float32
    )
    return running + jnp.einsum(
        "krc,xk->rxc", segment[:, :, channels:], sin_table, preferred_element_type=jnp.float32
    )


def split_gradients(dblock, channels):
    grad_real = dblock[:, :channels, :channels] + dblock[:, channels:, channels:]
    grad_imag = dblock[:, :channels, channels:] - dblock[:, channels:, :channels]
    return jnp.stack([grad_real, grad_imag])


def sum_gradients(local_grads):
    return butterfly_sum(butterfly_sum(local_grads, "gy"), "gz")


def per_device(
    features, depth_weight, expand_weight, project_weight, spec_real, spec_imag, cotangent
):
    planes, y_cells, merged = features.shape
    channels = depth_weight.shape[1]
    x_cells = merged // channels
    row_count = planes * y_cells
    mode_count = spec_real.shape[0]
    group_size = lax.axis_size("gx")
    x_length = x_cells * group_size
    x_start = lax.axis_index("gx") * x_cells
    share_size = mode_count // group_size
    cos_part, sin_part = dft_tables(
        x_start, x_cells, x_length, jnp.arange(mode_count, dtype=jnp.int32)
    )
    order = gathered_order("gx", share_size)
    cos_order, sin_order = dft_tables(x_start, x_cells, x_length, order)
    cos_scaled = scaled_table(cos_order, order, x_length)
    sin_scaled = scaled_table(sin_order, order, x_length)
    cos_fwd_scaled = scaled_table(cos_part, jnp.arange(mode_count, dtype=jnp.int32), x_length)
    sin_fwd_scaled = scaled_table(sin_part, jnp.arange(mode_count, dtype=jnp.int32), x_length)
    blocks = block_weights(spec_real, spec_imag)
    padded = spatial_rims(features, channels)
    activation = depthwise(padded, depth_weight, False, x_cells, channels, jnp.bfloat16)
    activation = activation.reshape(row_count * x_cells, channels)
    hidden_pre = jnp.dot(activation, expand_weight, preferred_element_type=jnp.float32)
    hidden, hidden_slope = gelu_parts(hidden_pre)
    local_branch = jnp.dot(
        hidden.astype(jnp.bfloat16), project_weight, preferred_element_type=jnp.float32
    )
    local_branch = local_branch.reshape(row_count, x_cells, channels)
    field3 = features.reshape(row_count, x_cells, channels)
    owned_blocks = lax.dynamic_slice_in_dim(
        blocks, lax.axis_index("gx") * share_size, share_size, 0
    )
    coeffs = share_terms(field3, cos_part, sin_part).astype(jnp.bfloat16)
    mixed_modes = jnp.einsum(
        "krc,kco->kro", coeffs, owned_blocks, preferred_element_type=jnp.float32
    ).astype(jnp.bfloat16)
    spectral = share_inverse(mixed_modes, cos_scaled, sin_scaled, channels)
    result, slopes = gelu_parts(local_branch + spectral)
    output = result.astype(jnp.bfloat16).reshape(planes, y_cells, merged)
    grad_pre = (
        cotangent.reshape(row_count, x_cells, channels).astype(jnp.float32) * slopes
    ).astype(jnp.bfloat16)
    hidden_grad = jnp.dot(
        grad_pre.reshape(row_count * x_cells, channels),
        project_weight.T,
        preferred_element_type=jnp.float32,
    )
    grad_hidden = (hidden_grad * hidden_slope).astype(jnp.bfloat16)
    grad_act = jnp.dot(grad_hidden, expand_weight.T, preferred_element_type=jnp.float32).astype(
        jnp.bfloat16
    )
    grad_act = grad_act.reshape(planes, y_cells, merged)
    dcoef = share_terms(grad_pre, cos_fwd_scaled, sin_fwd_scaled).astype(jnp.bfloat16)
    dmode = jnp.einsum(
        "kro,kco->krc", dcoef, owned_blocks, preferred_element_type=jnp.float32
    ).astype(jnp.bfloat16)
    spectral_grad = share_inverse(dmode, cos_order, sin_order, channels)
    dblock = jnp.einsum("krc,kro->kco", coeffs, dcoef, preferred_element_type=jnp.float32)
    grad_spec = sum_gradients(split_gradients(dblock, channels))
    padded_grad = spatial_rims(grad_act, channels)
    grad_local = depthwise(padded_grad, depth_weight, True, x_cells, channels)
    grad_features = (grad_local + spectral_grad.reshape(planes, y_cells, merged)).astype(
        jnp.bfloat16
    )
    return (output, grad_features, grad_spec)


def solution(mesh):
    placed = (P("gz", "gy", "gx"), P(), P(), P(), P(), P(), P("gz", "gy", "gx"))
    return jax.shard_map(
        per_device,
        mesh=mesh,
        in_specs=placed,
        out_specs=(P("gz", "gy", "gx"), P("gz", "gy", "gx"), P(None, "gx", None, None)),
        check_vma=False,
    )
```

```python
import functools
import math

import jax
import jax.numpy as jnp
from jax import lax
from jax.experimental import pallas as pl
from jax.experimental.pallas import tpu as pltpu
from jax.sharding import PartitionSpec as P


def padded_2(value, sides, width, wrap):
    for axis, dim in sides:
        size, length = (lax.axis_size(axis), value.shape[dim])
        up = [(i, (i + 1) % size) for i in range(size if wrap else size - 1)]
        down = [(j, i) for i, j in up]
        last = lax.slice_in_dim(value, length - width, length, axis=dim)
        leading = lax.slice_in_dim(value, 0, width, axis=dim)
        before = lax.ppermute(last, axis, up)
        after = lax.ppermute(leading, axis, down)
        value = jnp.concatenate([before, value, after], axis=dim)
    return value


def gelu_parts(values):
    normal_cdf = 0.5 * (1.0 + jax.scipy.special.erf(values * (1.0 / math.sqrt(2.0))))
    density = jnp.exp(-0.5 * values * values) * (1.0 / math.sqrt(2.0 * math.pi))
    return (values * normal_cdf, normal_cdf + values * density)


def dft_tables(offset, cells, x_length, frequency):
    position = offset + jnp.arange(cells, dtype=jnp.int32)
    phase_int = position[:, None] * frequency[None, :] % x_length
    angles = phase_int.astype(jnp.float32) * (2.0 * math.pi / x_length)
    return (jnp.cos(angles).astype(jnp.bfloat16), (-jnp.sin(angles)).astype(jnp.bfloat16))


def scaled_table(table, frequency, x_length):
    mode_scale = jnp.where(frequency == 0, 1.0, 2.0).astype(jnp.float32) / x_length
    return (table.astype(jnp.float32) * mode_scale[None, :]).astype(jnp.bfloat16)


def gathered_order(axis, share_size):
    size = lax.axis_size(axis)
    shifts = jnp.arange(size, dtype=jnp.int32)
    sources = (lax.axis_index(axis) - shifts) % size
    local = jnp.arange(share_size, dtype=jnp.int32)
    return (sources[:, None] * share_size + local[None, :]).reshape(-1)


def ring_gather(block, axis):
    size = lax.axis_size(axis)
    pieces = [block]
    for shift in range(1, size):
        pieces.append(lax.ppermute(block, axis, [(i, (i + shift) % size) for i in range(size)]))
    return jnp.concatenate(pieces, axis=0)


def butterfly_sum(value, axis):
    size = lax.axis_size(axis)
    if size & (size - 1):
        return lax.psum(value, axis)
    step = 1
    while step < size:
        value = value + lax.ppermute(value, axis, [(i, i ^ step) for i in range(size)])
        step *= 2
    return value


def block_weights(spec_real, spec_imag):
    upper_row = jnp.concatenate([spec_real, spec_imag], axis=2)
    lower_row = jnp.concatenate([-spec_imag, spec_real], axis=2)
    return jnp.concatenate([upper_row, lower_row], axis=1)


def spatial_rims(field_block, channels):
    x_wide = padded_2(field_block, (("gx", 2),), 2 * channels, True)
    return padded_2(x_wide, (("gy", 1), ("gz", 0)), 1, False)


def stencil_kernel(chunk, x_pad, planes, y_cells, p_ref, w_ref, o_ref, s_ref):
    s_ref[...] = p_ref[...].astype(jnp.float32)
    width = chunk + 2 * x_pad
    count = o_ref.shape[2] // chunk

    def body(index, carry):
        base = pl.multiple_of(index * chunk, chunk)
        for plane in range(planes):
            left = jnp.zeros((y_cells, chunk + x_pad), jnp.float32)
            centre = jnp.zeros((y_cells, chunk), jnp.float32)
            right = jnp.zeros((y_cells, chunk + x_pad), jnp.float32)
            for step_z in range(3):
                for step_y in range(3):
                    window = s_ref[plane + step_z, pl.ds(step_y, y_cells), pl.ds(base, width)]
                    tap = 9 * step_z + 3 * step_y
                    left = left + window[:, : chunk + x_pad] * w_ref[tap : tap + 1, : chunk + x_pad]
                    centre = centre + window[:, x_pad : x_pad + chunk] * w_ref[
                        tap + 1 : tap + 2, :chunk
                    ]
                    right = right + window[:, x_pad:] * w_ref[tap + 2 : tap + 3, : chunk + x_pad]
            shift = chunk + x_pad - x_pad // 2
            total = (
                centre
                + pltpu.roll(left, shift, 1)[:, :chunk]
                + pltpu.roll(right, shift, 1)[:, :chunk]
            )
            o_ref[plane, :, pl.ds(base, chunk)] = total.astype(o_ref.dtype)
        return carry

    lax.fori_loop(0, count, body, 0)


def depthwise(padded, taps, flipped, x_cells, channels, out_dtype=jnp.float32):
    planes = padded.shape[0] - 2
    y_cells = padded.shape[1] - 2
    x_pad = 2 * channels
    lanes = x_cells * channels
    chunk = min(512, lanes)
    if flipped:
        taps = taps[::-1]
    gains = jnp.tile(taps.astype(jnp.float32), (1, (chunk + x_pad) // channels))
    kernel = functools.partial(stencil_kernel, chunk, x_pad, planes, y_cells)
    return pl.pallas_call(
        kernel,
        out_shape=jax.ShapeDtypeStruct((planes, y_cells, lanes), out_dtype),
        scratch_shapes=[pltpu.VMEM(padded.shape, jnp.float32)],
    )(padded, gains)


def share_terms(field3, cos_table, sin_table):
    real_part = jnp.einsum("rxc,xk->krc", field3, cos_table, preferred_element_type=jnp.float32)
    imag_part = jnp.einsum("rxc,xk->krc", field3, sin_table, preferred_element_type=jnp.float32)
    return lax.psum_scatter(
        jnp.concatenate([real_part, imag_part], axis=2), "gx", scatter_dimension=0, tiled=True
    )


def share_inverse(modes_share, cos_table, sin_table, channels):
    segment = ring_gather(modes_share, "gx")
    running = jnp.einsum(
        "krc,xk->rxc", segment[:, :, :channels], cos_table, preferred_element_type=jnp.float32
    )
    return running + jnp.einsum(
        "krc,xk->rxc", segment[:, :, channels:], sin_table, preferred_element_type=jnp.float32
    )


def split_gradients(dblock, channels):
    grad_real = dblock[:, :channels, :channels] + dblock[:, channels:, channels:]
    grad_imag = dblock[:, :channels, channels:] - dblock[:, channels:, :channels]
    return jnp.stack([grad_real, grad_imag])


def sum_gradients(local_grads):
    return butterfly_sum(butterfly_sum(local_grads, "gy"), "gz")


def per_device(
    features, depth_weight, expand_weight, project_weight, spec_real, spec_imag, cotangent
):
    planes, y_cells, merged = features.shape
    channels = depth_weight.shape[1]
    x_cells = merged // channels
    row_count = planes * y_cells
    mode_count = spec_real.shape[0]
    group_size = lax.axis_size("gx")
    x_length = x_cells * group_size
    x_start = lax.axis_index("gx") * x_cells
    share_size = mode_count // group_size
    cos_part, sin_part = dft_tables(
        x_start, x_cells, x_length, jnp.arange(mode_count, dtype=jnp.int32)
    )
    order = gathered_order("gx", share_size)
    cos_order, sin_order = dft_tables(x_start, x_cells, x_length, order)
    cos_scaled = scaled_table(cos_order, order, x_length)
    sin_scaled = scaled_table(sin_order, order, x_length)
    cos_fwd_scaled = scaled_table(cos_part, jnp.arange(mode_count, dtype=jnp.int32), x_length)
    sin_fwd_scaled = scaled_table(sin_part, jnp.arange(mode_count, dtype=jnp.int32), x_length)
    blocks = block_weights(spec_real, spec_imag)
    padded = spatial_rims(features, channels)
    activation = depthwise(padded, depth_weight, False, x_cells, channels, jnp.bfloat16)
    field3 = features.reshape(row_count, x_cells, channels)
    owned_blocks = lax.dynamic_slice_in_dim(
        blocks, lax.axis_index("gx") * share_size, share_size, 0
    )
    coeffs = share_terms(field3, cos_part, sin_part).astype(jnp.bfloat16)
    mixed_modes = jnp.einsum(
        "krc,kco->kro", coeffs, owned_blocks, preferred_element_type=jnp.float32
    ).astype(jnp.bfloat16)
    mixed_modes, activation = lax.optimization_barrier((mixed_modes, activation))
    activation = activation.reshape(row_count * x_cells, channels)
    hidden_pre = jnp.dot(activation, expand_weight, preferred_element_type=jnp.float32)
    hidden, hidden_slope = gelu_parts(hidden_pre)
    local_branch = jnp.dot(
        hidden.astype(jnp.bfloat16), project_weight, preferred_element_type=jnp.float32
    )
    local_branch = local_branch.reshape(row_count, x_cells, channels)
    spectral = share_inverse(mixed_modes, cos_scaled, sin_scaled, channels)
    result, slopes = gelu_parts(local_branch + spectral)
    output = result.astype(jnp.bfloat16).reshape(planes, y_cells, merged)
    grad_pre = (
        cotangent.reshape(row_count, x_cells, channels).astype(jnp.float32) * slopes
    ).astype(jnp.bfloat16)
    hidden_grad = jnp.dot(
        grad_pre.reshape(row_count * x_cells, channels),
        project_weight.T,
        preferred_element_type=jnp.float32,
    )
    grad_hidden = (hidden_grad * hidden_slope).astype(jnp.bfloat16)
    grad_act = jnp.dot(grad_hidden, expand_weight.T, preferred_element_type=jnp.float32).astype(
        jnp.bfloat16
    )
    grad_act = grad_act.reshape(planes, y_cells, merged)
    dcoef = share_terms(grad_pre, cos_fwd_scaled, sin_fwd_scaled).astype(jnp.bfloat16)
    dmode = jnp.einsum(
        "kro,kco->krc", dcoef, owned_blocks, preferred_element_type=jnp.float32
    ).astype(jnp.bfloat16)
    dblock = jnp.einsum("krc,kro->kco", coeffs, dcoef, preferred_element_type=jnp.float32)
    local_grads = split_gradients(dblock, channels)
    dmode, local_grads, grad_act = lax.optimization_barrier((dmode, local_grads, grad_act))
    spectral_grad = share_inverse(dmode, cos_order, sin_order, channels)
    grad_spec = sum_gradients(local_grads)
    padded_grad = spatial_rims(grad_act, channels)
    grad_local = depthwise(padded_grad, depth_weight, True, x_cells, channels)
    grad_features = (grad_local + spectral_grad.reshape(planes, y_cells, merged)).astype(
        jnp.bfloat16
    )
    return (output, grad_features, grad_spec)


def solution(mesh):
    placed = (P("gz", "gy", "gx"), P(), P(), P(), P(), P(), P("gz", "gy", "gx"))
    return jax.shard_map(
        per_device,
        mesh=mesh,
        in_specs=placed,
        out_specs=(P("gz", "gy", "gx"), P("gz", "gy", "gx"), P(None, "gx", None, None)),
        check_vma=False,
    )
```

```python
import functools
import math

import jax
import jax.numpy as jnp
from jax import lax
from jax.experimental import pallas as pl
from jax.experimental.pallas import tpu as pltpu
from jax.sharding import PartitionSpec as P


def padded_2(value, sides, width, wrap):
    for axis, dim in sides:
        size, length = (lax.axis_size(axis), value.shape[dim])
        up = [(i, (i + 1) % size) for i in range(size if wrap else size - 1)]
        down = [(j, i) for i, j in up]
        last = lax.slice_in_dim(value, length - width, length, axis=dim)
        leading = lax.slice_in_dim(value, 0, width, axis=dim)
        before = lax.ppermute(last, axis, up)
        after = lax.ppermute(leading, axis, down)
        value = jnp.concatenate([before, value, after], axis=dim)
    return value


def gelu_parts(values):
    normal_cdf = 0.5 * (1.0 + jax.scipy.special.erf(values * (1.0 / math.sqrt(2.0))))
    density = jnp.exp(-0.5 * values * values) * (1.0 / math.sqrt(2.0 * math.pi))
    return (values * normal_cdf, normal_cdf + values * density)


def dft_tables(offset, cells, x_length, frequency):
    position = offset + jnp.arange(cells, dtype=jnp.int32)
    phase_int = position[:, None] * frequency[None, :] % x_length
    angles = phase_int.astype(jnp.float32) * (2.0 * math.pi / x_length)
    return (jnp.cos(angles).astype(jnp.bfloat16), (-jnp.sin(angles)).astype(jnp.bfloat16))


def scaled_table(table, frequency, x_length):
    mode_scale = jnp.where(frequency == 0, 1.0, 2.0).astype(jnp.float32) / x_length
    return (table.astype(jnp.float32) * mode_scale[None, :]).astype(jnp.bfloat16)


def gathered_order(axis, share_size):
    size = lax.axis_size(axis)
    shifts = jnp.arange(size, dtype=jnp.int32)
    sources = (lax.axis_index(axis) - shifts) % size
    local = jnp.arange(share_size, dtype=jnp.int32)
    return (sources[:, None] * share_size + local[None, :]).reshape(-1)


def ring_gather(block, axis):
    size = lax.axis_size(axis)
    pieces = [block]
    for shift in range(1, size):
        pieces.append(lax.ppermute(block, axis, [(i, (i + shift) % size) for i in range(size)]))
    return jnp.concatenate(pieces, axis=0)


def butterfly_sum(value, axis):
    size = lax.axis_size(axis)
    if size & (size - 1):
        return lax.psum(value, axis)
    step = 1
    while step < size:
        value = value + lax.ppermute(value, axis, [(i, i ^ step) for i in range(size)])
        step *= 2
    return value


def block_weights(spec_real, spec_imag):
    upper_row = jnp.concatenate([spec_real, spec_imag], axis=2)
    lower_row = jnp.concatenate([-spec_imag, spec_real], axis=2)
    return jnp.concatenate([upper_row, lower_row], axis=1)


def spatial_rims(field_block, channels):
    x_wide = padded_2(field_block, (("gx", 2),), 2 * channels, True)
    return padded_2(x_wide, (("gy", 1), ("gz", 0)), 1, False)


def stencil_kernel(chunk, x_pad, planes, y_cells, rows, p_ref, w_ref, o_ref):
    width = chunk + 2 * x_pad
    count = o_ref.shape[2] // chunk
    shift = chunk + x_pad - x_pad // 2

    def body(index, carry):
        base = pl.multiple_of(index * chunk, chunk)
        for plane in range(planes):
            for row in range(0, y_cells, rows):
                left = jnp.zeros((rows, chunk + x_pad), jnp.float32)
                centre = jnp.zeros((rows, chunk), jnp.float32)
                right = jnp.zeros((rows, chunk + x_pad), jnp.float32)
                for step_z in range(3):
                    for step_y in range(3):
                        window = p_ref[plane + step_z, pl.ds(row + step_y, rows), pl.ds(base, width)]
                        tap = 9 * step_z + 3 * step_y
                        left = left + window[:, : chunk + x_pad] * w_ref[tap, :, : chunk + x_pad]
                        centre = centre + window[:, x_pad : x_pad + chunk] * w_ref[tap + 1, :, :chunk]
                        right = right + window[:, x_pad:] * w_ref[tap + 2, :, : chunk + x_pad]
                total = (
                    centre
                    + pltpu.roll(left, shift, 1)[:, :chunk]
                    + pltpu.roll(right, shift, 1)[:, :chunk]
                )
                o_ref[plane, pl.ds(row, rows), pl.ds(base, chunk)] = total.astype(o_ref.dtype)
        return carry

    lax.fori_loop(0, count, body, 0)


def depthwise(padded, taps, flipped, x_cells, channels, out_dtype=jnp.float32):
    planes = padded.shape[0] - 2
    y_cells = padded.shape[1] - 2
    x_pad = 2 * channels
    lanes = x_cells * channels
    chunk = min(2048, lanes)
    rows = 8 if y_cells % 8 == 0 else y_cells
    if flipped:
        taps = taps[::-1]
    gains = jnp.tile(taps.astype(jnp.float32), (1, (chunk + x_pad) // channels))
    gains = jnp.broadcast_to(gains[:, None, :], (gains.shape[0], rows, gains.shape[1]))
    kernel = functools.partial(stencil_kernel, chunk, x_pad, planes, y_cells, rows)
    return pl.pallas_call(
        kernel,
        out_shape=jax.ShapeDtypeStruct((planes, y_cells, lanes), out_dtype),
    )(padded.astype(jnp.float32), gains)


def share_terms(field3, cos_table, sin_table):
    real_part = jnp.einsum("rxc,xk->krc", field3, cos_table, preferred_element_type=jnp.float32)
    imag_part = jnp.einsum("rxc,xk->krc", field3, sin_table, preferred_element_type=jnp.float32)
    return lax.psum_scatter(
        jnp.concatenate([real_part, imag_part], axis=2), "gx", scatter_dimension=0, tiled=True
    )


def share_inverse(modes_share, cos_table, sin_table, channels):
    segment = ring_gather(modes_share, "gx")
    running = jnp.einsum(
        "krc,xk->rxc", segment[:, :, :channels], cos_table, preferred_element_type=jnp.float32
    )
    return running + jnp.einsum(
        "krc,xk->rxc", segment[:, :, channels:], sin_table, preferred_element_type=jnp.float32
    )


def split_gradients(dblock, channels):
    grad_real = dblock[:, :channels, :channels] + dblock[:, channels:, channels:]
    grad_imag = dblock[:, :channels, channels:] - dblock[:, channels:, :channels]
    return jnp.stack([grad_real, grad_imag])


def sum_gradients(local_grads):
    flat = local_grads.reshape(-1, 1024)
    return butterfly_sum(butterfly_sum(flat, "gy"), "gz").reshape(local_grads.shape)


def per_device(
    features, depth_weight, expand_weight, project_weight, spec_real, spec_imag, cotangent
):
    planes, y_cells, merged = features.shape
    channels = depth_weight.shape[1]
    x_cells = merged // channels
    row_count = planes * y_cells
    mode_count = spec_real.shape[0]
    group_size = lax.axis_size("gx")
    x_length = x_cells * group_size
    x_start = lax.axis_index("gx") * x_cells
    share_size = mode_count // group_size
    cos_part, sin_part = dft_tables(
        x_start, x_cells, x_length, jnp.arange(mode_count, dtype=jnp.int32)
    )
    order = gathered_order("gx", share_size)
    cos_order, sin_order = dft_tables(x_start, x_cells, x_length, order)
    cos_scaled = scaled_table(cos_order, order, x_length)
    sin_scaled = scaled_table(sin_order, order, x_length)
    cos_fwd_scaled = scaled_table(cos_part, jnp.arange(mode_count, dtype=jnp.int32), x_length)
    sin_fwd_scaled = scaled_table(sin_part, jnp.arange(mode_count, dtype=jnp.int32), x_length)
    blocks = block_weights(spec_real, spec_imag)
    padded = spatial_rims(features, channels)
    activation = depthwise(padded, depth_weight, False, x_cells, channels, jnp.bfloat16)
    field3 = features.reshape(row_count, x_cells, channels)
    owned_blocks = lax.dynamic_slice_in_dim(
        blocks, lax.axis_index("gx") * share_size, share_size, 0
    )
    coeffs = share_terms(field3, cos_part, sin_part).astype(jnp.bfloat16)
    mixed_modes = jnp.einsum(
        "krc,kco->kro", coeffs, owned_blocks, preferred_element_type=jnp.float32
    ).astype(jnp.bfloat16)
    mixed_modes, activation = lax.optimization_barrier((mixed_modes, activation))
    activation = activation.reshape(row_count * x_cells, channels)
    hidden_pre = jnp.dot(activation, expand_weight, preferred_element_type=jnp.float32)
    hidden, hidden_slope = gelu_parts(hidden_pre)
    local_branch = jnp.dot(
        hidden.astype(jnp.bfloat16), project_weight, preferred_element_type=jnp.float32
    )
    local_branch = local_branch.reshape(row_count, x_cells, channels)
    spectral = share_inverse(mixed_modes, cos_scaled, sin_scaled, channels)
    result, slopes = gelu_parts(local_branch + spectral)
    output = result.astype(jnp.bfloat16).reshape(planes, y_cells, merged)
    grad_pre = (
        cotangent.reshape(row_count, x_cells, channels).astype(jnp.float32) * slopes
    ).astype(jnp.bfloat16)
    hidden_grad = jnp.dot(
        grad_pre.reshape(row_count * x_cells, channels),
        project_weight.T,
        preferred_element_type=jnp.float32,
    )
    grad_hidden = (hidden_grad * hidden_slope).astype(jnp.bfloat16)
    grad_act = jnp.dot(grad_hidden, expand_weight.T, preferred_element_type=jnp.float32).astype(
        jnp.bfloat16
    )
    grad_act = grad_act.reshape(planes, y_cells, merged)
    dcoef = share_terms(grad_pre, cos_fwd_scaled, sin_fwd_scaled).astype(jnp.bfloat16)
    dmode = jnp.einsum(
        "kro,kco->krc", dcoef, owned_blocks, preferred_element_type=jnp.float32
    ).astype(jnp.bfloat16)
    dblock = jnp.einsum("krc,kro->kco", coeffs, dcoef, preferred_element_type=jnp.float32)
    local_grads = split_gradients(dblock, channels)
    dmode, local_grads, grad_act = lax.optimization_barrier((dmode, local_grads, grad_act))
    spectral_grad = share_inverse(dmode, cos_order, sin_order, channels)
    grad_spec = sum_gradients(local_grads)
    padded_grad = spatial_rims(grad_act, channels)
    grad_local = depthwise(padded_grad, depth_weight, True, x_cells, channels)
    grad_features = (grad_local + spectral_grad.reshape(planes, y_cells, merged)).astype(
        jnp.bfloat16
    )
    return (output, grad_features, grad_spec)


def solution(mesh):
    placed = (P("gz", "gy", "gx"), P(), P(), P(), P(), P(), P("gz", "gy", "gx"))
    return jax.shard_map(
        per_device,
        mesh=mesh,
        in_specs=placed,
        out_specs=(P("gz", "gy", "gx"), P("gz", "gy", "gx"), P(None, "gx", None, None)),
        check_vma=False,
    )
```

```python
import functools
import math

import jax
import jax.numpy as jnp
from jax import lax
from jax.experimental import pallas as pl
from jax.experimental.pallas import tpu as pltpu
from jax.sharding import PartitionSpec as P


def padded_2(value, sides, width, wrap):
    for axis, dim in sides:
        size, length = (lax.axis_size(axis), value.shape[dim])
        last = lax.slice_in_dim(value, length - width, length, axis=dim)
        leading = lax.slice_in_dim(value, 0, width, axis=dim)
        if size == 2 and not wrap:
            first = lax.axis_index(axis) == 0
            swapped = lax.ppermute(jnp.where(first, last, leading), axis, [(0, 1), (1, 0)])
            zeros = jnp.zeros_like(swapped)
            before = jnp.where(first, zeros, swapped)
            after = jnp.where(first, swapped, zeros)
        else:
            up = [(i, (i + 1) % size) for i in range(size if wrap else size - 1)]
            down = [(j, i) for i, j in up]
            before = lax.ppermute(last, axis, up)
            after = lax.ppermute(leading, axis, down)
        value = jnp.concatenate([before, value, after], axis=dim)
    return value


def gelu_parts(values):
    normal_cdf = 0.5 * (1.0 + jax.scipy.special.erf(values * (1.0 / math.sqrt(2.0))))
    density = jnp.exp(-0.5 * values * values) * (1.0 / math.sqrt(2.0 * math.pi))
    return (values * normal_cdf, normal_cdf + values * density)


def dft_tables(offset, cells, x_length, frequency):
    position = offset + jnp.arange(cells, dtype=jnp.int32)
    phase_int = position[:, None] * frequency[None, :] % x_length
    angles = phase_int.astype(jnp.float32) * (2.0 * math.pi / x_length)
    return (jnp.cos(angles).astype(jnp.bfloat16), (-jnp.sin(angles)).astype(jnp.bfloat16))


def scaled_table(table, frequency, x_length):
    mode_scale = jnp.where(frequency == 0, 1.0, 2.0).astype(jnp.float32) / x_length
    return (table.astype(jnp.float32) * mode_scale[None, :]).astype(jnp.bfloat16)


def gathered_order(axis, share_size):
    size = lax.axis_size(axis)
    shifts = jnp.arange(size, dtype=jnp.int32)
    sources = (lax.axis_index(axis) - shifts) % size
    local = jnp.arange(share_size, dtype=jnp.int32)
    return (sources[:, None] * share_size + local[None, :]).reshape(-1)


def ring_gather(block, axis):
    size = lax.axis_size(axis)
    pieces = [block]
    for shift in range(1, size):
        pieces.append(lax.ppermute(block, axis, [(i, (i + shift) % size) for i in range(size)]))
    return jnp.concatenate(pieces, axis=0)


def butterfly_sum(value, axis):
    size = lax.axis_size(axis)
    if size & (size - 1):
        return lax.psum(value, axis)
    step = 1
    while step < size:
        value = value + lax.ppermute(value, axis, [(i, i ^ step) for i in range(size)])
        step *= 2
    return value


def block_weights(spec_real, spec_imag):
    upper_row = jnp.concatenate([spec_real, spec_imag], axis=2)
    lower_row = jnp.concatenate([-spec_imag, spec_real], axis=2)
    return jnp.concatenate([upper_row, lower_row], axis=1)


def spatial_rims(field_block, channels):
    x_wide = padded_2(field_block, (("gx", 2),), 2 * channels, True)
    return padded_2(x_wide, (("gy", 1), ("gz", 0)), 1, False)


def stencil_kernel(chunk, x_pad, planes, y_cells, rows, p_ref, w_ref, o_ref):
    width = chunk + 2 * x_pad
    count = o_ref.shape[2] // chunk
    shift = chunk + x_pad - x_pad // 2

    def body(index, carry):
        base = pl.multiple_of(index * chunk, chunk)
        for plane in range(planes):
            for row in range(0, y_cells, rows):
                left = jnp.zeros((rows, chunk + x_pad), jnp.float32)
                centre = jnp.zeros((rows, chunk), jnp.float32)
                right = jnp.zeros((rows, chunk + x_pad), jnp.float32)
                for step_z in range(3):
                    for step_y in range(3):
                        window = p_ref[plane + step_z, pl.ds(row + step_y, rows), pl.ds(base, width)]
                        tap = 9 * step_z + 3 * step_y
                        left = left + window[:, : chunk + x_pad] * w_ref[tap, :, : chunk + x_pad]
                        centre = centre + window[:, x_pad : x_pad + chunk] * w_ref[tap + 1, :, :chunk]
                        right = right + window[:, x_pad:] * w_ref[tap + 2, :, : chunk + x_pad]
                total = (
                    centre
                    + pltpu.roll(left, shift, 1)[:, :chunk]
                    + pltpu.roll(right, shift, 1)[:, :chunk]
                )
                o_ref[plane, pl.ds(row, rows), pl.ds(base, chunk)] = total.astype(o_ref.dtype)
        return carry

    lax.fori_loop(0, count, body, 0)


def depthwise(padded, taps, flipped, x_cells, channels, out_dtype=jnp.float32):
    planes = padded.shape[0] - 2
    y_cells = padded.shape[1] - 2
    x_pad = 2 * channels
    lanes = x_cells * channels
    chunk = min(2048, lanes)
    rows = 8 if y_cells % 8 == 0 else y_cells
    if flipped:
        taps = taps[::-1]
    gains = jnp.tile(taps.astype(jnp.float32), (1, (chunk + x_pad) // channels))
    gains = jnp.broadcast_to(gains[:, None, :], (gains.shape[0], rows, gains.shape[1]))
    kernel = functools.partial(stencil_kernel, chunk, x_pad, planes, y_cells, rows)
    return pl.pallas_call(
        kernel,
        out_shape=jax.ShapeDtypeStruct((planes, y_cells, lanes), out_dtype),
    )(padded.astype(jnp.float32), gains)


def share_terms(field3, cos_table, sin_table):
    real_part = jnp.einsum("rxc,xk->krc", field3, cos_table, preferred_element_type=jnp.float32)
    imag_part = jnp.einsum("rxc,xk->krc", field3, sin_table, preferred_element_type=jnp.float32)
    return lax.psum_scatter(
        jnp.concatenate([real_part, imag_part], axis=2), "gx", scatter_dimension=0, tiled=True
    )


def share_inverse(modes_share, cos_table, sin_table, channels):
    segment = ring_gather(modes_share, "gx")
    running = jnp.einsum(
        "krc,xk->rxc", segment[:, :, :channels], cos_table, preferred_element_type=jnp.float32
    )
    return running + jnp.einsum(
        "krc,xk->rxc", segment[:, :, channels:], sin_table, preferred_element_type=jnp.float32
    )


def split_gradients(dblock, channels):
    grad_real = dblock[:, :channels, :channels] + dblock[:, channels:, channels:]
    grad_imag = dblock[:, :channels, channels:] - dblock[:, channels:, :channels]
    return jnp.stack([grad_real, grad_imag])


def sum_gradients(local_grads):
    flat = local_grads.reshape(-1, 1024)
    return butterfly_sum(butterfly_sum(flat, "gy"), "gz").reshape(local_grads.shape)


def per_device(
    features, depth_weight, expand_weight, project_weight, spec_real, spec_imag, cotangent
):
    planes, y_cells, merged = features.shape
    channels = depth_weight.shape[1]
    x_cells = merged // channels
    row_count = planes * y_cells
    mode_count = spec_real.shape[0]
    group_size = lax.axis_size("gx")
    x_length = x_cells * group_size
    x_start = lax.axis_index("gx") * x_cells
    share_size = mode_count // group_size
    cos_part, sin_part = dft_tables(
        x_start, x_cells, x_length, jnp.arange(mode_count, dtype=jnp.int32)
    )
    order = gathered_order("gx", share_size)
    cos_order, sin_order = dft_tables(x_start, x_cells, x_length, order)
    cos_scaled = scaled_table(cos_order, order, x_length)
    sin_scaled = scaled_table(sin_order, order, x_length)
    cos_fwd_scaled = scaled_table(cos_part, jnp.arange(mode_count, dtype=jnp.int32), x_length)
    sin_fwd_scaled = scaled_table(sin_part, jnp.arange(mode_count, dtype=jnp.int32), x_length)
    blocks = block_weights(spec_real, spec_imag)
    padded = spatial_rims(features, channels)
    activation = depthwise(padded, depth_weight, False, x_cells, channels, jnp.bfloat16)
    field3 = features.reshape(row_count, x_cells, channels)
    owned_blocks = lax.dynamic_slice_in_dim(
        blocks, lax.axis_index("gx") * share_size, share_size, 0
    )
    coeffs = share_terms(field3, cos_part, sin_part).astype(jnp.bfloat16)
    mixed_modes = jnp.einsum(
        "krc,kco->kro", coeffs, owned_blocks, preferred_element_type=jnp.float32
    ).astype(jnp.bfloat16)
    mixed_modes, activation = lax.optimization_barrier((mixed_modes, activation))
    activation = activation.reshape(row_count * x_cells, channels)
    hidden_pre = jnp.dot(activation, expand_weight, preferred_element_type=jnp.float32)
    hidden, hidden_slope = gelu_parts(hidden_pre)
    local_branch = jnp.dot(
        hidden.astype(jnp.bfloat16), project_weight, preferred_element_type=jnp.float32
    )
    local_branch = local_branch.reshape(row_count, x_cells, channels)
    spectral = share_inverse(mixed_modes, cos_scaled, sin_scaled, channels)
    result, slopes = gelu_parts(local_branch + spectral)
    output = result.astype(jnp.bfloat16).reshape(planes, y_cells, merged)
    grad_pre = (
        cotangent.reshape(row_count, x_cells, channels).astype(jnp.float32) * slopes
    ).astype(jnp.bfloat16)
    hidden_grad = jnp.dot(
        grad_pre.reshape(row_count * x_cells, channels),
        project_weight.T,
        preferred_element_type=jnp.float32,
    )
    grad_hidden = (hidden_grad * hidden_slope).astype(jnp.bfloat16)
    grad_act = jnp.dot(grad_hidden, expand_weight.T, preferred_element_type=jnp.float32).astype(
        jnp.bfloat16
    )
    grad_act = grad_act.reshape(planes, y_cells, merged)
    dcoef = share_terms(grad_pre, cos_fwd_scaled, sin_fwd_scaled).astype(jnp.bfloat16)
    dmode = jnp.einsum(
        "kro,kco->krc", dcoef, owned_blocks, preferred_element_type=jnp.float32
    ).astype(jnp.bfloat16)
    dblock = jnp.einsum("krc,kro->kco", coeffs, dcoef, preferred_element_type=jnp.float32)
    local_grads = split_gradients(dblock, channels)
    padded_grad = spatial_rims(grad_act, channels)
    dmode, local_grads, padded_grad = lax.optimization_barrier((dmode, local_grads, padded_grad))
    spectral_grad = share_inverse(dmode, cos_order, sin_order, channels)
    grad_spec = sum_gradients(local_grads)
    grad_local = depthwise(padded_grad, depth_weight, True, x_cells, channels)
    grad_features = (grad_local + spectral_grad.reshape(planes, y_cells, merged)).astype(
        jnp.bfloat16
    )
    return (output, grad_features, grad_spec)


def solution(mesh):
    placed = (P("gz", "gy", "gx"), P(), P(), P(), P(), P(), P("gz", "gy", "gx"))
    return jax.shard_map(
        per_device,
        mesh=mesh,
        in_specs=placed,
        out_specs=(P("gz", "gy", "gx"), P("gz", "gy", "gx"), P(None, "gx", None, None)),
        check_vma=False,
    )
```

```python
import functools
import math

import jax
import jax.numpy as jnp
from jax import lax
from jax.experimental import pallas as pl
from jax.experimental.pallas import tpu as pltpu
from jax.sharding import PartitionSpec as P


def padded_2(value, sides, width, wrap):
    for axis, dim in sides:
        size, length = (lax.axis_size(axis), value.shape[dim])
        up = [(i, (i + 1) % size) for i in range(size if wrap else size - 1)]
        down = [(j, i) for i, j in up]
        last = lax.slice_in_dim(value, length - width, length, axis=dim)
        leading = lax.slice_in_dim(value, 0, width, axis=dim)
        before = lax.ppermute(last, axis, up)
        after = lax.ppermute(leading, axis, down)
        value = jnp.concatenate([before, value, after], axis=dim)
    return value


def gelu_parts(values):
    normal_cdf = 0.5 * (1.0 + jax.scipy.special.erf(values * (1.0 / math.sqrt(2.0))))
    density = jnp.exp(-0.5 * values * values) * (1.0 / math.sqrt(2.0 * math.pi))
    return (values * normal_cdf, normal_cdf + values * density)


def dft_tables(offset, cells, x_length, frequency):
    position = offset + jnp.arange(cells, dtype=jnp.int32)
    phase_int = position[:, None] * frequency[None, :] % x_length
    angles = phase_int.astype(jnp.float32) * (2.0 * math.pi / x_length)
    return (jnp.cos(angles).astype(jnp.bfloat16), (-jnp.sin(angles)).astype(jnp.bfloat16))


def scaled_table(table, frequency, x_length):
    mode_scale = jnp.where(frequency == 0, 1.0, 2.0).astype(jnp.float32) / x_length
    return (table.astype(jnp.float32) * mode_scale[None, :]).astype(jnp.bfloat16)


def gathered_order(axis, share_size):
    size = lax.axis_size(axis)
    shifts = jnp.arange(size, dtype=jnp.int32)
    sources = (lax.axis_index(axis) - shifts) % size
    local = jnp.arange(share_size, dtype=jnp.int32)
    return (sources[:, None] * share_size + local[None, :]).reshape(-1)


def ring_gather(block, axis):
    size = lax.axis_size(axis)
    pieces = [block]
    for shift in range(1, size):
        pieces.append(lax.ppermute(block, axis, [(i, (i + shift) % size) for i in range(size)]))
    return jnp.concatenate(pieces, axis=0)


def butterfly_sum(value, axis):
    size = lax.axis_size(axis)
    if size & (size - 1):
        return lax.psum(value, axis)
    step = 1
    while step < size:
        value = value + lax.ppermute(value, axis, [(i, i ^ step) for i in range(size)])
        step *= 2
    return value


def block_weights(spec_real, spec_imag):
    upper_row = jnp.concatenate([spec_real, spec_imag], axis=2)
    lower_row = jnp.concatenate([-spec_imag, spec_real], axis=2)
    return jnp.concatenate([upper_row, lower_row], axis=1)


def spatial_rims(field_block, channels):
    x_wide = padded_2(field_block, (("gx", 2),), 2 * channels, True)
    return padded_2(x_wide, (("gy", 1), ("gz", 0)), 1, False)


def stencil_kernel(chunk, x_pad, planes, y_cells, rows, p_ref, w_ref, o_ref):
    count = o_ref.shape[2] // chunk
    shift = chunk + x_pad - x_pad // 2

    def body(index, carry):
        base = pl.multiple_of(index * chunk, chunk)
        for plane in range(planes):
            for row in range(0, y_cells, rows):
                total = jnp.zeros((rows, chunk), jnp.float32)
                for step_x, offset, span in ((0, 0, chunk + x_pad), (1, x_pad, chunk), (2, x_pad, chunk + x_pad)):
                    running = jnp.zeros((rows, span), jnp.float32)
                    for step_z in range(3):
                        for step_y in range(3):
                            window = p_ref[
                                plane + step_z, pl.ds(row + step_y, rows), pl.ds(base + offset, span)
                            ]
                            running = running + window * w_ref[9 * step_z + 3 * step_y + step_x, :, :span]
                    if step_x == 1:
                        total = total + running
                    else:
                        total = total + pltpu.roll(running, shift, 1)[:, :chunk]
                o_ref[plane, pl.ds(row, rows), pl.ds(base, chunk)] = total.astype(o_ref.dtype)
        return carry

    lax.fori_loop(0, count, body, 0)


def depthwise(padded, taps, flipped, x_cells, channels, out_dtype=jnp.float32):
    planes = padded.shape[0] - 2
    y_cells = padded.shape[1] - 2
    x_pad = 2 * channels
    lanes = x_cells * channels
    chunk = min(1024, lanes)
    rows = 8 if y_cells % 8 == 0 else y_cells
    if flipped:
        taps = taps[::-1]
    gains = jnp.tile(taps.astype(jnp.float32), (1, (chunk + x_pad) // channels))
    gains = jnp.broadcast_to(gains[:, None, :], (gains.shape[0], rows, gains.shape[1]))
    kernel = functools.partial(stencil_kernel, chunk, x_pad, planes, y_cells, rows)
    return pl.pallas_call(
        kernel,
        out_shape=jax.ShapeDtypeStruct((planes, y_cells, lanes), out_dtype),
    )(padded.astype(jnp.float32), gains)


def share_terms(field3, cos_table, sin_table):
    real_part = jnp.einsum("rxc,xk->krc", field3, cos_table, preferred_element_type=jnp.float32)
    imag_part = jnp.einsum("rxc,xk->krc", field3, sin_table, preferred_element_type=jnp.float32)
    return lax.psum_scatter(
        jnp.concatenate([real_part, imag_part], axis=2), "gx", scatter_dimension=0, tiled=True
    )


def share_inverse(modes_share, cos_table, sin_table, channels):
    segment = ring_gather(modes_share, "gx")
    running = jnp.einsum(
        "krc,xk->rxc", segment[:, :, :channels], cos_table, preferred_element_type=jnp.float32
    )
    return running + jnp.einsum(
        "krc,xk->rxc", segment[:, :, channels:], sin_table, preferred_element_type=jnp.float32
    )


def split_gradients(dblock, channels):
    grad_real = dblock[:, :channels, :channels] + dblock[:, channels:, channels:]
    grad_imag = dblock[:, :channels, channels:] - dblock[:, channels:, :channels]
    return jnp.stack([grad_real, grad_imag])


def sum_gradients(local_grads):
    flat = local_grads.reshape(-1, 1024)
    return butterfly_sum(butterfly_sum(flat, "gy"), "gz").reshape(local_grads.shape)


def per_device(
    features, depth_weight, expand_weight, project_weight, spec_real, spec_imag, cotangent
):
    planes, y_cells, merged = features.shape
    channels = depth_weight.shape[1]
    x_cells = merged // channels
    row_count = planes * y_cells
    mode_count = spec_real.shape[0]
    group_size = lax.axis_size("gx")
    x_length = x_cells * group_size
    x_start = lax.axis_index("gx") * x_cells
    share_size = mode_count // group_size
    cos_part, sin_part = dft_tables(
        x_start, x_cells, x_length, jnp.arange(mode_count, dtype=jnp.int32)
    )
    order = gathered_order("gx", share_size)
    cos_order, sin_order = dft_tables(x_start, x_cells, x_length, order)
    cos_scaled = scaled_table(cos_order, order, x_length)
    sin_scaled = scaled_table(sin_order, order, x_length)
    cos_fwd_scaled = scaled_table(cos_part, jnp.arange(mode_count, dtype=jnp.int32), x_length)
    sin_fwd_scaled = scaled_table(sin_part, jnp.arange(mode_count, dtype=jnp.int32), x_length)
    blocks = block_weights(spec_real, spec_imag)
    padded = spatial_rims(features, channels)
    activation = depthwise(padded, depth_weight, False, x_cells, channels, jnp.bfloat16)
    field3 = features.reshape(row_count, x_cells, channels)
    owned_blocks = lax.dynamic_slice_in_dim(
        blocks, lax.axis_index("gx") * share_size, share_size, 0
    )
    coeffs = share_terms(field3, cos_part, sin_part).astype(jnp.bfloat16)
    mixed_modes = jnp.einsum(
        "krc,kco->kro", coeffs, owned_blocks, preferred_element_type=jnp.float32
    ).astype(jnp.bfloat16)
    mixed_modes, activation = lax.optimization_barrier((mixed_modes, activation))
    activation = activation.reshape(row_count * x_cells, channels)
    hidden_pre = jnp.dot(activation, expand_weight, preferred_element_type=jnp.float32)
    hidden, hidden_slope = gelu_parts(hidden_pre)
    local_branch = jnp.dot(
        hidden.astype(jnp.bfloat16), project_weight, preferred_element_type=jnp.float32
    )
    local_branch = local_branch.reshape(row_count, x_cells, channels)
    spectral = share_inverse(mixed_modes, cos_scaled, sin_scaled, channels)
    result, slopes = gelu_parts(local_branch + spectral)
    output = result.astype(jnp.bfloat16).reshape(planes, y_cells, merged)
    grad_pre = (
        cotangent.reshape(row_count, x_cells, channels).astype(jnp.float32) * slopes
    ).astype(jnp.bfloat16)
    hidden_grad = jnp.dot(
        grad_pre.reshape(row_count * x_cells, channels),
        project_weight.T,
        preferred_element_type=jnp.float32,
    )
    grad_hidden = (hidden_grad * hidden_slope).astype(jnp.bfloat16)
    grad_act = jnp.dot(grad_hidden, expand_weight.T, preferred_element_type=jnp.float32).astype(
        jnp.bfloat16
    )
    grad_act = grad_act.reshape(planes, y_cells, merged)
    dcoef = share_terms(grad_pre, cos_fwd_scaled, sin_fwd_scaled).astype(jnp.bfloat16)
    dmode = jnp.einsum(
        "kro,kco->krc", dcoef, owned_blocks, preferred_element_type=jnp.float32
    ).astype(jnp.bfloat16)
    dblock = jnp.einsum("krc,kro->kco", coeffs, dcoef, preferred_element_type=jnp.float32)
    local_grads = split_gradients(dblock, channels)
    dmode, local_grads, grad_act = lax.optimization_barrier((dmode, local_grads, grad_act))
    spectral_grad = share_inverse(dmode, cos_order, sin_order, channels)
    grad_spec = sum_gradients(local_grads)
    padded_grad = spatial_rims(grad_act, channels)
    grad_local = depthwise(padded_grad, depth_weight, True, x_cells, channels)
    grad_features = (grad_local + spectral_grad.reshape(planes, y_cells, merged)).astype(
        jnp.bfloat16
    )
    return (output, grad_features, grad_spec)


def solution(mesh):
    placed = (P("gz", "gy", "gx"), P(), P(), P(), P(), P(), P("gz", "gy", "gx"))
    return jax.shard_map(
        per_device,
        mesh=mesh,
        in_specs=placed,
        out_specs=(P("gz", "gy", "gx"), P("gz", "gy", "gx"), P(None, "gx", None, None)),
        check_vma=False,
    )
```

```python
import functools
import math

import jax
import jax.numpy as jnp
from jax import lax
from jax.experimental import pallas as pl
from jax.experimental.pallas import tpu as pltpu
from jax.sharding import PartitionSpec as P


def padded_2(value, sides, width, wrap):
    for axis, dim in sides:
        size, length = (lax.axis_size(axis), value.shape[dim])
        up = [(i, (i + 1) % size) for i in range(size if wrap else size - 1)]
        down = [(j, i) for i, j in up]
        last = lax.slice_in_dim(value, length - width, length, axis=dim)
        leading = lax.slice_in_dim(value, 0, width, axis=dim)
        before = lax.ppermute(last, axis, up)
        after = lax.ppermute(leading, axis, down)
        value = jnp.concatenate([before, value, after], axis=dim)
    return value


def gelu_parts(values):
    normal_cdf = 0.5 * (1.0 + jax.scipy.special.erf(values * (1.0 / math.sqrt(2.0))))
    density = jnp.exp(-0.5 * values * values) * (1.0 / math.sqrt(2.0 * math.pi))
    return (values * normal_cdf, normal_cdf + values * density)


def dft_tables(offset, cells, x_length, frequency):
    position = offset + jnp.arange(cells, dtype=jnp.int32)
    phase_int = position[:, None] * frequency[None, :] % x_length
    angles = phase_int.astype(jnp.float32) * (2.0 * math.pi / x_length)
    return (jnp.cos(angles).astype(jnp.bfloat16), (-jnp.sin(angles)).astype(jnp.bfloat16))


def scaled_table(table, frequency, x_length):
    mode_scale = jnp.where(frequency == 0, 1.0, 2.0).astype(jnp.float32) / x_length
    return (table.astype(jnp.float32) * mode_scale[None, :]).astype(jnp.bfloat16)


def gathered_order(axis, share_size):
    size = lax.axis_size(axis)
    shifts = jnp.arange(size, dtype=jnp.int32)
    sources = (lax.axis_index(axis) - shifts) % size
    local = jnp.arange(share_size, dtype=jnp.int32)
    return (sources[:, None] * share_size + local[None, :]).reshape(-1)


def ring_gather(block, axis):
    size = lax.axis_size(axis)
    pieces = [block]
    for shift in range(1, size):
        pieces.append(lax.ppermute(block, axis, [(i, (i + shift) % size) for i in range(size)]))
    return jnp.concatenate(pieces, axis=0)


def butterfly_sum(value, axis):
    size = lax.axis_size(axis)
    if size & (size - 1):
        return lax.psum(value, axis)
    step = 1
    while step < size:
        value = value + lax.ppermute(value, axis, [(i, i ^ step) for i in range(size)])
        step *= 2
    return value


def block_weights(spec_real, spec_imag):
    upper_row = jnp.concatenate([spec_real, spec_imag], axis=2)
    lower_row = jnp.concatenate([-spec_imag, spec_real], axis=2)
    return jnp.concatenate([upper_row, lower_row], axis=1)


def spatial_rims(field_block, channels):
    x_wide = padded_2(field_block, (("gx", 2),), 2 * channels, True)
    return padded_2(x_wide, (("gy", 1), ("gz", 0)), 1, False)


def stencil_kernel(chunk, x_pad, planes, y_cells, rows, p_ref, w_ref, o_ref):
    width = chunk + 2 * x_pad
    count = o_ref.shape[2] // chunk
    shift = chunk + x_pad - x_pad // 2
    side = (chunk + x_pad) // 128

    def body(index, carry):
        base = pl.multiple_of(index * chunk, chunk)
        for plane in range(planes):
            for row in range(0, y_cells, rows):
                left = jnp.zeros((rows, chunk + x_pad), jnp.float32)
                centre = jnp.zeros((rows, chunk), jnp.float32)
                right = jnp.zeros((rows, chunk + x_pad), jnp.float32)
                for step_z in range(3):
                    for step_y in range(3):
                        window = p_ref[plane + step_z, pl.ds(row + step_y, rows), pl.ds(base, width)]
                        tap = 9 * step_z + 3 * step_y
                        gain_l = jnp.concatenate([w_ref[tap]] * side, axis=1)
                        gain_c = jnp.concatenate([w_ref[tap + 1]] * (side - 1), axis=1)
                        gain_r = jnp.concatenate([w_ref[tap + 2]] * side, axis=1)
                        left = left + window[:, : chunk + x_pad] * gain_l
                        centre = centre + window[:, x_pad : x_pad + chunk] * gain_c
                        right = right + window[:, x_pad:] * gain_r
                total = (
                    centre
                    + pltpu.roll(left, shift, 1)[:, :chunk]
                    + pltpu.roll(right, shift, 1)[:, :chunk]
                )
                o_ref[plane, pl.ds(row, rows), pl.ds(base, chunk)] = total.astype(o_ref.dtype)
        return carry

    lax.fori_loop(0, count, body, 0)


def depthwise(padded, taps, flipped, x_cells, channels, out_dtype=jnp.float32):
    planes = padded.shape[0] - 2
    y_cells = padded.shape[1] - 2
    x_pad = 2 * channels
    lanes = x_cells * channels
    chunk = min(1024, lanes)
    rows = 8 if y_cells % 8 == 0 else y_cells
    if flipped:
        taps = taps[::-1]
    gains = jnp.tile(taps.astype(jnp.float32), (1, 128 // channels))
    gains = jnp.broadcast_to(gains[:, None, :], (gains.shape[0], rows, 128))
    kernel = functools.partial(stencil_kernel, chunk, x_pad, planes, y_cells, rows)
    return pl.pallas_call(
        kernel,
        out_shape=jax.ShapeDtypeStruct((planes, y_cells, lanes), out_dtype),
    )(padded.astype(jnp.float32), gains)


def share_terms(field3, cos_table, sin_table):
    real_part = jnp.einsum("rxc,xk->krc", field3, cos_table, preferred_element_type=jnp.float32)
    imag_part = jnp.einsum("rxc,xk->krc", field3, sin_table, preferred_element_type=jnp.float32)
    return lax.psum_scatter(
        jnp.concatenate([real_part, imag_part], axis=2), "gx", scatter_dimension=0, tiled=True
    )


def share_inverse(modes_share, cos_table, sin_table, channels):
    segment = ring_gather(modes_share, "gx")
    running = jnp.einsum(
        "krc,xk->rxc", segment[:, :, :channels], cos_table, preferred_element_type=jnp.float32
    )
    return running + jnp.einsum(
        "krc,xk->rxc", segment[:, :, channels:], sin_table, preferred_element_type=jnp.float32
    )


def split_gradients(dblock, channels):
    grad_real = dblock[:, :channels, :channels] + dblock[:, channels:, channels:]
    grad_imag = dblock[:, :channels, channels:] - dblock[:, channels:, :channels]
    return jnp.stack([grad_real, grad_imag])


def sum_gradients(local_grads):
    flat = local_grads.reshape(-1, 1024)
    return butterfly_sum(butterfly_sum(flat, "gy"), "gz").reshape(local_grads.shape)


def per_device(
    features, depth_weight, expand_weight, project_weight, spec_real, spec_imag, cotangent
):
    planes, y_cells, merged = features.shape
    channels = depth_weight.shape[1]
    x_cells = merged // channels
    row_count = planes * y_cells
    mode_count = spec_real.shape[0]
    group_size = lax.axis_size("gx")
    x_length = x_cells * group_size
    x_start = lax.axis_index("gx") * x_cells
    share_size = mode_count // group_size
    cos_part, sin_part = dft_tables(
        x_start, x_cells, x_length, jnp.arange(mode_count, dtype=jnp.int32)
    )
    order = gathered_order("gx", share_size)
    cos_order, sin_order = dft_tables(x_start, x_cells, x_length, order)
    cos_scaled = scaled_table(cos_order, order, x_length)
    sin_scaled = scaled_table(sin_order, order, x_length)
    cos_fwd_scaled = scaled_table(cos_part, jnp.arange(mode_count, dtype=jnp.int32), x_length)
    sin_fwd_scaled = scaled_table(sin_part, jnp.arange(mode_count, dtype=jnp.int32), x_length)
    blocks = block_weights(spec_real, spec_imag)
    padded = spatial_rims(features, channels)
    activation = depthwise(padded, depth_weight, False, x_cells, channels, jnp.bfloat16)
    field3 = features.reshape(row_count, x_cells, channels)
    owned_blocks = lax.dynamic_slice_in_dim(
        blocks, lax.axis_index("gx") * share_size, share_size, 0
    )
    coeffs = share_terms(field3, cos_part, sin_part).astype(jnp.bfloat16)
    mixed_modes = jnp.einsum(
        "krc,kco->kro", coeffs, owned_blocks, preferred_element_type=jnp.float32
    ).astype(jnp.bfloat16)
    mixed_modes, activation = lax.optimization_barrier((mixed_modes, activation))
    activation = activation.reshape(row_count * x_cells, channels)
    hidden_pre = jnp.dot(activation, expand_weight, preferred_element_type=jnp.float32)
    hidden, hidden_slope = gelu_parts(hidden_pre)
    local_branch = jnp.dot(
        hidden.astype(jnp.bfloat16), project_weight, preferred_element_type=jnp.float32
    )
    local_branch = local_branch.reshape(row_count, x_cells, channels)
    spectral = share_inverse(mixed_modes, cos_scaled, sin_scaled, channels)
    result, slopes = gelu_parts(local_branch + spectral)
    output = result.astype(jnp.bfloat16).reshape(planes, y_cells, merged)
    grad_pre = (
        cotangent.reshape(row_count, x_cells, channels).astype(jnp.float32) * slopes
    ).astype(jnp.bfloat16)
    hidden_grad = jnp.dot(
        grad_pre.reshape(row_count * x_cells, channels),
        project_weight.T,
        preferred_element_type=jnp.float32,
    )
    grad_hidden = (hidden_grad * hidden_slope).astype(jnp.bfloat16)
    grad_act = jnp.dot(grad_hidden, expand_weight.T, preferred_element_type=jnp.float32).astype(
        jnp.bfloat16
    )
    grad_act = grad_act.reshape(planes, y_cells, merged)
    dcoef = share_terms(grad_pre, cos_fwd_scaled, sin_fwd_scaled).astype(jnp.bfloat16)
    dmode = jnp.einsum(
        "kro,kco->krc", dcoef, owned_blocks, preferred_element_type=jnp.float32
    ).astype(jnp.bfloat16)
    dblock = jnp.einsum("krc,kro->kco", coeffs, dcoef, preferred_element_type=jnp.float32)
    local_grads = split_gradients(dblock, channels)
    dmode, local_grads, grad_act = lax.optimization_barrier((dmode, local_grads, grad_act))
    spectral_grad = share_inverse(dmode, cos_order, sin_order, channels)
    grad_spec = sum_gradients(local_grads)
    padded_grad = spatial_rims(grad_act, channels)
    grad_local = depthwise(padded_grad, depth_weight, True, x_cells, channels)
    grad_features = (grad_local + spectral_grad.reshape(planes, y_cells, merged)).astype(
        jnp.bfloat16
    )
    return (output, grad_features, grad_spec)


def solution(mesh):
    placed = (P("gz", "gy", "gx"), P(), P(), P(), P(), P(), P("gz", "gy", "gx"))
    return jax.shard_map(
        per_device,
        mesh=mesh,
        in_specs=placed,
        out_specs=(P("gz", "gy", "gx"), P("gz", "gy", "gx"), P(None, "gx", None, None)),
        check_vma=False,
    )
```

```python
import functools
import math

import jax
import jax.numpy as jnp
from jax import lax
from jax.experimental import pallas as pl
from jax.experimental.pallas import tpu as pltpu
from jax.sharding import PartitionSpec as P


def padded_2(value, sides, width, wrap):
    for axis, dim in sides:
        size, length = (lax.axis_size(axis), value.shape[dim])
        up = [(i, (i + 1) % size) for i in range(size if wrap else size - 1)]
        down = [(j, i) for i, j in up]
        last = lax.slice_in_dim(value, length - width, length, axis=dim)
        leading = lax.slice_in_dim(value, 0, width, axis=dim)
        before = lax.ppermute(last, axis, up)
        after = lax.ppermute(leading, axis, down)
        value = jnp.concatenate([before, value, after], axis=dim)
    return value


def gelu_parts(values):
    normal_cdf = 0.5 * (1.0 + jax.scipy.special.erf(values * (1.0 / math.sqrt(2.0))))
    density = jnp.exp(-0.5 * values * values) * (1.0 / math.sqrt(2.0 * math.pi))
    return (values * normal_cdf, normal_cdf + values * density)


def dft_tables(offset, cells, x_length, frequency):
    position = offset + jnp.arange(cells, dtype=jnp.int32)
    phase_int = position[:, None] * frequency[None, :] % x_length
    angles = phase_int.astype(jnp.float32) * (2.0 * math.pi / x_length)
    return (jnp.cos(angles).astype(jnp.bfloat16), (-jnp.sin(angles)).astype(jnp.bfloat16))


def scaled_table(table, frequency, x_length):
    mode_scale = jnp.where(frequency == 0, 1.0, 2.0).astype(jnp.float32) / x_length
    return (table.astype(jnp.float32) * mode_scale[None, :]).astype(jnp.bfloat16)


def gathered_order(axis, share_size):
    size = lax.axis_size(axis)
    shifts = jnp.arange(size, dtype=jnp.int32)
    sources = (lax.axis_index(axis) - shifts) % size
    local = jnp.arange(share_size, dtype=jnp.int32)
    return (sources[:, None] * share_size + local[None, :]).reshape(-1)


def ring_gather(block, axis):
    size = lax.axis_size(axis)
    pieces = [block]
    for shift in range(1, size):
        pieces.append(lax.ppermute(block, axis, [(i, (i + shift) % size) for i in range(size)]))
    return jnp.concatenate(pieces, axis=0)


def butterfly_sum(value, axis):
    size = lax.axis_size(axis)
    if size & (size - 1):
        return lax.psum(value, axis)
    step = 1
    while step < size:
        value = value + lax.ppermute(value, axis, [(i, i ^ step) for i in range(size)])
        step *= 2
    return value


def block_weights(spec_real, spec_imag):
    upper_row = jnp.concatenate([spec_real, spec_imag], axis=2)
    lower_row = jnp.concatenate([-spec_imag, spec_real], axis=2)
    return jnp.concatenate([upper_row, lower_row], axis=1)


def spatial_rims(field_block, channels):
    x_wide = padded_2(field_block, (("gx", 2),), 2 * channels, True)
    return padded_2(x_wide, (("gy", 1), ("gz", 0)), 1, False)


def stencil_kernel(chunk, x_pad, y_cells, rows, lo_ref, mid_ref, hi_ref, w_ref, o_ref):
    width = chunk + 2 * x_pad
    count = o_ref.shape[1] // chunk
    shift = chunk + x_pad - x_pad // 2
    side = (chunk + x_pad) // 128
    sources = (lo_ref, mid_ref, hi_ref)

    def body(index, carry):
        base = pl.multiple_of(index * chunk, chunk)
        for row in range(0, y_cells, rows):
            left = jnp.zeros((rows, chunk + x_pad), jnp.float32)
            centre = jnp.zeros((rows, chunk), jnp.float32)
            right = jnp.zeros((rows, chunk + x_pad), jnp.float32)
            for step_z in range(3):
                for step_y in range(3):
                    window = sources[step_z][pl.ds(row + step_y, rows), pl.ds(base, width)].astype(
                        jnp.float32
                    )
                    tap = 9 * step_z + 3 * step_y
                    gain_l = jnp.concatenate([w_ref[tap]] * side, axis=1)
                    gain_c = jnp.concatenate([w_ref[tap + 1]] * (side - 1), axis=1)
                    gain_r = jnp.concatenate([w_ref[tap + 2]] * side, axis=1)
                    left = left + window[:, : chunk + x_pad] * gain_l
                    centre = centre + window[:, x_pad : x_pad + chunk] * gain_c
                    right = right + window[:, x_pad:] * gain_r
            total = (
                centre
                + pltpu.roll(left, shift, 1)[:, :chunk]
                + pltpu.roll(right, shift, 1)[:, :chunk]
            )
            o_ref[pl.ds(row, rows), pl.ds(base, chunk)] = total.astype(o_ref.dtype)
        return carry

    lax.fori_loop(0, count, body, 0)


def depthwise(padded, taps, flipped, x_cells, channels, out_dtype=jnp.float32):
    planes = padded.shape[0] - 2
    y_cells = padded.shape[1] - 2
    x_pad = 2 * channels
    lanes = x_cells * channels
    chunk = min(1024, lanes)
    rows = 8 if y_cells % 8 == 0 else y_cells
    if flipped:
        taps = taps[::-1]
    gains = jnp.tile(taps.astype(jnp.float32), (1, 128 // channels))
    gains = jnp.broadcast_to(gains[:, None, :], (gains.shape[0], rows, 128))
    kernel = functools.partial(stencil_kernel, chunk, x_pad, y_cells, rows)
    plane_block = padded.shape[1:]
    in_specs = [
        pl.BlockSpec((None,) + plane_block, functools.partial(lambda d, z: (z + d, 0, 0), d))
        for d in range(3)
    ]
    in_specs.append(pl.BlockSpec(gains.shape, lambda z: (0, 0, 0)))
    return pl.pallas_call(
        kernel,
        grid=(planes,),
        in_specs=in_specs,
        out_specs=pl.BlockSpec((None, y_cells, lanes), lambda z: (z, 0, 0)),
        out_shape=jax.ShapeDtypeStruct((planes, y_cells, lanes), out_dtype),
    )(padded, padded, padded, gains)


def share_terms(field3, cos_table, sin_table):
    real_part = jnp.einsum("rxc,xk->krc", field3, cos_table, preferred_element_type=jnp.float32)
    imag_part = jnp.einsum("rxc,xk->krc", field3, sin_table, preferred_element_type=jnp.float32)
    return lax.psum_scatter(
        jnp.concatenate([real_part, imag_part], axis=2), "gx", scatter_dimension=0, tiled=True
    )


def share_inverse(modes_share, cos_table, sin_table, channels):
    segment = ring_gather(modes_share, "gx")
    running = jnp.einsum(
        "krc,xk->rxc", segment[:, :, :channels], cos_table, preferred_element_type=jnp.float32
    )
    return running + jnp.einsum(
        "krc,xk->rxc", segment[:, :, channels:], sin_table, preferred_element_type=jnp.float32
    )


def split_gradients(dblock, channels):
    grad_real = dblock[:, :channels, :channels] + dblock[:, channels:, channels:]
    grad_imag = dblock[:, :channels, channels:] - dblock[:, channels:, :channels]
    return jnp.stack([grad_real, grad_imag])


def sum_gradients(local_grads):
    flat = local_grads.reshape(-1, 1024)
    return butterfly_sum(butterfly_sum(flat, "gy"), "gz").reshape(local_grads.shape)


def per_device(
    features, depth_weight, expand_weight, project_weight, spec_real, spec_imag, cotangent
):
    planes, y_cells, merged = features.shape
    channels = depth_weight.shape[1]
    x_cells = merged // channels
    row_count = planes * y_cells
    mode_count = spec_real.shape[0]
    group_size = lax.axis_size("gx")
    x_length = x_cells * group_size
    x_start = lax.axis_index("gx") * x_cells
    share_size = mode_count // group_size
    cos_part, sin_part = dft_tables(
        x_start, x_cells, x_length, jnp.arange(mode_count, dtype=jnp.int32)
    )
    order = gathered_order("gx", share_size)
    cos_order, sin_order = dft_tables(x_start, x_cells, x_length, order)
    cos_scaled = scaled_table(cos_order, order, x_length)
    sin_scaled = scaled_table(sin_order, order, x_length)
    cos_fwd_scaled = scaled_table(cos_part, jnp.arange(mode_count, dtype=jnp.int32), x_length)
    sin_fwd_scaled = scaled_table(sin_part, jnp.arange(mode_count, dtype=jnp.int32), x_length)
    blocks = block_weights(spec_real, spec_imag)
    padded = spatial_rims(features, channels)
    activation = depthwise(padded, depth_weight, False, x_cells, channels, jnp.bfloat16)
    field3 = features.reshape(row_count, x_cells, channels)
    owned_blocks = lax.dynamic_slice_in_dim(
        blocks, lax.axis_index("gx") * share_size, share_size, 0
    )
    coeffs = share_terms(field3, cos_part, sin_part).astype(jnp.bfloat16)
    mixed_modes = jnp.einsum(
        "krc,kco->kro", coeffs, owned_blocks, preferred_element_type=jnp.float32
    ).astype(jnp.bfloat16)
    mixed_modes, activation = lax.optimization_barrier((mixed_modes, activation))
    activation = activation.reshape(row_count * x_cells, channels)
    hidden_pre = jnp.dot(activation, expand_weight, preferred_element_type=jnp.float32)
    hidden, hidden_slope = gelu_parts(hidden_pre)
    local_branch = jnp.dot(
        hidden.astype(jnp.bfloat16), project_weight, preferred_element_type=jnp.float32
    )
    local_branch = local_branch.reshape(row_count, x_cells, channels)
    spectral = share_inverse(mixed_modes, cos_scaled, sin_scaled, channels)
    result, slopes = gelu_parts(local_branch + spectral)
    output = result.astype(jnp.bfloat16).reshape(planes, y_cells, merged)
    grad_pre = (
        cotangent.reshape(row_count, x_cells, channels).astype(jnp.float32) * slopes
    ).astype(jnp.bfloat16)
    hidden_grad = jnp.dot(
        grad_pre.reshape(row_count * x_cells, channels),
        project_weight.T,
        preferred_element_type=jnp.float32,
    )
    grad_hidden = (hidden_grad * hidden_slope).astype(jnp.bfloat16)
    grad_act = jnp.dot(grad_hidden, expand_weight.T, preferred_element_type=jnp.float32).astype(
        jnp.bfloat16
    )
    grad_act = grad_act.reshape(planes, y_cells, merged)
    dcoef = share_terms(grad_pre, cos_fwd_scaled, sin_fwd_scaled).astype(jnp.bfloat16)
    dmode = jnp.einsum(
        "kro,kco->krc", dcoef, owned_blocks, preferred_element_type=jnp.float32
    ).astype(jnp.bfloat16)
    dblock = jnp.einsum("krc,kro->kco", coeffs, dcoef, preferred_element_type=jnp.float32)
    local_grads = split_gradients(dblock, channels)
    dmode, local_grads, grad_act = lax.optimization_barrier((dmode, local_grads, grad_act))
    spectral_grad = share_inverse(dmode, cos_order, sin_order, channels)
    grad_spec = sum_gradients(local_grads)
    padded_grad = spatial_rims(grad_act, channels)
    grad_local = depthwise(padded_grad, depth_weight, True, x_cells, channels)
    grad_features = (grad_local + spectral_grad.reshape(planes, y_cells, merged)).astype(
        jnp.bfloat16
    )
    return (output, grad_features, grad_spec)


def solution(mesh):
    placed = (P("gz", "gy", "gx"), P(), P(), P(), P(), P(), P("gz", "gy", "gx"))
    return jax.shard_map(
        per_device,
        mesh=mesh,
        in_specs=placed,
        out_specs=(P("gz", "gy", "gx"), P("gz", "gy", "gx"), P(None, "gx", None, None)),
        check_vma=False,
    )
```

```python
import functools
import math

import jax
import jax.numpy as jnp
from jax import lax
from jax.experimental import pallas as pl
from jax.experimental.pallas import tpu as pltpu
from jax.sharding import PartitionSpec as P


def padded_2(value, sides, width, wrap):
    for axis, dim in sides:
        size, length = (lax.axis_size(axis), value.shape[dim])
        up = [(i, (i + 1) % size) for i in range(size if wrap else size - 1)]
        down = [(j, i) for i, j in up]
        last = lax.slice_in_dim(value, length - width, length, axis=dim)
        leading = lax.slice_in_dim(value, 0, width, axis=dim)
        before = lax.ppermute(last, axis, up)
        after = lax.ppermute(leading, axis, down)
        value = jnp.concatenate([before, value, after], axis=dim)
    return value


def gelu_parts(values):
    normal_cdf = 0.5 * (1.0 + jax.scipy.special.erf(values * (1.0 / math.sqrt(2.0))))
    density = jnp.exp(-0.5 * values * values) * (1.0 / math.sqrt(2.0 * math.pi))
    return (values * normal_cdf, normal_cdf + values * density)


def dft_tables(offset, cells, x_length, frequency):
    position = offset + jnp.arange(cells, dtype=jnp.int32)
    phase_int = position[:, None] * frequency[None, :] % x_length
    angles = phase_int.astype(jnp.float32) * (2.0 * math.pi / x_length)
    return (jnp.cos(angles).astype(jnp.bfloat16), (-jnp.sin(angles)).astype(jnp.bfloat16))


def scaled_table(table, frequency, x_length):
    mode_scale = jnp.where(frequency == 0, 1.0, 2.0).astype(jnp.float32) / x_length
    return (table.astype(jnp.float32) * mode_scale[None, :]).astype(jnp.bfloat16)


def gathered_order(axis, share_size):
    size = lax.axis_size(axis)
    shifts = jnp.arange(size, dtype=jnp.int32)
    sources = (lax.axis_index(axis) - shifts) % size
    local = jnp.arange(share_size, dtype=jnp.int32)
    return (sources[:, None] * share_size + local[None, :]).reshape(-1)


def ring_gather(block, axis):
    size = lax.axis_size(axis)
    pieces = [block]
    for shift in range(1, size):
        pieces.append(lax.ppermute(block, axis, [(i, (i + shift) % size) for i in range(size)]))
    return jnp.concatenate(pieces, axis=0)


def ring_reduce_scatter(value, axis):
    size = lax.axis_size(axis)
    share = value.shape[0] // size
    me = lax.axis_index(axis)
    total = lax.dynamic_slice_in_dim(value, me * share, share, 0)
    for shift in range(1, size):
        piece = lax.dynamic_slice_in_dim(value, ((me + shift) % size) * share, share, 0)
        total = total + lax.ppermute(piece, axis, [(i, (i + shift) % size) for i in range(size)])
    return total


def butterfly_sum(value, axis):
    size = lax.axis_size(axis)
    if size & (size - 1):
        return lax.psum(value, axis)
    step = 1
    while step < size:
        value = value + lax.ppermute(value, axis, [(i, i ^ step) for i in range(size)])
        step *= 2
    return value


def block_weights(spec_real, spec_imag):
    upper_row = jnp.concatenate([spec_real, spec_imag], axis=2)
    lower_row = jnp.concatenate([-spec_imag, spec_real], axis=2)
    return jnp.concatenate([upper_row, lower_row], axis=1)


def spatial_rims(field_block, channels):
    x_wide = padded_2(field_block, (("gx", 2),), 2 * channels, True)
    return padded_2(x_wide, (("gy", 1), ("gz", 0)), 1, False)


def stencil_kernel(chunk, x_pad, y_cells, rows, lo_ref, mid_ref, hi_ref, w_ref, o_ref):
    width = chunk + 2 * x_pad
    count = o_ref.shape[1] // chunk
    shift = chunk + x_pad - x_pad // 2
    side = (chunk + x_pad) // 128
    sources = (lo_ref, mid_ref, hi_ref)

    def body(index, carry):
        base = pl.multiple_of(index * chunk, chunk)
        for row in range(0, y_cells, rows):
            left = jnp.zeros((rows, chunk + x_pad), jnp.float32)
            centre = jnp.zeros((rows, chunk), jnp.float32)
            right = jnp.zeros((rows, chunk + x_pad), jnp.float32)
            for step_z in range(3):
                for step_y in range(3):
                    window = sources[step_z][pl.ds(row + step_y, rows), pl.ds(base, width)].astype(
                        jnp.float32
                    )
                    tap = 9 * step_z + 3 * step_y
                    gain_l = jnp.concatenate([w_ref[tap]] * side, axis=1)
                    gain_c = jnp.concatenate([w_ref[tap + 1]] * (side - 1), axis=1)
                    gain_r = jnp.concatenate([w_ref[tap + 2]] * side, axis=1)
                    left = left + window[:, : chunk + x_pad] * gain_l
                    centre = centre + window[:, x_pad : x_pad + chunk] * gain_c
                    right = right + window[:, x_pad:] * gain_r
            total = (
                centre
                + pltpu.roll(left, shift, 1)[:, :chunk]
                + pltpu.roll(right, shift, 1)[:, :chunk]
            )
            o_ref[pl.ds(row, rows), pl.ds(base, chunk)] = total.astype(o_ref.dtype)
        return carry

    lax.fori_loop(0, count, body, 0)


def depthwise(padded, taps, flipped, x_cells, channels, out_dtype=jnp.float32):
    planes = padded.shape[0] - 2
    y_cells = padded.shape[1] - 2
    x_pad = 2 * channels
    lanes = x_cells * channels
    chunk = min(1024, lanes)
    rows = 8 if y_cells % 8 == 0 else y_cells
    if flipped:
        taps = taps[::-1]
    gains = jnp.tile(taps.astype(jnp.float32), (1, 128 // channels))
    gains = jnp.broadcast_to(gains[:, None, :], (gains.shape[0], rows, 128))
    kernel = functools.partial(stencil_kernel, chunk, x_pad, y_cells, rows)
    plane_block = padded.shape[1:]
    in_specs = [
        pl.BlockSpec((None,) + plane_block, functools.partial(lambda d, z: (z + d, 0, 0), d))
        for d in range(3)
    ]
    in_specs.append(pl.BlockSpec(gains.shape, lambda z: (0, 0, 0)))
    return pl.pallas_call(
        kernel,
        grid=(planes,),
        in_specs=in_specs,
        out_specs=pl.BlockSpec((None, y_cells, lanes), lambda z: (z, 0, 0)),
        out_shape=jax.ShapeDtypeStruct((planes, y_cells, lanes), out_dtype),
    )(padded, padded, padded, gains)


def share_terms(field3, cos_table, sin_table):
    real_part = jnp.einsum("rxc,xk->krc", field3, cos_table, preferred_element_type=jnp.float32)
    imag_part = jnp.einsum("rxc,xk->krc", field3, sin_table, preferred_element_type=jnp.float32)
    return ring_reduce_scatter(jnp.concatenate([real_part, imag_part], axis=2), "gx")


def share_inverse(modes_share, cos_table, sin_table, channels):
    segment = ring_gather(modes_share, "gx")
    running = jnp.einsum(
        "krc,xk->rxc", segment[:, :, :channels], cos_table, preferred_element_type=jnp.float32
    )
    return running + jnp.einsum(
        "krc,xk->rxc", segment[:, :, channels:], sin_table, preferred_element_type=jnp.float32
    )


def split_gradients(dblock, channels):
    grad_real = dblock[:, :channels, :channels] + dblock[:, channels:, channels:]
    grad_imag = dblock[:, :channels, channels:] - dblock[:, channels:, :channels]
    return jnp.stack([grad_real, grad_imag])


def sum_gradients(local_grads):
    flat = local_grads.reshape(-1, 1024)
    return butterfly_sum(butterfly_sum(flat, "gy"), "gz").reshape(local_grads.shape)


def per_device(
    features, depth_weight, expand_weight, project_weight, spec_real, spec_imag, cotangent
):
    planes, y_cells, merged = features.shape
    channels = depth_weight.shape[1]
    x_cells = merged // channels
    row_count = planes * y_cells
    mode_count = spec_real.shape[0]
    group_size = lax.axis_size("gx")
    x_length = x_cells * group_size
    x_start = lax.axis_index("gx") * x_cells
    share_size = mode_count // group_size
    cos_part, sin_part = dft_tables(
        x_start, x_cells, x_length, jnp.arange(mode_count, dtype=jnp.int32)
    )
    order = gathered_order("gx", share_size)
    cos_order, sin_order = dft_tables(x_start, x_cells, x_length, order)
    cos_scaled = scaled_table(cos_order, order, x_length)
    sin_scaled = scaled_table(sin_order, order, x_length)
    cos_fwd_scaled = scaled_table(cos_part, jnp.arange(mode_count, dtype=jnp.int32), x_length)
    sin_fwd_scaled = scaled_table(sin_part, jnp.arange(mode_count, dtype=jnp.int32), x_length)
    blocks = block_weights(spec_real, spec_imag)
    padded = spatial_rims(features, channels)
    activation = depthwise(padded, depth_weight, False, x_cells, channels, jnp.bfloat16)
    field3 = features.reshape(row_count, x_cells, channels)
    owned_blocks = lax.dynamic_slice_in_dim(
        blocks, lax.axis_index("gx") * share_size, share_size, 0
    )
    coeffs = share_terms(field3, cos_part, sin_part).astype(jnp.bfloat16)
    mixed_modes = jnp.einsum(
        "krc,kco->kro", coeffs, owned_blocks, preferred_element_type=jnp.float32
    ).astype(jnp.bfloat16)
    mixed_modes, activation = lax.optimization_barrier((mixed_modes, activation))
    activation = activation.reshape(row_count * x_cells, channels)
    hidden_pre = jnp.dot(activation, expand_weight, preferred_element_type=jnp.float32)
    hidden, hidden_slope = gelu_parts(hidden_pre)
    local_branch = jnp.dot(
        hidden.astype(jnp.bfloat16), project_weight, preferred_element_type=jnp.float32
    )
    local_branch = local_branch.reshape(row_count, x_cells, channels)
    spectral = share_inverse(mixed_modes, cos_scaled, sin_scaled, channels)
    result, slopes = gelu_parts(local_branch + spectral)
    output = result.astype(jnp.bfloat16).reshape(planes, y_cells, merged)
    grad_pre = (
        cotangent.reshape(row_count, x_cells, channels).astype(jnp.float32) * slopes
    ).astype(jnp.bfloat16)
    hidden_grad = jnp.dot(
        grad_pre.reshape(row_count * x_cells, channels),
        project_weight.T,
        preferred_element_type=jnp.float32,
    )
    grad_hidden = (hidden_grad * hidden_slope).astype(jnp.bfloat16)
    grad_act = jnp.dot(grad_hidden, expand_weight.T, preferred_element_type=jnp.float32).astype(
        jnp.bfloat16
    )
    grad_act = grad_act.reshape(planes, y_cells, merged)
    dcoef = share_terms(grad_pre, cos_fwd_scaled, sin_fwd_scaled).astype(jnp.bfloat16)
    dmode = jnp.einsum(
        "kro,kco->krc", dcoef, owned_blocks, preferred_element_type=jnp.float32
    ).astype(jnp.bfloat16)
    dblock = jnp.einsum("krc,kro->kco", coeffs, dcoef, preferred_element_type=jnp.float32)
    local_grads = split_gradients(dblock, channels)
    dmode, local_grads, grad_act = lax.optimization_barrier((dmode, local_grads, grad_act))
    spectral_grad = share_inverse(dmode, cos_order, sin_order, channels)
    grad_spec = sum_gradients(local_grads)
    padded_grad = spatial_rims(grad_act, channels)
    grad_local = depthwise(padded_grad, depth_weight, True, x_cells, channels)
    grad_features = (grad_local + spectral_grad.reshape(planes, y_cells, merged)).astype(
        jnp.bfloat16
    )
    return (output, grad_features, grad_spec)


def solution(mesh):
    placed = (P("gz", "gy", "gx"), P(), P(), P(), P(), P(), P("gz", "gy", "gx"))
    return jax.shard_map(
        per_device,
        mesh=mesh,
        in_specs=placed,
        out_specs=(P("gz", "gy", "gx"), P("gz", "gy", "gx"), P(None, "gx", None, None)),
        check_vma=False,
    )
```

```python
import functools
import math

import jax
import jax.numpy as jnp
from jax import lax
from jax.experimental import pallas as pl
from jax.experimental.pallas import tpu as pltpu
from jax.sharding import PartitionSpec as P


def padded_2(value, sides, width, wrap):
    for axis, dim in sides:
        size, length = (lax.axis_size(axis), value.shape[dim])
        up = [(i, (i + 1) % size) for i in range(size if wrap else size - 1)]
        down = [(j, i) for i, j in up]
        last = lax.slice_in_dim(value, length - width, length, axis=dim)
        leading = lax.slice_in_dim(value, 0, width, axis=dim)
        before = lax.ppermute(last, axis, up)
        after = lax.ppermute(leading, axis, down)
        value = jnp.concatenate([before, value, after], axis=dim)
    return value


def gelu_parts(values):
    normal_cdf = 0.5 * (1.0 + jax.scipy.special.erf(values * (1.0 / math.sqrt(2.0))))
    density = jnp.exp(-0.5 * values * values) * (1.0 / math.sqrt(2.0 * math.pi))
    return (values * normal_cdf, normal_cdf + values * density)


def dft_tables(offset, cells, x_length, frequency):
    position = offset + jnp.arange(cells, dtype=jnp.int32)
    phase_int = position[:, None] * frequency[None, :] % x_length
    angles = phase_int.astype(jnp.float32) * (2.0 * math.pi / x_length)
    return (jnp.cos(angles).astype(jnp.bfloat16), (-jnp.sin(angles)).astype(jnp.bfloat16))


def scaled_table(table, frequency, x_length):
    mode_scale = jnp.where(frequency == 0, 1.0, 2.0).astype(jnp.float32) / x_length
    return (table.astype(jnp.float32) * mode_scale[None, :]).astype(jnp.bfloat16)


def gathered_order(axis, share_size):
    size = lax.axis_size(axis)
    shifts = jnp.arange(size, dtype=jnp.int32)
    sources = (lax.axis_index(axis) - shifts) % size
    local = jnp.arange(share_size, dtype=jnp.int32)
    return (sources[:, None] * share_size + local[None, :]).reshape(-1)


def ring_gather(block, axis):
    size = lax.axis_size(axis)
    pieces = [block]
    for shift in range(1, size):
        pieces.append(lax.ppermute(block, axis, [(i, (i + shift) % size) for i in range(size)]))
    return jnp.concatenate(pieces, axis=0)


def ring_reduce_scatter(value, axis):
    size = lax.axis_size(axis)
    share = value.shape[0] // size
    me = lax.axis_index(axis)
    total = lax.dynamic_slice_in_dim(value, me * share, share, 0)
    for shift in range(1, size):
        piece = lax.dynamic_slice_in_dim(value, ((me + shift) % size) * share, share, 0)
        total = total + lax.ppermute(piece, axis, [(i, (i + shift) % size) for i in range(size)])
    return total


def butterfly_sum(value, axis):
    size = lax.axis_size(axis)
    if size & (size - 1):
        return lax.psum(value, axis)
    step = 1
    while step < size:
        value = value.astype(jnp.bfloat16)
        value = value.astype(jnp.float32) + lax.ppermute(
            value, axis, [(i, i ^ step) for i in range(size)]
        ).astype(jnp.float32)
        step *= 2
    return value


def block_weights(spec_real, spec_imag):
    upper_row = jnp.concatenate([spec_real, spec_imag], axis=2)
    lower_row = jnp.concatenate([-spec_imag, spec_real], axis=2)
    return jnp.concatenate([upper_row, lower_row], axis=1)


def spatial_rims(field_block, channels):
    x_wide = padded_2(field_block, (("gx", 2),), 2 * channels, True)
    return padded_2(x_wide, (("gy", 1), ("gz", 0)), 1, False)


def stencil_kernel(chunk, x_pad, y_cells, rows, lo_ref, mid_ref, hi_ref, w_ref, o_ref):
    width = chunk + 2 * x_pad
    count = o_ref.shape[1] // chunk
    shift = chunk + x_pad - x_pad // 2
    side = (chunk + x_pad) // 128
    sources = (lo_ref, mid_ref, hi_ref)

    def body(index, carry):
        base = pl.multiple_of(index * chunk, chunk)
        for row in range(0, y_cells, rows):
            left = jnp.zeros((rows, chunk + x_pad), jnp.float32)
            centre = jnp.zeros((rows, chunk), jnp.float32)
            right = jnp.zeros((rows, chunk + x_pad), jnp.float32)
            for step_z in range(3):
                for step_y in range(3):
                    window = sources[step_z][pl.ds(row + step_y, rows), pl.ds(base, width)].astype(
                        jnp.float32
                    )
                    tap = 9 * step_z + 3 * step_y
                    gain_l = jnp.concatenate([w_ref[tap]] * side, axis=1)
                    gain_c = jnp.concatenate([w_ref[tap + 1]] * (side - 1), axis=1)
                    gain_r = jnp.concatenate([w_ref[tap + 2]] * side, axis=1)
                    left = left + window[:, : chunk + x_pad] * gain_l
                    centre = centre + window[:, x_pad : x_pad + chunk] * gain_c
                    right = right + window[:, x_pad:] * gain_r
            total = (
                centre
                + pltpu.roll(left, shift, 1)[:, :chunk]
                + pltpu.roll(right, shift, 1)[:, :chunk]
            )
            o_ref[pl.ds(row, rows), pl.ds(base, chunk)] = total.astype(o_ref.dtype)
        return carry

    lax.fori_loop(0, count, body, 0)


def depthwise(padded, taps, flipped, x_cells, channels, out_dtype=jnp.float32):
    planes = padded.shape[0] - 2
    y_cells = padded.shape[1] - 2
    x_pad = 2 * channels
    lanes = x_cells * channels
    chunk = min(1024, lanes)
    rows = 8 if y_cells % 8 == 0 else y_cells
    if flipped:
        taps = taps[::-1]
    gains = jnp.tile(taps.astype(jnp.float32), (1, 128 // channels))
    gains = jnp.broadcast_to(gains[:, None, :], (gains.shape[0], rows, 128))
    kernel = functools.partial(stencil_kernel, chunk, x_pad, y_cells, rows)
    plane_block = padded.shape[1:]
    in_specs = [
        pl.BlockSpec((None,) + plane_block, functools.partial(lambda d, z: (z + d, 0, 0), d))
        for d in range(3)
    ]
    in_specs.append(pl.BlockSpec(gains.shape, lambda z: (0, 0, 0)))
    return pl.pallas_call(
        kernel,
        grid=(planes,),
        in_specs=in_specs,
        out_specs=pl.BlockSpec((None, y_cells, lanes), lambda z: (z, 0, 0)),
        out_shape=jax.ShapeDtypeStruct((planes, y_cells, lanes), out_dtype),
    )(padded, padded, padded, gains)


def share_terms(field3, cos_table, sin_table):
    real_part = jnp.einsum("rxc,xk->krc", field3, cos_table, preferred_element_type=jnp.float32)
    imag_part = jnp.einsum("rxc,xk->krc", field3, sin_table, preferred_element_type=jnp.float32)
    return ring_reduce_scatter(jnp.concatenate([real_part, imag_part], axis=2), "gx")


def share_inverse(modes_share, cos_table, sin_table, channels):
    segment = ring_gather(modes_share, "gx")
    running = jnp.einsum(
        "krc,xk->rxc", segment[:, :, :channels], cos_table, preferred_element_type=jnp.float32
    )
    return running + jnp.einsum(
        "krc,xk->rxc", segment[:, :, channels:], sin_table, preferred_element_type=jnp.float32
    )


def split_gradients(dblock, channels):
    grad_real = dblock[:, :channels, :channels] + dblock[:, channels:, channels:]
    grad_imag = dblock[:, :channels, channels:] - dblock[:, channels:, :channels]
    return jnp.stack([grad_real, grad_imag])


def sum_gradients(local_grads):
    flat = local_grads.reshape(-1, 1024)
    return butterfly_sum(butterfly_sum(flat, "gy"), "gz").reshape(local_grads.shape)


def per_device(
    features, depth_weight, expand_weight, project_weight, spec_real, spec_imag, cotangent
):
    planes, y_cells, merged = features.shape
    channels = depth_weight.shape[1]
    x_cells = merged // channels
    row_count = planes * y_cells
    mode_count = spec_real.shape[0]
    group_size = lax.axis_size("gx")
    x_length = x_cells * group_size
    x_start = lax.axis_index("gx") * x_cells
    share_size = mode_count // group_size
    cos_part, sin_part = dft_tables(
        x_start, x_cells, x_length, jnp.arange(mode_count, dtype=jnp.int32)
    )
    order = gathered_order("gx", share_size)
    cos_order, sin_order = dft_tables(x_start, x_cells, x_length, order)
    cos_scaled = scaled_table(cos_order, order, x_length)
    sin_scaled = scaled_table(sin_order, order, x_length)
    cos_fwd_scaled = scaled_table(cos_part, jnp.arange(mode_count, dtype=jnp.int32), x_length)
    sin_fwd_scaled = scaled_table(sin_part, jnp.arange(mode_count, dtype=jnp.int32), x_length)
    blocks = block_weights(spec_real, spec_imag)
    padded = spatial_rims(features, channels)
    activation = depthwise(padded, depth_weight, False, x_cells, channels, jnp.bfloat16)
    field3 = features.reshape(row_count, x_cells, channels)
    owned_blocks = lax.dynamic_slice_in_dim(
        blocks, lax.axis_index("gx") * share_size, share_size, 0
    )
    coeffs = share_terms(field3, cos_part, sin_part).astype(jnp.bfloat16)
    mixed_modes = jnp.einsum(
        "krc,kco->kro", coeffs, owned_blocks, preferred_element_type=jnp.float32
    ).astype(jnp.bfloat16)
    mixed_modes, activation = lax.optimization_barrier((mixed_modes, activation))
    activation = activation.reshape(row_count * x_cells, channels)
    hidden_pre = jnp.dot(activation, expand_weight, preferred_element_type=jnp.float32)
    hidden, hidden_slope = gelu_parts(hidden_pre)
    local_branch = jnp.dot(
        hidden.astype(jnp.bfloat16), project_weight, preferred_element_type=jnp.float32
    )
    local_branch = local_branch.reshape(row_count, x_cells, channels)
    spectral = share_inverse(mixed_modes, cos_scaled, sin_scaled, channels)
    result, slopes = gelu_parts(local_branch + spectral)
    output = result.astype(jnp.bfloat16).reshape(planes, y_cells, merged)
    grad_pre = (
        cotangent.reshape(row_count, x_cells, channels).astype(jnp.float32) * slopes
    ).astype(jnp.bfloat16)
    hidden_grad = jnp.dot(
        grad_pre.reshape(row_count * x_cells, channels),
        project_weight.T,
        preferred_element_type=jnp.float32,
    )
    grad_hidden = (hidden_grad * hidden_slope).astype(jnp.bfloat16)
    grad_act = jnp.dot(grad_hidden, expand_weight.T, preferred_element_type=jnp.float32).astype(
        jnp.bfloat16
    )
    grad_act = grad_act.reshape(planes, y_cells, merged)
    dcoef = share_terms(grad_pre, cos_fwd_scaled, sin_fwd_scaled).astype(jnp.bfloat16)
    dmode = jnp.einsum(
        "kro,kco->krc", dcoef, owned_blocks, preferred_element_type=jnp.float32
    ).astype(jnp.bfloat16)
    dblock = jnp.einsum("krc,kro->kco", coeffs, dcoef, preferred_element_type=jnp.float32)
    local_grads = split_gradients(dblock, channels)
    dmode, local_grads, grad_act = lax.optimization_barrier((dmode, local_grads, grad_act))
    spectral_grad = share_inverse(dmode, cos_order, sin_order, channels)
    grad_spec = sum_gradients(local_grads)
    padded_grad = spatial_rims(grad_act, channels)
    grad_local = depthwise(padded_grad, depth_weight, True, x_cells, channels)
    grad_features = (grad_local + spectral_grad.reshape(planes, y_cells, merged)).astype(
        jnp.bfloat16
    )
    return (output, grad_features, grad_spec)


def solution(mesh):
    placed = (P("gz", "gy", "gx"), P(), P(), P(), P(), P(), P("gz", "gy", "gx"))
    return jax.shard_map(
        per_device,
        mesh=mesh,
        in_specs=placed,
        out_specs=(P("gz", "gy", "gx"), P("gz", "gy", "gx"), P(None, "gx", None, None)),
        check_vma=False,
    )
```

```python
import functools
import math

import jax
import jax.numpy as jnp
from jax import lax
from jax.experimental import pallas as pl
from jax.experimental.pallas import tpu as pltpu
from jax.sharding import PartitionSpec as P


def padded_2(value, sides, width, wrap):
    for axis, dim in sides:
        size, length = (lax.axis_size(axis), value.shape[dim])
        up = [(i, (i + 1) % size) for i in range(size if wrap else size - 1)]
        down = [(j, i) for i, j in up]
        last = lax.slice_in_dim(value, length - width, length, axis=dim)
        leading = lax.slice_in_dim(value, 0, width, axis=dim)
        before = lax.ppermute(last, axis, up)
        after = lax.ppermute(leading, axis, down)
        value = jnp.concatenate([before, value, after], axis=dim)
    return value


def gelu_parts(values):
    normal_cdf = 0.5 * (1.0 + jax.scipy.special.erf(values * (1.0 / math.sqrt(2.0))))
    density = jnp.exp(-0.5 * values * values) * (1.0 / math.sqrt(2.0 * math.pi))
    return (values * normal_cdf, normal_cdf + values * density)


def dft_tables(offset, cells, x_length, frequency):
    position = offset + jnp.arange(cells, dtype=jnp.int32)
    phase_int = position[:, None] * frequency[None, :] % x_length
    angles = phase_int.astype(jnp.float32) * (2.0 * math.pi / x_length)
    return (jnp.cos(angles).astype(jnp.bfloat16), (-jnp.sin(angles)).astype(jnp.bfloat16))


def scaled_table(table, frequency, x_length):
    mode_scale = jnp.where(frequency == 0, 1.0, 2.0).astype(jnp.float32) / x_length
    return (table.astype(jnp.float32) * mode_scale[None, :]).astype(jnp.bfloat16)


def gathered_order(axis, share_size):
    size = lax.axis_size(axis)
    shifts = jnp.arange(size, dtype=jnp.int32)
    sources = (lax.axis_index(axis) - shifts) % size
    local = jnp.arange(share_size, dtype=jnp.int32)
    return (sources[:, None] * share_size + local[None, :]).reshape(-1)


def ring_gather(block, axis):
    size = lax.axis_size(axis)
    pieces = [block]
    for shift in range(1, size):
        pieces.append(lax.ppermute(block, axis, [(i, (i + shift) % size) for i in range(size)]))
    return jnp.concatenate(pieces, axis=0)


def ring_reduce_scatter(value, axis):
    size = lax.axis_size(axis)
    share = value.shape[0] // size
    me = lax.axis_index(axis)
    total = lax.dynamic_slice_in_dim(value, me * share, share, 0)
    for shift in range(1, size):
        piece = lax.dynamic_slice_in_dim(value, ((me + shift) % size) * share, share, 0)
        total = total + lax.ppermute(piece, axis, [(i, (i + shift) % size) for i in range(size)])
    return total


def butterfly_sum(value, axis):
    size = lax.axis_size(axis)
    if size & (size - 1):
        return lax.psum(value, axis)
    step = 1
    while step < size:
        value = value.astype(jnp.bfloat16)
        value = value.astype(jnp.float32) + lax.ppermute(
            value, axis, [(i, i ^ step) for i in range(size)]
        ).astype(jnp.float32)
        step *= 2
    return value


def block_weights(spec_real, spec_imag):
    upper_row = jnp.concatenate([spec_real, spec_imag], axis=2)
    lower_row = jnp.concatenate([-spec_imag, spec_real], axis=2)
    return jnp.concatenate([upper_row, lower_row], axis=1)


def spatial_rims(field_block, channels):
    x_wide = padded_2(field_block, (("gx", 2),), 2 * channels, True)
    inner = padded_2(x_wide, (("gy", 1),), 1, False)
    size = lax.axis_size("gz")
    up = [(i, i + 1) for i in range(size - 1)]
    down = [(j, i) for i, j in up]
    below = lax.ppermute(inner[-1:], "gz", up)
    above = lax.ppermute(inner[:1], "gz", down)
    return (inner, below, above)


def stencil_kernel(chunk, x_pad, y_cells, rows, plan, sources, has_acc, *refs):
    src_refs = refs[:sources]
    acc_ref = refs[sources] if has_acc else None
    w_ref, o_ref = refs[sources + has_acc :]
    width = chunk + 2 * x_pad
    count = o_ref.shape[2] // chunk
    shift = chunk + x_pad - x_pad // 2
    side = (chunk + x_pad) // 128

    def body(index, carry):
        base = pl.multiple_of(index * chunk, chunk)
        for plane, terms in enumerate(plan):
            for row in range(0, y_cells, rows):
                left = jnp.zeros((rows, chunk + x_pad), jnp.float32)
                centre = jnp.zeros((rows, chunk), jnp.float32)
                right = jnp.zeros((rows, chunk + x_pad), jnp.float32)
                for source, source_plane, step_z in terms:
                    for step_y in range(3):
                        window = src_refs[source][
                            source_plane, pl.ds(row + step_y, rows), pl.ds(base, width)
                        ].astype(jnp.float32)
                        tap = 9 * step_z + 3 * step_y
                        gain_l = jnp.concatenate([w_ref[tap]] * side, axis=1)
                        gain_c = jnp.concatenate([w_ref[tap + 1]] * (side - 1), axis=1)
                        gain_r = jnp.concatenate([w_ref[tap + 2]] * side, axis=1)
                        left = left + window[:, : chunk + x_pad] * gain_l
                        centre = centre + window[:, x_pad : x_pad + chunk] * gain_c
                        right = right + window[:, x_pad:] * gain_r
                total = (
                    centre
                    + pltpu.roll(left, shift, 1)[:, :chunk]
                    + pltpu.roll(right, shift, 1)[:, :chunk]
                )
                if has_acc:
                    total = total + acc_ref[plane, pl.ds(row, rows), pl.ds(base, chunk)]
                o_ref[plane, pl.ds(row, rows), pl.ds(base, chunk)] = total.astype(o_ref.dtype)
        return carry

    lax.fori_loop(0, count, body, 0)


def stencil_call(plan, inputs, acc, gains, y_cells, lanes, channels, out_dtype):
    chunk = min(1024, lanes)
    rows = 8 if y_cells % 8 == 0 else y_cells
    kernel = functools.partial(
        stencil_kernel, chunk, 2 * channels, y_cells, rows, plan, len(inputs), acc is not None
    )
    operands = list(inputs) + ([acc] if acc is not None else []) + [gains]
    return pl.pallas_call(
        kernel,
        out_shape=jax.ShapeDtypeStruct((len(plan), y_cells, lanes), out_dtype),
    )(*operands)


def depthwise(rims, taps, flipped, x_cells, channels, out_dtype=jnp.float32):
    inner, below, above = rims
    planes = inner.shape[0]
    y_cells = inner.shape[1] - 2
    lanes = x_cells * channels
    rows = 8 if y_cells % 8 == 0 else y_cells
    if flipped:
        taps = taps[::-1]
    gains = jnp.tile(taps.astype(jnp.float32), (1, 128 // channels))
    gains = jnp.broadcast_to(gains[:, None, :], (gains.shape[0], rows, 128))
    local_plan = tuple(
        tuple((0, plane + step_z - 1, step_z) for step_z in range(3) if 0 <= plane + step_z - 1 < planes)
        for plane in range(planes)
    )
    local = stencil_call(local_plan, (inner,), None, gains, y_cells, lanes, channels, jnp.float32)
    rim_plan = tuple(
        ((((0, 0, 0),) if plane == 0 else ()) + (((1, 0, 2),) if plane == planes - 1 else ()))
        for plane in range(planes)
    )
    return stencil_call(rim_plan, (below, above), local, gains, y_cells, lanes, channels, out_dtype)


def share_terms(field3, cos_table, sin_table):
    real_part = jnp.einsum("rxc,xk->krc", field3, cos_table, preferred_element_type=jnp.float32)
    imag_part = jnp.einsum("rxc,xk->krc", field3, sin_table, preferred_element_type=jnp.float32)
    return ring_reduce_scatter(jnp.concatenate([real_part, imag_part], axis=2), "gx")


def share_inverse(modes_share, cos_table, sin_table, channels):
    segment = ring_gather(modes_share, "gx")
    running = jnp.einsum(
        "krc,xk->rxc", segment[:, :, :channels], cos_table, preferred_element_type=jnp.float32
    )
    return running + jnp.einsum(
        "krc,xk->rxc", segment[:, :, channels:], sin_table, preferred_element_type=jnp.float32
    )


def split_gradients(dblock, channels):
    grad_real = dblock[:, :channels, :channels] + dblock[:, channels:, channels:]
    grad_imag = dblock[:, :channels, channels:] - dblock[:, channels:, :channels]
    return jnp.stack([grad_real, grad_imag])


def sum_gradients(local_grads):
    flat = local_grads.reshape(-1, 1024)
    return butterfly_sum(butterfly_sum(flat, "gy"), "gz").reshape(local_grads.shape)


def per_device(
    features, depth_weight, expand_weight, project_weight, spec_real, spec_imag, cotangent
):
    planes, y_cells, merged = features.shape
    channels = depth_weight.shape[1]
    x_cells = merged // channels
    row_count = planes * y_cells
    mode_count = spec_real.shape[0]
    group_size = lax.axis_size("gx")
    x_length = x_cells * group_size
    x_start = lax.axis_index("gx") * x_cells
    share_size = mode_count // group_size
    cos_part, sin_part = dft_tables(
        x_start, x_cells, x_length, jnp.arange(mode_count, dtype=jnp.int32)
    )
    order = gathered_order("gx", share_size)
    cos_order, sin_order = dft_tables(x_start, x_cells, x_length, order)
    cos_scaled = scaled_table(cos_order, order, x_length)
    sin_scaled = scaled_table(sin_order, order, x_length)
    cos_fwd_scaled = scaled_table(cos_part, jnp.arange(mode_count, dtype=jnp.int32), x_length)
    sin_fwd_scaled = scaled_table(sin_part, jnp.arange(mode_count, dtype=jnp.int32), x_length)
    blocks = block_weights(spec_real, spec_imag)
    padded = spatial_rims(features, channels)
    activation = depthwise(padded, depth_weight, False, x_cells, channels, jnp.bfloat16)
    field3 = features.reshape(row_count, x_cells, channels)
    owned_blocks = lax.dynamic_slice_in_dim(
        blocks, lax.axis_index("gx") * share_size, share_size, 0
    )
    coeffs = share_terms(field3, cos_part, sin_part).astype(jnp.bfloat16)
    mixed_modes = jnp.einsum(
        "krc,kco->kro", coeffs, owned_blocks, preferred_element_type=jnp.float32
    ).astype(jnp.bfloat16)
    mixed_modes, activation = lax.optimization_barrier((mixed_modes, activation))
    activation = activation.reshape(row_count * x_cells, channels)
    hidden_pre = jnp.dot(activation, expand_weight, preferred_element_type=jnp.float32)
    hidden, hidden_slope = gelu_parts(hidden_pre)
    local_branch = jnp.dot(
        hidden.astype(jnp.bfloat16), project_weight, preferred_element_type=jnp.float32
    )
    local_branch = local_branch.reshape(row_count, x_cells, channels)
    spectral = share_inverse(mixed_modes, cos_scaled, sin_scaled, channels)
    result, slopes = gelu_parts(local_branch + spectral)
    output = result.astype(jnp.bfloat16).reshape(planes, y_cells, merged)
    grad_pre = (
        cotangent.reshape(row_count, x_cells, channels).astype(jnp.float32) * slopes
    ).astype(jnp.bfloat16)
    hidden_grad = jnp.dot(
        grad_pre.reshape(row_count * x_cells, channels),
        project_weight.T,
        preferred_element_type=jnp.float32,
    )
    grad_hidden = (hidden_grad * hidden_slope).astype(jnp.bfloat16)
    grad_act = jnp.dot(grad_hidden, expand_weight.T, preferred_element_type=jnp.float32).astype(
        jnp.bfloat16
    )
    grad_act = grad_act.reshape(planes, y_cells, merged)
    dcoef = share_terms(grad_pre, cos_fwd_scaled, sin_fwd_scaled).astype(jnp.bfloat16)
    dmode = jnp.einsum(
        "kro,kco->krc", dcoef, owned_blocks, preferred_element_type=jnp.float32
    ).astype(jnp.bfloat16)
    dblock = jnp.einsum("krc,kro->kco", coeffs, dcoef, preferred_element_type=jnp.float32)
    local_grads = split_gradients(dblock, channels)
    dmode, local_grads, grad_act = lax.optimization_barrier((dmode, local_grads, grad_act))
    spectral_grad = share_inverse(dmode, cos_order, sin_order, channels)
    grad_spec = sum_gradients(local_grads)
    padded_grad = spatial_rims(grad_act, channels)
    grad_local = depthwise(padded_grad, depth_weight, True, x_cells, channels)
    grad_features = (grad_local + spectral_grad.reshape(planes, y_cells, merged)).astype(
        jnp.bfloat16
    )
    return (output, grad_features, grad_spec)


def solution(mesh):
    placed = (P("gz", "gy", "gx"), P(), P(), P(), P(), P(), P("gz", "gy", "gx"))
    return jax.shard_map(
        per_device,
        mesh=mesh,
        in_specs=placed,
        out_specs=(P("gz", "gy", "gx"), P("gz", "gy", "gx"), P(None, "gx", None, None)),
        check_vma=False,
    )
```

```python
import functools
import math

import jax
import jax.numpy as jnp
from jax import lax
from jax.experimental import pallas as pl
from jax.experimental.pallas import tpu as pltpu
from jax.sharding import PartitionSpec as P


def padded_2(value, sides, width, wrap):
    for axis, dim in sides:
        size, length = (lax.axis_size(axis), value.shape[dim])
        last = lax.slice_in_dim(value, length - width, length, axis=dim)
        leading = lax.slice_in_dim(value, 0, width, axis=dim)
        if size == 2 and not wrap:
            first = lax.axis_index(axis) == 0
            swapped = lax.ppermute(jnp.where(first, last, leading), axis, [(0, 1), (1, 0)])
            zeros = jnp.zeros_like(swapped)
            before = jnp.where(first, zeros, swapped)
            after = jnp.where(first, swapped, zeros)
        else:
            up = [(i, (i + 1) % size) for i in range(size if wrap else size - 1)]
            down = [(j, i) for i, j in up]
            before = lax.ppermute(last, axis, up)
            after = lax.ppermute(leading, axis, down)
        value = jnp.concatenate([before, value, after], axis=dim)
    return value


def gelu_parts(values):
    normal_cdf = 0.5 * (1.0 + jax.scipy.special.erf(values * (1.0 / math.sqrt(2.0))))
    density = jnp.exp(-0.5 * values * values) * (1.0 / math.sqrt(2.0 * math.pi))
    return (values * normal_cdf, normal_cdf + values * density)


def dft_tables(offset, cells, x_length, frequency):
    position = offset + jnp.arange(cells, dtype=jnp.int32)
    phase_int = position[:, None] * frequency[None, :] % x_length
    angles = phase_int.astype(jnp.float32) * (2.0 * math.pi / x_length)
    return (jnp.cos(angles).astype(jnp.bfloat16), (-jnp.sin(angles)).astype(jnp.bfloat16))


def scaled_table(table, frequency, x_length):
    mode_scale = jnp.where(frequency == 0, 1.0, 2.0).astype(jnp.float32) / x_length
    return (table.astype(jnp.float32) * mode_scale[None, :]).astype(jnp.bfloat16)


def gathered_order(axis, share_size):
    size = lax.axis_size(axis)
    shifts = jnp.arange(size, dtype=jnp.int32)
    sources = (lax.axis_index(axis) - shifts) % size
    local = jnp.arange(share_size, dtype=jnp.int32)
    return (sources[:, None] * share_size + local[None, :]).reshape(-1)


def ring_gather(block, axis):
    size = lax.axis_size(axis)
    pieces = [block]
    for shift in range(1, size):
        pieces.append(lax.ppermute(block, axis, [(i, (i + shift) % size) for i in range(size)]))
    return jnp.concatenate(pieces, axis=0)


def ring_reduce_scatter(value, axis):
    size = lax.axis_size(axis)
    share = value.shape[0] // size
    me = lax.axis_index(axis)
    total = lax.dynamic_slice_in_dim(value, me * share, share, 0)
    for shift in range(1, size):
        piece = lax.dynamic_slice_in_dim(value, ((me + shift) % size) * share, share, 0)
        total = total + lax.ppermute(piece, axis, [(i, (i + shift) % size) for i in range(size)])
    return total


def butterfly_sum(value, axis):
    size = lax.axis_size(axis)
    if size & (size - 1):
        return lax.psum(value, axis)
    step = 1
    while step < size:
        value = value.astype(jnp.bfloat16)
        value = value.astype(jnp.float32) + lax.ppermute(
            value, axis, [(i, i ^ step) for i in range(size)]
        ).astype(jnp.float32)
        step *= 2
    return value


def block_weights(spec_real, spec_imag):
    upper_row = jnp.concatenate([spec_real, spec_imag], axis=2)
    lower_row = jnp.concatenate([-spec_imag, spec_real], axis=2)
    return jnp.concatenate([upper_row, lower_row], axis=1)


def spatial_rims(field_block, channels):
    x_wide = padded_2(field_block, (("gx", 2),), 2 * channels, True)
    inner = padded_2(x_wide, (("gy", 1),), 1, False)
    size = lax.axis_size("gz")
    up = [(i, i + 1) for i in range(size - 1)]
    down = [(j, i) for i, j in up]
    below = lax.ppermute(inner[-1:], "gz", up)
    above = lax.ppermute(inner[:1], "gz", down)
    return (inner, below, above)


def stencil_kernel(chunk, x_pad, y_cells, rows, plan, sources, has_acc, *refs):
    src_refs = refs[:sources]
    acc_ref = refs[sources] if has_acc else None
    w_ref, o_ref = refs[sources + has_acc :]
    width = chunk + 2 * x_pad
    count = o_ref.shape[2] // chunk
    shift = chunk + x_pad - x_pad // 2
    side = (chunk + x_pad) // 128

    def body(index, carry):
        base = pl.multiple_of(index * chunk, chunk)
        for plane, terms in enumerate(plan):
            for row in range(0, y_cells, rows):
                left = jnp.zeros((rows, chunk + x_pad), jnp.float32)
                centre = jnp.zeros((rows, chunk), jnp.float32)
                right = jnp.zeros((rows, chunk + x_pad), jnp.float32)
                for source, source_plane, step_z in terms:
                    for step_y in range(3):
                        window = src_refs[source][
                            source_plane, pl.ds(row + step_y, rows), pl.ds(base, width)
                        ].astype(jnp.float32)
                        tap = 9 * step_z + 3 * step_y
                        gain_l = jnp.concatenate([w_ref[tap]] * side, axis=1)
                        gain_c = jnp.concatenate([w_ref[tap + 1]] * (side - 1), axis=1)
                        gain_r = jnp.concatenate([w_ref[tap + 2]] * side, axis=1)
                        left = left + window[:, : chunk + x_pad] * gain_l
                        centre = centre + window[:, x_pad : x_pad + chunk] * gain_c
                        right = right + window[:, x_pad:] * gain_r
                total = (
                    centre
                    + pltpu.roll(left, shift, 1)[:, :chunk]
                    + pltpu.roll(right, shift, 1)[:, :chunk]
                )
                if has_acc:
                    total = total + acc_ref[plane, pl.ds(row, rows), pl.ds(base, chunk)]
                o_ref[plane, pl.ds(row, rows), pl.ds(base, chunk)] = total.astype(o_ref.dtype)
        return carry

    lax.fori_loop(0, count, body, 0)


def stencil_call(plan, inputs, acc, gains, y_cells, lanes, channels, out_dtype):
    chunk = min(1024, lanes)
    rows = 8 if y_cells % 8 == 0 else y_cells
    kernel = functools.partial(
        stencil_kernel, chunk, 2 * channels, y_cells, rows, plan, len(inputs), acc is not None
    )
    operands = list(inputs) + ([acc] if acc is not None else []) + [gains]
    return pl.pallas_call(
        kernel,
        out_shape=jax.ShapeDtypeStruct((len(plan), y_cells, lanes), out_dtype),
    )(*operands)


def depthwise(rims, taps, flipped, x_cells, channels, out_dtype=jnp.float32):
    inner, below, above = rims
    planes = inner.shape[0]
    y_cells = inner.shape[1] - 2
    lanes = x_cells * channels
    rows = 8 if y_cells % 8 == 0 else y_cells
    if flipped:
        taps = taps[::-1]
    gains = jnp.tile(taps.astype(jnp.float32), (1, 128 // channels))
    gains = jnp.broadcast_to(gains[:, None, :], (gains.shape[0], rows, 128))
    local_plan = tuple(
        tuple((0, plane + step_z - 1, step_z) for step_z in range(3) if 0 <= plane + step_z - 1 < planes)
        for plane in range(planes)
    )
    local = stencil_call(local_plan, (inner,), None, gains, y_cells, lanes, channels, jnp.float32)
    rim_plan = tuple(
        ((((0, 0, 0),) if plane == 0 else ()) + (((1, 0, 2),) if plane == planes - 1 else ()))
        for plane in range(planes)
    )
    return stencil_call(rim_plan, (below, above), local, gains, y_cells, lanes, channels, out_dtype)


def share_terms(field3, cos_table, sin_table):
    real_part = jnp.einsum("rxc,xk->krc", field3, cos_table, preferred_element_type=jnp.float32)
    imag_part = jnp.einsum("rxc,xk->krc", field3, sin_table, preferred_element_type=jnp.float32)
    return ring_reduce_scatter(jnp.concatenate([real_part, imag_part], axis=2), "gx")


def share_inverse(modes_share, cos_table, sin_table, channels):
    segment = ring_gather(modes_share, "gx")
    running = jnp.einsum(
        "krc,xk->rxc", segment[:, :, :channels], cos_table, preferred_element_type=jnp.float32
    )
    return running + jnp.einsum(
        "krc,xk->rxc", segment[:, :, channels:], sin_table, preferred_element_type=jnp.float32
    )


def split_gradients(dblock, channels):
    grad_real = dblock[:, :channels, :channels] + dblock[:, channels:, channels:]
    grad_imag = dblock[:, :channels, channels:] - dblock[:, channels:, :channels]
    return jnp.stack([grad_real, grad_imag])


def sum_gradients(local_grads):
    flat = local_grads.reshape(-1, 1024)
    return butterfly_sum(butterfly_sum(flat, "gy"), "gz").reshape(local_grads.shape)


def per_device(
    features, depth_weight, expand_weight, project_weight, spec_real, spec_imag, cotangent
):
    planes, y_cells, merged = features.shape
    channels = depth_weight.shape[1]
    x_cells = merged // channels
    row_count = planes * y_cells
    mode_count = spec_real.shape[0]
    group_size = lax.axis_size("gx")
    x_length = x_cells * group_size
    x_start = lax.axis_index("gx") * x_cells
    share_size = mode_count // group_size
    cos_part, sin_part = dft_tables(
        x_start, x_cells, x_length, jnp.arange(mode_count, dtype=jnp.int32)
    )
    order = gathered_order("gx", share_size)
    cos_order, sin_order = dft_tables(x_start, x_cells, x_length, order)
    cos_scaled = scaled_table(cos_order, order, x_length)
    sin_scaled = scaled_table(sin_order, order, x_length)
    cos_fwd_scaled = scaled_table(cos_part, jnp.arange(mode_count, dtype=jnp.int32), x_length)
    sin_fwd_scaled = scaled_table(sin_part, jnp.arange(mode_count, dtype=jnp.int32), x_length)
    blocks = block_weights(spec_real, spec_imag)
    padded = spatial_rims(features, channels)
    activation = depthwise(padded, depth_weight, False, x_cells, channels, jnp.bfloat16)
    field3 = features.reshape(row_count, x_cells, channels)
    owned_blocks = lax.dynamic_slice_in_dim(
        blocks, lax.axis_index("gx") * share_size, share_size, 0
    )
    coeffs = share_terms(field3, cos_part, sin_part).astype(jnp.bfloat16)
    mixed_modes = jnp.einsum(
        "krc,kco->kro", coeffs, owned_blocks, preferred_element_type=jnp.float32
    ).astype(jnp.bfloat16)
    mixed_modes, activation = lax.optimization_barrier((mixed_modes, activation))
    activation = activation.reshape(row_count * x_cells, channels)
    hidden_pre = jnp.dot(activation, expand_weight, preferred_element_type=jnp.float32)
    hidden, hidden_slope = gelu_parts(hidden_pre)
    local_branch = jnp.dot(
        hidden.astype(jnp.bfloat16), project_weight, preferred_element_type=jnp.float32
    )
    local_branch = local_branch.reshape(row_count, x_cells, channels)
    spectral = share_inverse(mixed_modes, cos_scaled, sin_scaled, channels)
    result, slopes = gelu_parts(local_branch + spectral)
    output = result.astype(jnp.bfloat16).reshape(planes, y_cells, merged)
    grad_pre = (
        cotangent.reshape(row_count, x_cells, channels).astype(jnp.float32) * slopes
    ).astype(jnp.bfloat16)
    hidden_grad = jnp.dot(
        grad_pre.reshape(row_count * x_cells, channels),
        project_weight.T,
        preferred_element_type=jnp.float32,
    )
    grad_hidden = (hidden_grad * hidden_slope).astype(jnp.bfloat16)
    grad_act = jnp.dot(grad_hidden, expand_weight.T, preferred_element_type=jnp.float32).astype(
        jnp.bfloat16
    )
    grad_act = grad_act.reshape(planes, y_cells, merged)
    dcoef = share_terms(grad_pre, cos_fwd_scaled, sin_fwd_scaled).astype(jnp.bfloat16)
    dmode = jnp.einsum(
        "kro,kco->krc", dcoef, owned_blocks, preferred_element_type=jnp.float32
    ).astype(jnp.bfloat16)
    dblock = jnp.einsum("krc,kro->kco", coeffs, dcoef, preferred_element_type=jnp.float32)
    local_grads = split_gradients(dblock, channels)
    dmode, local_grads, grad_act = lax.optimization_barrier((dmode, local_grads, grad_act))
    spectral_grad = share_inverse(dmode, cos_order, sin_order, channels)
    grad_spec = sum_gradients(local_grads)
    padded_grad = spatial_rims(grad_act, channels)
    grad_local = depthwise(padded_grad, depth_weight, True, x_cells, channels)
    grad_features = (grad_local + spectral_grad.reshape(planes, y_cells, merged)).astype(
        jnp.bfloat16
    )
    return (output, grad_features, grad_spec)


def solution(mesh):
    placed = (P("gz", "gy", "gx"), P(), P(), P(), P(), P(), P("gz", "gy", "gx"))
    return jax.shard_map(
        per_device,
        mesh=mesh,
        in_specs=placed,
        out_specs=(P("gz", "gy", "gx"), P("gz", "gy", "gx"), P(None, "gx", None, None)),
        check_vma=False,
    )
```

```python
import functools
import math

import jax
import jax.numpy as jnp
from jax import lax
from jax.experimental import pallas as pl
from jax.experimental.pallas import tpu as pltpu
from jax.sharding import PartitionSpec as P


def padded_2(value, sides, width, wrap):
    for axis, dim in sides:
        size, length = (lax.axis_size(axis), value.shape[dim])
        last = lax.slice_in_dim(value, length - width, length, axis=dim)
        leading = lax.slice_in_dim(value, 0, width, axis=dim)
        if size == 2 and not wrap:
            first = lax.axis_index(axis) == 0
            swapped = lax.ppermute(jnp.where(first, last, leading), axis, [(0, 1), (1, 0)])
            zeros = jnp.zeros_like(swapped)
            before = jnp.where(first, zeros, swapped)
            after = jnp.where(first, swapped, zeros)
        else:
            up = [(i, (i + 1) % size) for i in range(size if wrap else size - 1)]
            down = [(j, i) for i, j in up]
            before = lax.ppermute(last, axis, up)
            after = lax.ppermute(leading, axis, down)
        value = jnp.concatenate([before, value, after], axis=dim)
    return value


def gelu_parts(values):
    normal_cdf = 0.5 * (1.0 + jax.scipy.special.erf(values * (1.0 / math.sqrt(2.0))))
    density = jnp.exp(-0.5 * values * values) * (1.0 / math.sqrt(2.0 * math.pi))
    return (values * normal_cdf, normal_cdf + values * density)


def dft_tables(offset, cells, x_length, frequency):
    position = offset + jnp.arange(cells, dtype=jnp.int32)
    phase_int = position[:, None] * frequency[None, :] % x_length
    angles = phase_int.astype(jnp.float32) * (2.0 * math.pi / x_length)
    return (jnp.cos(angles).astype(jnp.bfloat16), (-jnp.sin(angles)).astype(jnp.bfloat16))


def scaled_table(table, frequency, x_length):
    mode_scale = jnp.where(frequency == 0, 1.0, 2.0).astype(jnp.float32) / x_length
    return (table.astype(jnp.float32) * mode_scale[None, :]).astype(jnp.bfloat16)


def gathered_order(axis, share_size):
    size = lax.axis_size(axis)
    shifts = jnp.arange(size, dtype=jnp.int32)
    sources = (lax.axis_index(axis) - shifts) % size
    local = jnp.arange(share_size, dtype=jnp.int32)
    return (sources[:, None] * share_size + local[None, :]).reshape(-1)


def ring_gather(block, axis):
    size = lax.axis_size(axis)
    pieces = [block]
    for shift in range(1, size):
        pieces.append(lax.ppermute(block, axis, [(i, (i + shift) % size) for i in range(size)]))
    return jnp.concatenate(pieces, axis=0)


def ring_reduce_scatter(value, axis):
    size = lax.axis_size(axis)
    share = value.shape[0] // size
    me = lax.axis_index(axis)
    total = lax.dynamic_slice_in_dim(value, me * share, share, 0)
    for shift in range(1, size):
        piece = lax.dynamic_slice_in_dim(value, ((me + shift) % size) * share, share, 0)
        total = total + lax.ppermute(piece, axis, [(i, (i + shift) % size) for i in range(size)])
    return total


def butterfly_sum(value, axis):
    size = lax.axis_size(axis)
    if size & (size - 1):
        return lax.psum(value, axis)
    step = 1
    while step < size:
        value = value.astype(jnp.bfloat16)
        value = value.astype(jnp.float32) + lax.ppermute(
            value, axis, [(i, i ^ step) for i in range(size)]
        ).astype(jnp.float32)
        step *= 2
    return value


def block_weights(spec_real, spec_imag):
    upper_row = jnp.concatenate([spec_real, spec_imag], axis=2)
    lower_row = jnp.concatenate([-spec_imag, spec_real], axis=2)
    return jnp.concatenate([upper_row, lower_row], axis=1)


def spatial_rims(field_block, channels):
    x_wide = padded_2(field_block, (("gx", 2),), 2 * channels, True)
    inner = padded_2(x_wide, (("gy", 1),), 1, False)
    size = lax.axis_size("gz")
    up = [(i, i + 1) for i in range(size - 1)]
    down = [(j, i) for i, j in up]
    below = lax.ppermute(inner[-1:], "gz", up)
    above = lax.ppermute(inner[:1], "gz", down)
    return (inner, below, above)


def stencil_kernel(chunk, x_pad, y_cells, rows, plan, sources, has_acc, *refs):
    src_refs = refs[:sources]
    acc_ref = refs[sources] if has_acc else None
    w_ref, o_ref = refs[sources + has_acc :]
    width = chunk + 2 * x_pad
    count = o_ref.shape[2] // chunk
    shift = chunk + x_pad - x_pad // 2
    side = (chunk + x_pad) // 128

    def body(index, carry):
        base = pl.multiple_of(index * chunk, chunk)
        for plane, terms in enumerate(plan):
            for row in range(0, y_cells, rows):
                left = jnp.zeros((rows, chunk + x_pad), jnp.float32)
                centre = jnp.zeros((rows, chunk), jnp.float32)
                right = jnp.zeros((rows, chunk + x_pad), jnp.float32)
                for source, source_plane, step_z in terms:
                    for step_y in range(3):
                        window = src_refs[source][
                            source_plane, pl.ds(row + step_y, rows), pl.ds(base, width)
                        ].astype(jnp.float32)
                        tap = 9 * step_z + 3 * step_y
                        gain_l = jnp.concatenate([w_ref[tap]] * side, axis=1)
                        gain_c = jnp.concatenate([w_ref[tap + 1]] * (side - 1), axis=1)
                        gain_r = jnp.concatenate([w_ref[tap + 2]] * side, axis=1)
                        left = left + window[:, : chunk + x_pad] * gain_l
                        centre = centre + window[:, x_pad : x_pad + chunk] * gain_c
                        right = right + window[:, x_pad:] * gain_r
                total = (
                    centre
                    + pltpu.roll(left, shift, 1)[:, :chunk]
                    + pltpu.roll(right, shift, 1)[:, :chunk]
                )
                if has_acc:
                    total = total + acc_ref[plane, pl.ds(row, rows), pl.ds(base, chunk)]
                o_ref[plane, pl.ds(row, rows), pl.ds(base, chunk)] = total.astype(o_ref.dtype)
        return carry

    lax.fori_loop(0, count, body, 0)


def stencil_call(plan, inputs, acc, gains, y_cells, lanes, channels, out_dtype):
    chunk = min(1024, lanes)
    rows = 8 if y_cells % 8 == 0 else y_cells
    kernel = functools.partial(
        stencil_kernel, chunk, 2 * channels, y_cells, rows, plan, len(inputs), acc is not None
    )
    operands = list(inputs) + ([acc] if acc is not None else []) + [gains]
    return pl.pallas_call(
        kernel,
        out_shape=jax.ShapeDtypeStruct((len(plan), y_cells, lanes), out_dtype),
    )(*operands)


def depthwise(rims, taps, flipped, x_cells, channels, out_dtype=jnp.float32):
    inner, below, above = rims
    planes = inner.shape[0]
    y_cells = inner.shape[1] - 2
    lanes = x_cells * channels
    rows = 8 if y_cells % 8 == 0 else y_cells
    if flipped:
        taps = taps[::-1]
    gains = jnp.tile(taps.astype(jnp.float32), (1, 128 // channels))
    gains = jnp.broadcast_to(gains[:, None, :], (gains.shape[0], rows, 128))
    local_plan = tuple(
        tuple((0, plane + step_z - 1, step_z) for step_z in range(3) if 0 <= plane + step_z - 1 < planes)
        for plane in range(planes)
    )
    local = stencil_call(local_plan, (inner,), None, gains, y_cells, lanes, channels, jnp.float32)
    rim_plan = tuple(
        ((((0, 0, 0),) if plane == 0 else ()) + (((1, 0, 2),) if plane == planes - 1 else ()))
        for plane in range(planes)
    )
    return stencil_call(rim_plan, (below, above), local, gains, y_cells, lanes, channels, out_dtype)


def share_terms(field3, cos_table, sin_table):
    real_part = jnp.einsum("rxc,xk->krc", field3, cos_table, preferred_element_type=jnp.float32)
    imag_part = jnp.einsum("rxc,xk->krc", field3, sin_table, preferred_element_type=jnp.float32)
    return ring_reduce_scatter(jnp.concatenate([real_part, imag_part], axis=2), "gx")


def share_inverse(modes_share, cos_table, sin_table, channels):
    segment = ring_gather(modes_share, "gx")
    running = jnp.einsum(
        "krc,xk->rxc", segment[:, :, :channels], cos_table, preferred_element_type=jnp.float32
    )
    return running + jnp.einsum(
        "krc,xk->rxc", segment[:, :, channels:], sin_table, preferred_element_type=jnp.float32
    )


def split_gradients(dblock, channels):
    grad_real = dblock[:, :channels, :channels] + dblock[:, channels:, channels:]
    grad_imag = dblock[:, :channels, channels:] - dblock[:, channels:, :channels]
    return jnp.stack([grad_real, grad_imag])


def sum_gradients(local_grads):
    flat = local_grads.reshape(-1, 1024)
    return butterfly_sum(butterfly_sum(flat, "gy"), "gz").reshape(local_grads.shape)


def per_device(
    features, depth_weight, expand_weight, project_weight, spec_real, spec_imag, cotangent
):
    planes, y_cells, merged = features.shape
    channels = depth_weight.shape[1]
    x_cells = merged // channels
    row_count = planes * y_cells
    mode_count = spec_real.shape[0]
    group_size = lax.axis_size("gx")
    x_length = x_cells * group_size
    x_start = lax.axis_index("gx") * x_cells
    share_size = mode_count // group_size
    cos_part, sin_part = dft_tables(
        x_start, x_cells, x_length, jnp.arange(mode_count, dtype=jnp.int32)
    )
    order = gathered_order("gx", share_size)
    cos_order, sin_order = dft_tables(x_start, x_cells, x_length, order)
    cos_scaled = scaled_table(cos_order, order, x_length)
    sin_scaled = scaled_table(sin_order, order, x_length)
    cos_fwd_scaled = scaled_table(cos_part, jnp.arange(mode_count, dtype=jnp.int32), x_length)
    sin_fwd_scaled = scaled_table(sin_part, jnp.arange(mode_count, dtype=jnp.int32), x_length)
    blocks = block_weights(spec_real, spec_imag)
    padded = spatial_rims(features, channels)
    activation = depthwise(padded, depth_weight, False, x_cells, channels, jnp.bfloat16)
    field3 = features.reshape(row_count, x_cells, channels)
    owned_blocks = lax.dynamic_slice_in_dim(
        blocks, lax.axis_index("gx") * share_size, share_size, 0
    )
    coeffs = share_terms(field3, cos_part, sin_part).astype(jnp.bfloat16)
    mixed_modes = jnp.einsum(
        "krc,kco->kro", coeffs, owned_blocks, preferred_element_type=jnp.float32
    ).astype(jnp.bfloat16)
    mixed_modes, activation = lax.optimization_barrier((mixed_modes, activation))
    activation = activation.reshape(row_count * x_cells, channels)
    hidden_pre = jnp.dot(activation, expand_weight, preferred_element_type=jnp.float32)
    hidden, hidden_slope = gelu_parts(hidden_pre)
    local_branch = jnp.dot(
        hidden.astype(jnp.bfloat16), project_weight, preferred_element_type=jnp.float32
    )
    local_branch = local_branch.reshape(row_count, x_cells, channels)
    spectral = share_inverse(mixed_modes, cos_scaled, sin_scaled, channels)
    result, slopes = gelu_parts(local_branch + spectral)
    output = result.astype(jnp.bfloat16).reshape(planes, y_cells, merged)
    grad_pre = (
        lax.optimization_barrier(cotangent.reshape(row_count, x_cells, channels)).astype(jnp.float32)
        * slopes
    ).astype(jnp.bfloat16)
    hidden_grad = jnp.dot(
        grad_pre.reshape(row_count * x_cells, channels),
        project_weight.T,
        preferred_element_type=jnp.float32,
    )
    grad_hidden = (hidden_grad * hidden_slope).astype(jnp.bfloat16)
    grad_act = jnp.dot(grad_hidden, expand_weight.T, preferred_element_type=jnp.float32).astype(
        jnp.bfloat16
    )
    grad_act = grad_act.reshape(planes, y_cells, merged)
    dcoef = share_terms(grad_pre, cos_fwd_scaled, sin_fwd_scaled).astype(jnp.bfloat16)
    dmode = jnp.einsum(
        "kro,kco->krc", dcoef, owned_blocks, preferred_element_type=jnp.float32
    ).astype(jnp.bfloat16)
    dblock = jnp.einsum("krc,kro->kco", coeffs, dcoef, preferred_element_type=jnp.float32)
    local_grads = split_gradients(dblock, channels)
    dmode, local_grads, grad_act = lax.optimization_barrier((dmode, local_grads, grad_act))
    spectral_grad = share_inverse(dmode, cos_order, sin_order, channels)
    grad_spec = sum_gradients(local_grads)
    padded_grad = spatial_rims(grad_act, channels)
    grad_local = depthwise(padded_grad, depth_weight, True, x_cells, channels)
    grad_features = (grad_local + spectral_grad.reshape(planes, y_cells, merged)).astype(
        jnp.bfloat16
    )
    return (output, grad_features, grad_spec)


def solution(mesh):
    placed = (P("gz", "gy", "gx"), P(), P(), P(), P(), P(), P("gz", "gy", "gx"))
    return jax.shard_map(
        per_device,
        mesh=mesh,
        in_specs=placed,
        out_specs=(P("gz", "gy", "gx"), P("gz", "gy", "gx"), P(None, "gx", None, None)),
        check_vma=False,
    )
```

```python
import functools
import math

import jax
import jax.numpy as jnp
from jax import lax
from jax.experimental import pallas as pl
from jax.experimental.pallas import tpu as pltpu
from jax.sharding import PartitionSpec as P


def padded_2(value, sides, width, wrap):
    for axis, dim in sides:
        size, length = (lax.axis_size(axis), value.shape[dim])
        last = lax.slice_in_dim(value, length - width, length, axis=dim)
        leading = lax.slice_in_dim(value, 0, width, axis=dim)
        if size == 2 and not wrap:
            first = lax.axis_index(axis) == 0
            swapped = lax.ppermute(jnp.where(first, last, leading), axis, [(0, 1), (1, 0)])
            zeros = jnp.zeros_like(swapped)
            before = jnp.where(first, zeros, swapped)
            after = jnp.where(first, swapped, zeros)
        else:
            up = [(i, (i + 1) % size) for i in range(size if wrap else size - 1)]
            down = [(j, i) for i, j in up]
            before = lax.ppermute(last, axis, up)
            after = lax.ppermute(leading, axis, down)
        value = jnp.concatenate([before, value, after], axis=dim)
    return value


def gelu_parts(values):
    normal_cdf = 0.5 * (1.0 + jax.scipy.special.erf(values * (1.0 / math.sqrt(2.0))))
    density = jnp.exp(-0.5 * values * values) * (1.0 / math.sqrt(2.0 * math.pi))
    return (values * normal_cdf, normal_cdf + values * density)


def dft_tables(offset, cells, x_length, frequency):
    position = offset + jnp.arange(cells, dtype=jnp.int32)
    phase_int = position[:, None] * frequency[None, :] % x_length
    angles = phase_int.astype(jnp.float32) * (2.0 * math.pi / x_length)
    return (jnp.cos(angles).astype(jnp.bfloat16), (-jnp.sin(angles)).astype(jnp.bfloat16))


def scaled_table(table, frequency, x_length):
    mode_scale = jnp.where(frequency == 0, 1.0, 2.0).astype(jnp.float32) / x_length
    return (table.astype(jnp.float32) * mode_scale[None, :]).astype(jnp.bfloat16)


def gathered_order(axis, share_size):
    size = lax.axis_size(axis)
    shifts = jnp.arange(size, dtype=jnp.int32)
    sources = (lax.axis_index(axis) - shifts) % size
    local = jnp.arange(share_size, dtype=jnp.int32)
    return (sources[:, None] * share_size + local[None, :]).reshape(-1)


def ring_gather(block, axis):
    size = lax.axis_size(axis)
    pieces = [block]
    for shift in range(1, size):
        pieces.append(lax.ppermute(block, axis, [(i, (i + shift) % size) for i in range(size)]))
    return jnp.concatenate(pieces, axis=0)


def ring_reduce_scatter(value, axis):
    size = lax.axis_size(axis)
    share = value.shape[0] // size
    me = lax.axis_index(axis)
    total = lax.dynamic_slice_in_dim(value, me * share, share, 0)
    for shift in range(1, size):
        piece = lax.dynamic_slice_in_dim(value, ((me + shift) % size) * share, share, 0)
        total = total + lax.ppermute(piece, axis, [(i, (i + shift) % size) for i in range(size)])
    return total


def butterfly_sum(value, axis):
    size = lax.axis_size(axis)
    if size & (size - 1):
        return lax.psum(value, axis)
    step = 1
    while step < size:
        value = value.astype(jnp.bfloat16)
        value = value.astype(jnp.float32) + lax.ppermute(
            value, axis, [(i, i ^ step) for i in range(size)]
        ).astype(jnp.float32)
        step *= 2
    return value


def block_weights(spec_real, spec_imag):
    upper_row = jnp.concatenate([spec_real, spec_imag], axis=2)
    lower_row = jnp.concatenate([-spec_imag, spec_real], axis=2)
    return jnp.concatenate([upper_row, lower_row], axis=1)


def spatial_rims(field_block, channels):
    x_wide = padded_2(field_block, (("gx", 2),), 2 * channels, True)
    inner = padded_2(x_wide, (("gy", 1),), 1, False)
    size = lax.axis_size("gz")
    up = [(i, i + 1) for i in range(size - 1)]
    down = [(j, i) for i, j in up]
    below = lax.ppermute(inner[-1:], "gz", up)
    above = lax.ppermute(inner[:1], "gz", down)
    return (inner, below, above)


def stencil_kernel(chunk, x_pad, y_cells, rows, plan, sources, has_acc, *refs):
    src_refs = refs[:sources]
    acc_ref = refs[sources] if has_acc else None
    w_ref, o_ref = refs[sources + has_acc :]
    width = chunk + 2 * x_pad
    count = o_ref.shape[1] // chunk
    shift = chunk + x_pad - x_pad // 2
    side = (chunk + x_pad) // 128
    current = pl.program_id(0)

    def run(terms):
        def body(index, carry):
            base = pl.multiple_of(index * chunk, chunk)
            for row in range(0, y_cells, rows):
                left = jnp.zeros((rows, chunk + x_pad), jnp.float32)
                centre = jnp.zeros((rows, chunk), jnp.float32)
                right = jnp.zeros((rows, chunk + x_pad), jnp.float32)
                for source, source_plane, step_z in terms:
                    for step_y in range(3):
                        window = src_refs[source][
                            source_plane, pl.ds(row + step_y, rows), pl.ds(base, width)
                        ].astype(jnp.float32)
                        tap = 9 * step_z + 3 * step_y
                        gain_l = jnp.concatenate([w_ref[tap]] * side, axis=1)
                        gain_c = jnp.concatenate([w_ref[tap + 1]] * (side - 1), axis=1)
                        gain_r = jnp.concatenate([w_ref[tap + 2]] * side, axis=1)
                        left = left + window[:, : chunk + x_pad] * gain_l
                        centre = centre + window[:, x_pad : x_pad + chunk] * gain_c
                        right = right + window[:, x_pad:] * gain_r
                total = (
                    centre
                    + pltpu.roll(left, shift, 1)[:, :chunk]
                    + pltpu.roll(right, shift, 1)[:, :chunk]
                )
                if has_acc:
                    total = total + acc_ref[pl.ds(row, rows), pl.ds(base, chunk)]
                o_ref[pl.ds(row, rows), pl.ds(base, chunk)] = total.astype(o_ref.dtype)
            return carry

        lax.fori_loop(0, count, body, 0)

    for plane, terms in enumerate(plan):
        pl.when(current == plane)(functools.partial(run, terms))


def stencil_call(plan, inputs, acc, gains, y_cells, lanes, channels, out_dtype):
    chunk = min(1024, lanes)
    rows = 8 if y_cells % 8 == 0 else y_cells
    kernel = functools.partial(
        stencil_kernel, chunk, 2 * channels, y_cells, rows, plan, len(inputs), acc is not None
    )
    plane_spec = pl.BlockSpec((None, y_cells, lanes), lambda z: (z, 0, 0))
    in_specs = [pl.BlockSpec(value.shape, lambda z: (0, 0, 0)) for value in inputs]
    operands = list(inputs)
    if acc is not None:
        in_specs.append(plane_spec)
        operands.append(acc)
    in_specs.append(pl.BlockSpec(gains.shape, lambda z: (0, 0, 0)))
    operands.append(gains)
    return pl.pallas_call(
        kernel,
        grid=(len(plan),),
        in_specs=in_specs,
        out_specs=plane_spec,
        out_shape=jax.ShapeDtypeStruct((len(plan), y_cells, lanes), out_dtype),
    )(*operands)


def depthwise(rims, taps, flipped, x_cells, channels, out_dtype=jnp.float32):
    inner, below, above = rims
    planes = inner.shape[0]
    y_cells = inner.shape[1] - 2
    lanes = x_cells * channels
    rows = 8 if y_cells % 8 == 0 else y_cells
    if flipped:
        taps = taps[::-1]
    gains = jnp.tile(taps.astype(jnp.float32), (1, 128 // channels))
    gains = jnp.broadcast_to(gains[:, None, :], (gains.shape[0], rows, 128))
    local_plan = tuple(
        tuple((0, plane + step_z - 1, step_z) for step_z in range(3) if 0 <= plane + step_z - 1 < planes)
        for plane in range(planes)
    )
    local = stencil_call(local_plan, (inner,), None, gains, y_cells, lanes, channels, jnp.float32)
    rim_plan = tuple(
        ((((0, 0, 0),) if plane == 0 else ()) + (((1, 0, 2),) if plane == planes - 1 else ()))
        for plane in range(planes)
    )
    return stencil_call(rim_plan, (below, above), local, gains, y_cells, lanes, channels, out_dtype)


def share_terms(field3, cos_table, sin_table):
    real_part = jnp.einsum("rxc,xk->krc", field3, cos_table, preferred_element_type=jnp.float32)
    imag_part = jnp.einsum("rxc,xk->krc", field3, sin_table, preferred_element_type=jnp.float32)
    return ring_reduce_scatter(jnp.concatenate([real_part, imag_part], axis=2), "gx")


def share_inverse(modes_share, cos_table, sin_table, channels):
    segment = ring_gather(modes_share, "gx")
    running = jnp.einsum(
        "krc,xk->rxc", segment[:, :, :channels], cos_table, preferred_element_type=jnp.float32
    )
    return running + jnp.einsum(
        "krc,xk->rxc", segment[:, :, channels:], sin_table, preferred_element_type=jnp.float32
    )


def split_gradients(dblock, channels):
    grad_real = dblock[:, :channels, :channels] + dblock[:, channels:, channels:]
    grad_imag = dblock[:, :channels, channels:] - dblock[:, channels:, :channels]
    return jnp.stack([grad_real, grad_imag])


def sum_gradients(local_grads):
    flat = local_grads.reshape(-1, 1024)
    return butterfly_sum(butterfly_sum(flat, "gy"), "gz").reshape(local_grads.shape)


def per_device(
    features, depth_weight, expand_weight, project_weight, spec_real, spec_imag, cotangent
):
    planes, y_cells, merged = features.shape
    channels = depth_weight.shape[1]
    x_cells = merged // channels
    row_count = planes * y_cells
    mode_count = spec_real.shape[0]
    group_size = lax.axis_size("gx")
    x_length = x_cells * group_size
    x_start = lax.axis_index("gx") * x_cells
    share_size = mode_count // group_size
    cos_part, sin_part = dft_tables(
        x_start, x_cells, x_length, jnp.arange(mode_count, dtype=jnp.int32)
    )
    order = gathered_order("gx", share_size)
    cos_order, sin_order = dft_tables(x_start, x_cells, x_length, order)
    cos_scaled = scaled_table(cos_order, order, x_length)
    sin_scaled = scaled_table(sin_order, order, x_length)
    cos_fwd_scaled = scaled_table(cos_part, jnp.arange(mode_count, dtype=jnp.int32), x_length)
    sin_fwd_scaled = scaled_table(sin_part, jnp.arange(mode_count, dtype=jnp.int32), x_length)
    blocks = block_weights(spec_real, spec_imag)
    padded = spatial_rims(features, channels)
    activation = depthwise(padded, depth_weight, False, x_cells, channels, jnp.bfloat16)
    field3 = features.reshape(row_count, x_cells, channels)
    owned_blocks = lax.dynamic_slice_in_dim(
        blocks, lax.axis_index("gx") * share_size, share_size, 0
    )
    coeffs = share_terms(field3, cos_part, sin_part).astype(jnp.bfloat16)
    mixed_modes = jnp.einsum(
        "krc,kco->kro", coeffs, owned_blocks, preferred_element_type=jnp.float32
    ).astype(jnp.bfloat16)
    mixed_modes, activation = lax.optimization_barrier((mixed_modes, activation))
    activation = activation.reshape(row_count * x_cells, channels)
    hidden_pre = jnp.dot(activation, expand_weight, preferred_element_type=jnp.float32)
    hidden, hidden_slope = gelu_parts(hidden_pre)
    local_branch = jnp.dot(
        hidden.astype(jnp.bfloat16), project_weight, preferred_element_type=jnp.float32
    )
    local_branch = local_branch.reshape(row_count, x_cells, channels)
    spectral = share_inverse(mixed_modes, cos_scaled, sin_scaled, channels)
    result, slopes = gelu_parts(local_branch + spectral)
    output = result.astype(jnp.bfloat16).reshape(planes, y_cells, merged)
    grad_pre = (
        lax.optimization_barrier(cotangent.reshape(row_count, x_cells, channels)).astype(jnp.float32)
        * slopes
    ).astype(jnp.bfloat16)
    hidden_grad = jnp.dot(
        grad_pre.reshape(row_count * x_cells, channels),
        project_weight.T,
        preferred_element_type=jnp.float32,
    )
    grad_hidden = (hidden_grad * hidden_slope).astype(jnp.bfloat16)
    grad_act = jnp.dot(grad_hidden, expand_weight.T, preferred_element_type=jnp.float32).astype(
        jnp.bfloat16
    )
    grad_act = grad_act.reshape(planes, y_cells, merged)
    dcoef = share_terms(grad_pre, cos_fwd_scaled, sin_fwd_scaled).astype(jnp.bfloat16)
    dmode = jnp.einsum(
        "kro,kco->krc", dcoef, owned_blocks, preferred_element_type=jnp.float32
    ).astype(jnp.bfloat16)
    dblock = jnp.einsum("krc,kro->kco", coeffs, dcoef, preferred_element_type=jnp.float32)
    local_grads = split_gradients(dblock, channels)
    dmode, local_grads, grad_act = lax.optimization_barrier((dmode, local_grads, grad_act))
    spectral_grad = share_inverse(dmode, cos_order, sin_order, channels)
    grad_spec = sum_gradients(local_grads)
    padded_grad = spatial_rims(grad_act, channels)
    grad_local = depthwise(padded_grad, depth_weight, True, x_cells, channels)
    grad_features = (grad_local + spectral_grad.reshape(planes, y_cells, merged)).astype(
        jnp.bfloat16
    )
    return (output, grad_features, grad_spec)


def solution(mesh):
    placed = (P("gz", "gy", "gx"), P(), P(), P(), P(), P(), P("gz", "gy", "gx"))
    return jax.shard_map(
        per_device,
        mesh=mesh,
        in_specs=placed,
        out_specs=(P("gz", "gy", "gx"), P("gz", "gy", "gx"), P(None, "gx", None, None)),
        check_vma=False,
    )
```

```python
import functools
import math

import jax
import jax.numpy as jnp
from jax import lax
from jax.experimental import pallas as pl
from jax.experimental.pallas import tpu as pltpu
from jax.sharding import PartitionSpec as P


def padded_2(value, sides, width, wrap):
    for axis, dim in sides:
        size, length = (lax.axis_size(axis), value.shape[dim])
        last = lax.slice_in_dim(value, length - width, length, axis=dim)
        leading = lax.slice_in_dim(value, 0, width, axis=dim)
        if size == 2 and not wrap:
            first = lax.axis_index(axis) == 0
            swapped = lax.ppermute(jnp.where(first, last, leading), axis, [(0, 1), (1, 0)])
            zeros = jnp.zeros_like(swapped)
            before = jnp.where(first, zeros, swapped)
            after = jnp.where(first, swapped, zeros)
        else:
            up = [(i, (i + 1) % size) for i in range(size if wrap else size - 1)]
            down = [(j, i) for i, j in up]
            before = lax.ppermute(last, axis, up)
            after = lax.ppermute(leading, axis, down)
        value = jnp.concatenate([before, value, after], axis=dim)
    return value


def gelu_parts(values):
    normal_cdf = 0.5 * (1.0 + jax.scipy.special.erf(values * (1.0 / math.sqrt(2.0))))
    density = jnp.exp(-0.5 * values * values) * (1.0 / math.sqrt(2.0 * math.pi))
    return (values * normal_cdf, normal_cdf + values * density)


def dft_tables(offset, cells, x_length, frequency):
    position = offset + jnp.arange(cells, dtype=jnp.int32)
    phase_int = position[:, None] * frequency[None, :] % x_length
    angles = phase_int.astype(jnp.float32) * (2.0 * math.pi / x_length)
    return (jnp.cos(angles).astype(jnp.bfloat16), (-jnp.sin(angles)).astype(jnp.bfloat16))


def scaled_table(table, frequency, x_length):
    mode_scale = jnp.where(frequency == 0, 1.0, 2.0).astype(jnp.float32) / x_length
    return (table.astype(jnp.float32) * mode_scale[None, :]).astype(jnp.bfloat16)


def gathered_order(axis, share_size):
    size = lax.axis_size(axis)
    shifts = jnp.arange(size, dtype=jnp.int32)
    me = lax.axis_index(axis)
    if size & (size - 1):
        sources = (me - shifts) % size
    else:
        sources = jnp.bitwise_xor(me, shifts)
    local = jnp.arange(share_size, dtype=jnp.int32)
    return (sources[:, None] * share_size + local[None, :]).reshape(-1)


def ring_gather(block, axis):
    size = lax.axis_size(axis)
    if size & (size - 1) == 0:
        step = 1
        while step < size:
            block = jnp.concatenate(
                [block, lax.ppermute(block, axis, [(i, i ^ step) for i in range(size)])], axis=0
            )
            step *= 2
        return block
    pieces = [block]
    for shift in range(1, size):
        pieces.append(lax.ppermute(block, axis, [(i, (i + shift) % size) for i in range(size)]))
    return jnp.concatenate(pieces, axis=0)


def ring_reduce_scatter(value, axis):
    size = lax.axis_size(axis)
    share = value.shape[0] // size
    me = lax.axis_index(axis)
    if size & (size - 1) == 0:
        step = size // 2
        count = size
        while step >= 1:
            count //= 2
            upper = jnp.bitwise_and(me, step) != 0
            keep = lax.dynamic_slice_in_dim(value, jnp.where(upper, count, 0) * share, count * share, 0)
            send = lax.dynamic_slice_in_dim(value, jnp.where(upper, 0, count) * share, count * share, 0)
            value = keep + lax.ppermute(send, axis, [(i, i ^ step) for i in range(size)])
            step //= 2
        return value
    total = lax.dynamic_slice_in_dim(value, me * share, share, 0)
    for shift in range(1, size):
        piece = lax.dynamic_slice_in_dim(value, ((me + shift) % size) * share, share, 0)
        total = total + lax.ppermute(piece, axis, [(i, (i + shift) % size) for i in range(size)])
    return total


def butterfly_sum(value, axis):
    size = lax.axis_size(axis)
    if size & (size - 1):
        return lax.psum(value, axis)
    step = 1
    while step < size:
        value = value.astype(jnp.bfloat16)
        value = value.astype(jnp.float32) + lax.ppermute(
            value, axis, [(i, i ^ step) for i in range(size)]
        ).astype(jnp.float32)
        step *= 2
    return value


def block_weights(spec_real, spec_imag):
    upper_row = jnp.concatenate([spec_real, spec_imag], axis=2)
    lower_row = jnp.concatenate([-spec_imag, spec_real], axis=2)
    return jnp.concatenate([upper_row, lower_row], axis=1)


def spatial_rims(field_block, channels):
    x_wide = padded_2(field_block, (("gx", 2),), 2 * channels, True)
    inner = padded_2(x_wide, (("gy", 1),), 1, False)
    size = lax.axis_size("gz")
    up = [(i, i + 1) for i in range(size - 1)]
    down = [(j, i) for i, j in up]
    below = lax.ppermute(inner[-1:], "gz", up)
    above = lax.ppermute(inner[:1], "gz", down)
    return (inner, below, above)


def stencil_kernel(chunk, x_pad, y_cells, rows, plan, sources, has_acc, *refs):
    src_refs = refs[:sources]
    acc_ref = refs[sources] if has_acc else None
    w_ref, o_ref = refs[sources + has_acc :]
    width = chunk + 2 * x_pad
    count = o_ref.shape[2] // chunk
    shift = chunk + x_pad - x_pad // 2
    side = (chunk + x_pad) // 128

    def body(index, carry):
        base = pl.multiple_of(index * chunk, chunk)
        for plane, terms in enumerate(plan):
            for row in range(0, y_cells, rows):
                left = jnp.zeros((rows, chunk + x_pad), jnp.float32)
                centre = jnp.zeros((rows, chunk), jnp.float32)
                right = jnp.zeros((rows, chunk + x_pad), jnp.float32)
                for source, source_plane, step_z in terms:
                    for step_y in range(3):
                        window = src_refs[source][
                            source_plane, pl.ds(row + step_y, rows), pl.ds(base, width)
                        ].astype(jnp.float32)
                        tap = 9 * step_z + 3 * step_y
                        gain_l = jnp.concatenate([w_ref[tap]] * side, axis=1)
                        gain_c = jnp.concatenate([w_ref[tap + 1]] * (side - 1), axis=1)
                        gain_r = jnp.concatenate([w_ref[tap + 2]] * side, axis=1)
                        left = left + window[:, : chunk + x_pad] * gain_l
                        centre = centre + window[:, x_pad : x_pad + chunk] * gain_c
                        right = right + window[:, x_pad:] * gain_r
                total = (
                    centre
                    + pltpu.roll(left, shift, 1)[:, :chunk]
                    + pltpu.roll(right, shift, 1)[:, :chunk]
                )
                if has_acc:
                    total = total + acc_ref[plane, pl.ds(row, rows), pl.ds(base, chunk)]
                o_ref[plane, pl.ds(row, rows), pl.ds(base, chunk)] = total.astype(o_ref.dtype)
        return carry

    lax.fori_loop(0, count, body, 0)


def stencil_call(plan, inputs, acc, gains, y_cells, lanes, channels, out_dtype):
    chunk = min(1024, lanes)
    rows = 8 if y_cells % 8 == 0 else y_cells
    kernel = functools.partial(
        stencil_kernel, chunk, 2 * channels, y_cells, rows, plan, len(inputs), acc is not None
    )
    operands = list(inputs) + ([acc] if acc is not None else []) + [gains]
    return pl.pallas_call(
        kernel,
        out_shape=jax.ShapeDtypeStruct((len(plan), y_cells, lanes), out_dtype),
    )(*operands)


def depthwise(rims, taps, flipped, x_cells, channels, out_dtype=jnp.float32):
    inner, below, above = rims
    planes = inner.shape[0]
    y_cells = inner.shape[1] - 2
    lanes = x_cells * channels
    rows = 8 if y_cells % 8 == 0 else y_cells
    if flipped:
        taps = taps[::-1]
    gains = jnp.tile(taps.astype(jnp.float32), (1, 128 // channels))
    gains = jnp.broadcast_to(gains[:, None, :], (gains.shape[0], rows, 128))
    local_plan = tuple(
        tuple((0, plane + step_z - 1, step_z) for step_z in range(3) if 0 <= plane + step_z - 1 < planes)
        for plane in range(planes)
    )
    local = stencil_call(local_plan, (inner,), None, gains, y_cells, lanes, channels, jnp.float32)
    rim_plan = tuple(
        ((((0, 0, 0),) if plane == 0 else ()) + (((1, 0, 2),) if plane == planes - 1 else ()))
        for plane in range(planes)
    )
    return stencil_call(rim_plan, (below, above), local, gains, y_cells, lanes, channels, out_dtype)


def share_terms(field3, cos_table, sin_table):
    real_part = jnp.einsum("rxc,xk->krc", field3, cos_table, preferred_element_type=jnp.float32)
    imag_part = jnp.einsum("rxc,xk->krc", field3, sin_table, preferred_element_type=jnp.float32)
    return ring_reduce_scatter(jnp.concatenate([real_part, imag_part], axis=2), "gx")


def share_inverse(modes_share, cos_table, sin_table, channels):
    segment = ring_gather(modes_share, "gx")
    running = jnp.einsum(
        "krc,xk->rxc", segment[:, :, :channels], cos_table, preferred_element_type=jnp.float32
    )
    return running + jnp.einsum(
        "krc,xk->rxc", segment[:, :, channels:], sin_table, preferred_element_type=jnp.float32
    )


def split_gradients(dblock, channels):
    grad_real = dblock[:, :channels, :channels] + dblock[:, channels:, channels:]
    grad_imag = dblock[:, :channels, channels:] - dblock[:, channels:, :channels]
    return jnp.stack([grad_real, grad_imag])


def sum_gradients(local_grads):
    flat = local_grads.reshape(-1, 1024)
    return butterfly_sum(butterfly_sum(flat, "gy"), "gz").reshape(local_grads.shape)


def per_device(
    features, depth_weight, expand_weight, project_weight, spec_real, spec_imag, cotangent
):
    planes, y_cells, merged = features.shape
    channels = depth_weight.shape[1]
    x_cells = merged // channels
    row_count = planes * y_cells
    mode_count = spec_real.shape[0]
    group_size = lax.axis_size("gx")
    x_length = x_cells * group_size
    x_start = lax.axis_index("gx") * x_cells
    share_size = mode_count // group_size
    cos_part, sin_part = dft_tables(
        x_start, x_cells, x_length, jnp.arange(mode_count, dtype=jnp.int32)
    )
    order = gathered_order("gx", share_size)
    cos_order, sin_order = dft_tables(x_start, x_cells, x_length, order)
    cos_scaled = scaled_table(cos_order, order, x_length)
    sin_scaled = scaled_table(sin_order, order, x_length)
    cos_fwd_scaled = scaled_table(cos_part, jnp.arange(mode_count, dtype=jnp.int32), x_length)
    sin_fwd_scaled = scaled_table(sin_part, jnp.arange(mode_count, dtype=jnp.int32), x_length)
    blocks = block_weights(spec_real, spec_imag)
    padded = spatial_rims(features, channels)
    activation = depthwise(padded, depth_weight, False, x_cells, channels, jnp.bfloat16)
    field3 = features.reshape(row_count, x_cells, channels)
    owned_blocks = lax.dynamic_slice_in_dim(
        blocks, lax.axis_index("gx") * share_size, share_size, 0
    )
    coeffs = share_terms(field3, cos_part, sin_part).astype(jnp.bfloat16)
    mixed_modes = jnp.einsum(
        "krc,kco->kro", coeffs, owned_blocks, preferred_element_type=jnp.float32
    ).astype(jnp.bfloat16)
    mixed_modes, activation = lax.optimization_barrier((mixed_modes, activation))
    activation = activation.reshape(row_count * x_cells, channels)
    hidden_pre = jnp.dot(activation, expand_weight, preferred_element_type=jnp.float32)
    hidden, hidden_slope = gelu_parts(hidden_pre)
    local_branch = jnp.dot(
        hidden.astype(jnp.bfloat16), project_weight, preferred_element_type=jnp.float32
    )
    local_branch = local_branch.reshape(row_count, x_cells, channels)
    spectral = share_inverse(mixed_modes, cos_scaled, sin_scaled, channels)
    result, slopes = gelu_parts(local_branch + spectral)
    output = result.astype(jnp.bfloat16).reshape(planes, y_cells, merged)
    grad_pre = (
        lax.optimization_barrier(cotangent.reshape(row_count, x_cells, channels)).astype(jnp.float32)
        * slopes
    ).astype(jnp.bfloat16)
    hidden_grad = jnp.dot(
        grad_pre.reshape(row_count * x_cells, channels),
        project_weight.T,
        preferred_element_type=jnp.float32,
    )
    grad_hidden = (hidden_grad * hidden_slope).astype(jnp.bfloat16)
    grad_act = jnp.dot(grad_hidden, expand_weight.T, preferred_element_type=jnp.float32).astype(
        jnp.bfloat16
    )
    grad_act = grad_act.reshape(planes, y_cells, merged)
    dcoef = share_terms(grad_pre, cos_fwd_scaled, sin_fwd_scaled).astype(jnp.bfloat16)
    dmode = jnp.einsum(
        "kro,kco->krc", dcoef, owned_blocks, preferred_element_type=jnp.float32
    ).astype(jnp.bfloat16)
    dblock = jnp.einsum("krc,kro->kco", coeffs, dcoef, preferred_element_type=jnp.float32)
    local_grads = split_gradients(dblock, channels)
    dmode, local_grads, grad_act = lax.optimization_barrier((dmode, local_grads, grad_act))
    spectral_grad = share_inverse(dmode, cos_order, sin_order, channels)
    grad_spec = sum_gradients(local_grads)
    padded_grad = spatial_rims(grad_act, channels)
    grad_local = depthwise(padded_grad, depth_weight, True, x_cells, channels)
    grad_features = (grad_local + spectral_grad.reshape(planes, y_cells, merged)).astype(
        jnp.bfloat16
    )
    return (output, grad_features, grad_spec)


def solution(mesh):
    placed = (P("gz", "gy", "gx"), P(), P(), P(), P(), P(), P("gz", "gy", "gx"))
    return jax.shard_map(
        per_device,
        mesh=mesh,
        in_specs=placed,
        out_specs=(P("gz", "gy", "gx"), P("gz", "gy", "gx"), P(None, "gx", None, None)),
        check_vma=False,
    )
```

```python
import functools
import math

import jax
import jax.numpy as jnp
from jax import lax
from jax.experimental import pallas as pl
from jax.experimental.pallas import tpu as pltpu
from jax.sharding import PartitionSpec as P


def padded_2(value, sides, width, wrap):
    for axis, dim in sides:
        size, length = (lax.axis_size(axis), value.shape[dim])
        last = lax.slice_in_dim(value, length - width, length, axis=dim)
        leading = lax.slice_in_dim(value, 0, width, axis=dim)
        if size == 2 and not wrap:
            first = lax.axis_index(axis) == 0
            swapped = lax.ppermute(jnp.where(first, last, leading), axis, [(0, 1), (1, 0)])
            zeros = jnp.zeros_like(swapped)
            before = jnp.where(first, zeros, swapped)
            after = jnp.where(first, swapped, zeros)
        else:
            up = [(i, (i + 1) % size) for i in range(size if wrap else size - 1)]
            down = [(j, i) for i, j in up]
            before = lax.ppermute(last, axis, up)
            after = lax.ppermute(leading, axis, down)
        value = jnp.concatenate([before, value, after], axis=dim)
    return value


def gelu_parts(values):
    normal_cdf = 0.5 * (1.0 + jax.scipy.special.erf(values * (1.0 / math.sqrt(2.0))))
    density = jnp.exp(-0.5 * values * values) * (1.0 / math.sqrt(2.0 * math.pi))
    return (values * normal_cdf, normal_cdf + values * density)


def dft_tables(offset, cells, x_length, frequency):
    position = offset + jnp.arange(cells, dtype=jnp.int32)
    phase_int = position[:, None] * frequency[None, :] % x_length
    angles = phase_int.astype(jnp.float32) * (2.0 * math.pi / x_length)
    return (jnp.cos(angles).astype(jnp.bfloat16), (-jnp.sin(angles)).astype(jnp.bfloat16))


def scaled_table(table, frequency, x_length):
    mode_scale = jnp.where(frequency == 0, 1.0, 2.0).astype(jnp.float32) / x_length
    return (table.astype(jnp.float32) * mode_scale[None, :]).astype(jnp.bfloat16)


def gathered_order(axis, share_size):
    size = lax.axis_size(axis)
    shifts = jnp.arange(size, dtype=jnp.int32)
    me = lax.axis_index(axis)
    if size & (size - 1):
        sources = (me - shifts) % size
    else:
        sources = jnp.bitwise_xor(me, shifts)
    local = jnp.arange(share_size, dtype=jnp.int32)
    return (sources[:, None] * share_size + local[None, :]).reshape(-1)


def ring_gather(block, axis):
    size = lax.axis_size(axis)
    if size & (size - 1) == 0:
        step = 1
        while step < size:
            block = jnp.concatenate(
                [block, lax.ppermute(block, axis, [(i, i ^ step) for i in range(size)])], axis=0
            )
            step *= 2
        return block
    pieces = [block]
    for shift in range(1, size):
        pieces.append(lax.ppermute(block, axis, [(i, (i + shift) % size) for i in range(size)]))
    return jnp.concatenate(pieces, axis=0)


def ring_reduce_scatter(value, axis):
    size = lax.axis_size(axis)
    share = value.shape[0] // size
    me = lax.axis_index(axis)
    if size & (size - 1) == 0:
        step = size // 2
        count = size
        while step >= 1:
            count //= 2
            upper = jnp.bitwise_and(me, step) != 0
            keep = lax.dynamic_slice_in_dim(value, jnp.where(upper, count, 0) * share, count * share, 0)
            send = lax.dynamic_slice_in_dim(value, jnp.where(upper, 0, count) * share, count * share, 0)
            value = keep + lax.ppermute(send, axis, [(i, i ^ step) for i in range(size)])
            step //= 2
        return value
    total = lax.dynamic_slice_in_dim(value, me * share, share, 0)
    for shift in range(1, size):
        piece = lax.dynamic_slice_in_dim(value, ((me + shift) % size) * share, share, 0)
        total = total + lax.ppermute(piece, axis, [(i, (i + shift) % size) for i in range(size)])
    return total


def butterfly_sum(value, axis):
    size = lax.axis_size(axis)
    if size & (size - 1):
        return lax.psum(value, axis)
    step = 1
    while step < size:
        value = value.astype(jnp.bfloat16)
        value = value.astype(jnp.float32) + lax.ppermute(
            value, axis, [(i, i ^ step) for i in range(size)]
        ).astype(jnp.float32)
        step *= 2
    return value


def block_weights(spec_real, spec_imag):
    upper_row = jnp.concatenate([spec_real, spec_imag], axis=2)
    lower_row = jnp.concatenate([-spec_imag, spec_real], axis=2)
    return jnp.concatenate([upper_row, lower_row], axis=1)


def spatial_rims(field_block, channels):
    x_wide = padded_2(field_block, (("gx", 2),), 2 * channels, True)
    inner = padded_2(x_wide, (("gy", 1),), 1, False)
    size = lax.axis_size("gz")
    up = [(i, i + 1) for i in range(size - 1)]
    down = [(j, i) for i, j in up]
    below = lax.ppermute(inner[-1:], "gz", up)
    above = lax.ppermute(inner[:1], "gz", down)
    return (inner, below, above)


def stencil_kernel(chunk, x_pad, y_cells, rows, plan, sources, has_acc, *refs):
    src_refs = refs[:sources]
    acc_ref = refs[sources] if has_acc else None
    w_ref, o_ref = refs[sources + has_acc :]
    width = chunk + 2 * x_pad
    count = o_ref.shape[2] // chunk
    shift = chunk + x_pad - x_pad // 2
    side = (chunk + x_pad) // 128

    def body(index, carry):
        base = pl.multiple_of(index * chunk, chunk)
        for plane, terms in enumerate(plan):
            for row in range(0, y_cells, rows):
                left = jnp.zeros((rows, chunk + x_pad), jnp.float32)
                centre = jnp.zeros((rows, chunk), jnp.float32)
                right = jnp.zeros((rows, chunk + x_pad), jnp.float32)
                for source, source_plane, step_z in terms:
                    for step_y in range(3):
                        window = src_refs[source][
                            source_plane, pl.ds(row + step_y, rows), pl.ds(base, width)
                        ].astype(jnp.float32)
                        tap = 9 * step_z + 3 * step_y
                        gain_l = jnp.concatenate([w_ref[tap]] * side, axis=1)
                        gain_c = jnp.concatenate([w_ref[tap + 1]] * (side - 1), axis=1)
                        gain_r = jnp.concatenate([w_ref[tap + 2]] * side, axis=1)
                        left = left + window[:, : chunk + x_pad] * gain_l
                        centre = centre + window[:, x_pad : x_pad + chunk] * gain_c
                        right = right + window[:, x_pad:] * gain_r
                total = (
                    centre
                    + pltpu.roll(left, shift, 1)[:, :chunk]
                    + pltpu.roll(right, shift, 1)[:, :chunk]
                )
                if has_acc:
                    total = total + acc_ref[plane, pl.ds(row, rows), pl.ds(base, chunk)]
                o_ref[plane, pl.ds(row, rows), pl.ds(base, chunk)] = total.astype(o_ref.dtype)
        return carry

    lax.fori_loop(0, count, body, 0)


def stencil_call(plan, inputs, acc, gains, y_cells, lanes, channels, out_dtype):
    chunk = min(1024, lanes)
    rows = 8 if y_cells % 8 == 0 else y_cells
    kernel = functools.partial(
        stencil_kernel, chunk, 2 * channels, y_cells, rows, plan, len(inputs), acc is not None
    )
    operands = list(inputs) + ([acc] if acc is not None else []) + [gains]
    return pl.pallas_call(
        kernel,
        out_shape=jax.ShapeDtypeStruct((len(plan), y_cells, lanes), out_dtype),
    )(*operands)


def depthwise(rims, taps, flipped, x_cells, channels, out_dtype=jnp.float32):
    inner, below, above = rims
    planes = inner.shape[0]
    y_cells = inner.shape[1] - 2
    lanes = x_cells * channels
    rows = 8 if y_cells % 8 == 0 else y_cells
    if flipped:
        taps = taps[::-1]
    gains = jnp.tile(taps.astype(jnp.float32), (1, 128 // channels))
    gains = jnp.broadcast_to(gains[:, None, :], (gains.shape[0], rows, 128))
    local_plan = tuple(
        tuple((0, plane + step_z - 1, step_z) for step_z in range(3) if 0 <= plane + step_z - 1 < planes)
        for plane in range(planes)
    )
    local = stencil_call(local_plan, (inner,), None, gains, y_cells, lanes, channels, jnp.float32)
    rim_plan = tuple(
        ((((0, 0, 0),) if plane == 0 else ()) + (((1, 0, 2),) if plane == planes - 1 else ()))
        for plane in range(planes)
    )
    return stencil_call(rim_plan, (below, above), local, gains, y_cells, lanes, channels, out_dtype)


def share_terms(field3, cos_table, sin_table):
    real_part = jnp.einsum("rxc,xk->krc", field3, cos_table, preferred_element_type=jnp.float32)
    imag_part = jnp.einsum("rxc,xk->krc", field3, sin_table, preferred_element_type=jnp.float32)
    return ring_reduce_scatter(jnp.concatenate([real_part, imag_part], axis=2), "gx")


def share_inverse(modes_share, cos_table, sin_table, channels):
    segment = ring_gather(modes_share, "gx")
    running = jnp.einsum(
        "krc,xk->rxc", segment[:, :, :channels], cos_table, preferred_element_type=jnp.float32
    )
    return running + jnp.einsum(
        "krc,xk->rxc", segment[:, :, channels:], sin_table, preferred_element_type=jnp.float32
    )


def split_gradients(dblock, channels):
    grad_real = dblock[:, :channels, :channels] + dblock[:, channels:, channels:]
    grad_imag = dblock[:, :channels, channels:] - dblock[:, channels:, :channels]
    return jnp.stack([grad_real, grad_imag])


def sum_gradients(local_grads):
    flat = local_grads.reshape(-1, 1024)
    return butterfly_sum(butterfly_sum(flat, "gy"), "gz").reshape(local_grads.shape)


def per_device(
    features, depth_weight, expand_weight, project_weight, spec_real, spec_imag, cotangent
):
    planes, y_cells, merged = features.shape
    channels = depth_weight.shape[1]
    x_cells = merged // channels
    row_count = planes * y_cells
    mode_count = spec_real.shape[0]
    group_size = lax.axis_size("gx")
    x_length = x_cells * group_size
    x_start = lax.axis_index("gx") * x_cells
    share_size = mode_count // group_size
    cos_part, sin_part = dft_tables(
        x_start, x_cells, x_length, jnp.arange(mode_count, dtype=jnp.int32)
    )
    order = gathered_order("gx", share_size)
    cos_order, sin_order = dft_tables(x_start, x_cells, x_length, order)
    cos_scaled = scaled_table(cos_order, order, x_length)
    sin_scaled = scaled_table(sin_order, order, x_length)
    cos_fwd_scaled = scaled_table(cos_part, jnp.arange(mode_count, dtype=jnp.int32), x_length)
    sin_fwd_scaled = scaled_table(sin_part, jnp.arange(mode_count, dtype=jnp.int32), x_length)
    blocks = block_weights(spec_real, spec_imag)
    padded = spatial_rims(features, channels)
    activation = depthwise(padded, depth_weight, False, x_cells, channels, jnp.bfloat16)
    field3 = features.reshape(row_count, x_cells, channels)
    owned_blocks = lax.dynamic_slice_in_dim(
        blocks, lax.axis_index("gx") * share_size, share_size, 0
    )
    coeffs = share_terms(field3, cos_part, sin_part).astype(jnp.bfloat16)
    mixed_modes = jnp.einsum(
        "krc,kco->kro", coeffs, owned_blocks, preferred_element_type=jnp.float32
    ).astype(jnp.bfloat16)
    mixed_modes, activation = lax.optimization_barrier((mixed_modes, activation))
    activation = activation.reshape(row_count * x_cells, channels)
    hidden_pre = jnp.dot(activation, expand_weight, preferred_element_type=jnp.float32)
    hidden, hidden_slope = gelu_parts(hidden_pre)
    local_branch = jnp.dot(
        hidden.astype(jnp.bfloat16), project_weight, preferred_element_type=jnp.float32
    )
    local_branch = local_branch.reshape(row_count, x_cells, channels)
    spectral = share_inverse(mixed_modes, cos_scaled, sin_scaled, channels)
    result, slopes = gelu_parts(local_branch + spectral)
    output = result.astype(jnp.bfloat16).reshape(planes, y_cells, merged)
    grad_pre = (
        lax.optimization_barrier(cotangent.reshape(row_count, x_cells, channels)).astype(jnp.float32)
        * slopes
    ).astype(jnp.bfloat16)
    hidden_grad = jnp.dot(
        grad_pre.reshape(row_count * x_cells, channels),
        project_weight.T,
        preferred_element_type=jnp.float32,
    )
    grad_hidden = (hidden_grad * hidden_slope).astype(jnp.bfloat16)
    grad_act = jnp.dot(grad_hidden, expand_weight.T, preferred_element_type=jnp.float32).astype(
        jnp.bfloat16
    )
    grad_act = grad_act.reshape(planes, y_cells, merged)
    dcoef = share_terms(grad_pre, cos_fwd_scaled, sin_fwd_scaled).astype(jnp.bfloat16)
    dmode = jnp.einsum(
        "kro,kco->krc", dcoef, owned_blocks, preferred_element_type=jnp.float32
    ).astype(jnp.bfloat16)
    dblock = jnp.einsum("krc,kro->kco", coeffs, dcoef, preferred_element_type=jnp.float32)
    local_grads = split_gradients(dblock, channels)
    dmode, local_grads, grad_act = lax.optimization_barrier((dmode, local_grads, grad_act))
    spectral_grad = share_inverse(dmode, cos_order, sin_order, channels)
    spectral_grad = spectral_grad.reshape(planes, y_cells, merged)
    spectral_grad, local_grads = lax.optimization_barrier((spectral_grad, local_grads))
    grad_spec = sum_gradients(local_grads)
    padded_grad = spatial_rims(grad_act, channels)
    grad_local = depthwise(padded_grad, depth_weight, True, x_cells, channels)
    grad_features = (grad_local + spectral_grad).astype(
        jnp.bfloat16
    )
    return (output, grad_features, grad_spec)


def solution(mesh):
    placed = (P("gz", "gy", "gx"), P(), P(), P(), P(), P(), P("gz", "gy", "gx"))
    return jax.shard_map(
        per_device,
        mesh=mesh,
        in_specs=placed,
        out_specs=(P("gz", "gy", "gx"), P("gz", "gy", "gx"), P(None, "gx", None, None)),
        check_vma=False,
    )
```

```python
import functools
import math

import jax
import jax.numpy as jnp
from jax import lax
from jax.experimental import pallas as pl
from jax.experimental.pallas import tpu as pltpu
from jax.sharding import PartitionSpec as P


def padded_2(value, sides, width, wrap):
    for axis, dim in sides:
        size, length = (lax.axis_size(axis), value.shape[dim])
        last = lax.slice_in_dim(value, length - width, length, axis=dim)
        leading = lax.slice_in_dim(value, 0, width, axis=dim)
        if size == 2 and not wrap:
            first = lax.axis_index(axis) == 0
            swapped = lax.ppermute(jnp.where(first, last, leading), axis, [(0, 1), (1, 0)])
            zeros = jnp.zeros_like(swapped)
            before = jnp.where(first, zeros, swapped)
            after = jnp.where(first, swapped, zeros)
        else:
            up = [(i, (i + 1) % size) for i in range(size if wrap else size - 1)]
            down = [(j, i) for i, j in up]
            before = lax.ppermute(last, axis, up)
            after = lax.ppermute(leading, axis, down)
        value = jnp.concatenate([before, value, after], axis=dim)
    return value


def gelu_parts(values):
    normal_cdf = 0.5 * (1.0 + jax.scipy.special.erf(values * (1.0 / math.sqrt(2.0))))
    density = jnp.exp(-0.5 * values * values) * (1.0 / math.sqrt(2.0 * math.pi))
    return (values * normal_cdf, normal_cdf + values * density)


def dft_tables(offset, cells, x_length, frequency):
    position = offset + jnp.arange(cells, dtype=jnp.int32)
    phase_int = position[:, None] * frequency[None, :] % x_length
    angles = phase_int.astype(jnp.float32) * (2.0 * math.pi / x_length)
    return (jnp.cos(angles).astype(jnp.bfloat16), (-jnp.sin(angles)).astype(jnp.bfloat16))


def scaled_table(table, frequency, x_length):
    mode_scale = jnp.where(frequency == 0, 1.0, 2.0).astype(jnp.float32) / x_length
    return (table.astype(jnp.float32) * mode_scale[None, :]).astype(jnp.bfloat16)


def gathered_order(axis, share_size):
    size = lax.axis_size(axis)
    shifts = jnp.arange(size, dtype=jnp.int32)
    me = lax.axis_index(axis)
    if size & (size - 1):
        sources = (me - shifts) % size
    else:
        sources = jnp.bitwise_xor(me, shifts)
    local = jnp.arange(share_size, dtype=jnp.int32)
    return (sources[:, None] * share_size + local[None, :]).reshape(-1)


def ring_gather(block, axis):
    size = lax.axis_size(axis)
    if size & (size - 1) == 0:
        step = 1
        while step < size:
            block = jnp.concatenate(
                [block, lax.ppermute(block, axis, [(i, i ^ step) for i in range(size)])], axis=0
            )
            step *= 2
        return block
    pieces = [block]
    for shift in range(1, size):
        pieces.append(lax.ppermute(block, axis, [(i, (i + shift) % size) for i in range(size)]))
    return jnp.concatenate(pieces, axis=0)


def ring_reduce_scatter(value, axis):
    size = lax.axis_size(axis)
    share = value.shape[0] // size
    me = lax.axis_index(axis)
    if size & (size - 1) == 0:
        step = size // 2
        count = size
        while step >= 1:
            count //= 2
            upper = jnp.bitwise_and(me, step) != 0
            keep = lax.dynamic_slice_in_dim(value, jnp.where(upper, count, 0) * share, count * share, 0)
            send = lax.dynamic_slice_in_dim(value, jnp.where(upper, 0, count) * share, count * share, 0)
            value = keep + lax.ppermute(send, axis, [(i, i ^ step) for i in range(size)])
            step //= 2
        return value
    total = lax.dynamic_slice_in_dim(value, me * share, share, 0)
    for shift in range(1, size):
        piece = lax.dynamic_slice_in_dim(value, ((me + shift) % size) * share, share, 0)
        total = total + lax.ppermute(piece, axis, [(i, (i + shift) % size) for i in range(size)])
    return total


def butterfly_sum(value, axis):
    size = lax.axis_size(axis)
    if size & (size - 1):
        return lax.psum(value, axis)
    step = 1
    while step < size:
        value = value.astype(jnp.bfloat16)
        value = value.astype(jnp.float32) + lax.ppermute(
            value, axis, [(i, i ^ step) for i in range(size)]
        ).astype(jnp.float32)
        step *= 2
    return value


def block_weights(spec_real, spec_imag):
    upper_row = jnp.concatenate([spec_real, spec_imag], axis=2)
    lower_row = jnp.concatenate([-spec_imag, spec_real], axis=2)
    return jnp.concatenate([upper_row, lower_row], axis=1)


def spatial_rims(field_block, channels):
    x_wide = padded_2(field_block, (("gx", 2),), 2 * channels, True)
    inner = padded_2(x_wide, (("gy", 1),), 1, False)
    size = lax.axis_size("gz")
    up = [(i, i + 1) for i in range(size - 1)]
    down = [(j, i) for i, j in up]
    below = lax.ppermute(inner[-1:], "gz", up)
    above = lax.ppermute(inner[:1], "gz", down)
    return (inner, below, above)


def stencil_kernel(chunk, x_pad, y_cells, rows, plan, sources, has_acc, *refs):
    src_refs = refs[:sources]
    acc_ref = refs[sources] if has_acc else None
    w_ref, o_ref = refs[sources + has_acc :]
    width = chunk + 2 * x_pad
    count = o_ref.shape[2] // chunk
    shift = chunk + x_pad - x_pad // 2
    side = (chunk + x_pad) // 128

    def body(index, carry):
        base = pl.multiple_of(index * chunk, chunk)
        for plane, terms in enumerate(plan):
            for row in range(0, y_cells, rows):
                left = jnp.zeros((rows, chunk + x_pad), jnp.float32)
                centre = jnp.zeros((rows, chunk), jnp.float32)
                right = jnp.zeros((rows, chunk + x_pad), jnp.float32)
                for source, source_plane, step_z in terms:
                    for step_y in range(3):
                        window = src_refs[source][
                            source_plane, pl.ds(row + step_y, rows), pl.ds(base, width)
                        ].astype(jnp.float32)
                        tap = 9 * step_z + 3 * step_y
                        gain_l = jnp.concatenate([w_ref[tap]] * side, axis=1)
                        gain_c = jnp.concatenate([w_ref[tap + 1]] * (side - 1), axis=1)
                        gain_r = jnp.concatenate([w_ref[tap + 2]] * side, axis=1)
                        left = left + window[:, : chunk + x_pad] * gain_l
                        centre = centre + window[:, x_pad : x_pad + chunk] * gain_c
                        right = right + window[:, x_pad:] * gain_r
                total = (
                    centre
                    + pltpu.roll(left, shift, 1)[:, :chunk]
                    + pltpu.roll(right, shift, 1)[:, :chunk]
                )
                if has_acc:
                    total = total + acc_ref[plane, pl.ds(row, rows), pl.ds(base, chunk)]
                o_ref[plane, pl.ds(row, rows), pl.ds(base, chunk)] = total.astype(o_ref.dtype)
        return carry

    lax.fori_loop(0, count, body, 0)


def stencil_call(plan, inputs, acc, gains, y_cells, lanes, channels, out_dtype):
    chunk = min(1024, lanes)
    rows = 8 if y_cells % 8 == 0 else y_cells
    kernel = functools.partial(
        stencil_kernel, chunk, 2 * channels, y_cells, rows, plan, len(inputs), acc is not None
    )
    operands = list(inputs) + ([acc] if acc is not None else []) + [gains]
    return pl.pallas_call(
        kernel,
        out_shape=jax.ShapeDtypeStruct((len(plan), y_cells, lanes), out_dtype),
    )(*operands)


def depthwise(rims, taps, flipped, x_cells, channels, out_dtype=jnp.float32):
    inner, below, above = rims
    planes = inner.shape[0]
    y_cells = inner.shape[1] - 2
    lanes = x_cells * channels
    rows = 8 if y_cells % 8 == 0 else y_cells
    if flipped:
        taps = taps[::-1]
    gains = jnp.tile(taps.astype(jnp.float32), (1, 128 // channels))
    gains = jnp.broadcast_to(gains[:, None, :], (gains.shape[0], rows, 128))
    local_plan = tuple(
        tuple((0, plane + step_z - 1, step_z) for step_z in range(3) if 0 <= plane + step_z - 1 < planes)
        for plane in range(planes)
    )
    local = stencil_call(local_plan, (inner,), None, gains, y_cells, lanes, channels, jnp.float32)
    rim_plan = tuple(
        ((((0, 0, 0),) if plane == 0 else ()) + (((1, 0, 2),) if plane == planes - 1 else ()))
        for plane in range(planes)
    )
    return stencil_call(rim_plan, (below, above), local, gains, y_cells, lanes, channels, out_dtype)


def share_terms(field3, cos_table, sin_table):
    modes = cos_table.shape[1]
    table = jnp.concatenate([cos_table, sin_table], axis=1)
    both = jnp.einsum("rxc,xk->krc", field3, table, preferred_element_type=jnp.float32)
    return ring_reduce_scatter(jnp.concatenate([both[:modes], both[modes:]], axis=2), "gx")


def share_inverse(modes_share, cos_table, sin_table, channels):
    segment = ring_gather(modes_share, "gx")
    stacked = jnp.concatenate([segment[:, :, :channels], segment[:, :, channels:]], axis=0)
    table = jnp.concatenate([cos_table, sin_table], axis=1)
    return jnp.einsum("krc,xk->rxc", stacked, table, preferred_element_type=jnp.float32)


def split_gradients(dblock, channels):
    grad_real = dblock[:, :channels, :channels] + dblock[:, channels:, channels:]
    grad_imag = dblock[:, :channels, channels:] - dblock[:, channels:, :channels]
    return jnp.stack([grad_real, grad_imag])


def sum_gradients(local_grads):
    flat = local_grads.reshape(-1, 1024)
    return butterfly_sum(butterfly_sum(flat, "gy"), "gz").reshape(local_grads.shape)


def per_device(
    features, depth_weight, expand_weight, project_weight, spec_real, spec_imag, cotangent
):
    planes, y_cells, merged = features.shape
    channels = depth_weight.shape[1]
    x_cells = merged // channels
    row_count = planes * y_cells
    mode_count = spec_real.shape[0]
    group_size = lax.axis_size("gx")
    x_length = x_cells * group_size
    x_start = lax.axis_index("gx") * x_cells
    share_size = mode_count // group_size
    cos_part, sin_part = dft_tables(
        x_start, x_cells, x_length, jnp.arange(mode_count, dtype=jnp.int32)
    )
    order = gathered_order("gx", share_size)
    cos_order, sin_order = dft_tables(x_start, x_cells, x_length, order)
    cos_scaled = scaled_table(cos_order, order, x_length)
    sin_scaled = scaled_table(sin_order, order, x_length)
    cos_fwd_scaled = scaled_table(cos_part, jnp.arange(mode_count, dtype=jnp.int32), x_length)
    sin_fwd_scaled = scaled_table(sin_part, jnp.arange(mode_count, dtype=jnp.int32), x_length)
    blocks = block_weights(spec_real, spec_imag)
    padded = spatial_rims(features, channels)
    activation = depthwise(padded, depth_weight, False, x_cells, channels, jnp.bfloat16)
    field3 = features.reshape(row_count, x_cells, channels)
    owned_blocks = lax.dynamic_slice_in_dim(
        blocks, lax.axis_index("gx") * share_size, share_size, 0
    )
    coeffs = share_terms(field3, cos_part, sin_part).astype(jnp.bfloat16)
    mixed_modes = jnp.einsum(
        "krc,kco->kro", coeffs, owned_blocks, preferred_element_type=jnp.float32
    ).astype(jnp.bfloat16)
    mixed_modes, activation = lax.optimization_barrier((mixed_modes, activation))
    activation = activation.reshape(row_count * x_cells, channels)
    hidden_pre = jnp.dot(activation, expand_weight, preferred_element_type=jnp.float32)
    hidden, hidden_slope = gelu_parts(hidden_pre)
    local_branch = jnp.dot(
        hidden.astype(jnp.bfloat16), project_weight, preferred_element_type=jnp.float32
    )
    local_branch = local_branch.reshape(row_count, x_cells, channels)
    spectral = share_inverse(mixed_modes, cos_scaled, sin_scaled, channels)
    result, slopes = gelu_parts(local_branch + spectral)
    output = result.astype(jnp.bfloat16).reshape(planes, y_cells, merged)
    grad_pre = (
        lax.optimization_barrier(cotangent.reshape(row_count, x_cells, channels)).astype(jnp.float32)
        * slopes
    ).astype(jnp.bfloat16)
    hidden_grad = jnp.dot(
        grad_pre.reshape(row_count * x_cells, channels),
        project_weight.T,
        preferred_element_type=jnp.float32,
    )
    grad_hidden = (hidden_grad * hidden_slope).astype(jnp.bfloat16)
    grad_act = jnp.dot(grad_hidden, expand_weight.T, preferred_element_type=jnp.float32).astype(
        jnp.bfloat16
    )
    grad_act = grad_act.reshape(planes, y_cells, merged)
    dcoef = share_terms(grad_pre, cos_fwd_scaled, sin_fwd_scaled).astype(jnp.bfloat16)
    dmode = jnp.einsum(
        "kro,kco->krc", dcoef, owned_blocks, preferred_element_type=jnp.float32
    ).astype(jnp.bfloat16)
    dblock = jnp.einsum("krc,kro->kco", coeffs, dcoef, preferred_element_type=jnp.float32)
    local_grads = split_gradients(dblock, channels)
    dmode, local_grads, grad_act = lax.optimization_barrier((dmode, local_grads, grad_act))
    spectral_grad = share_inverse(dmode, cos_order, sin_order, channels)
    grad_spec = sum_gradients(local_grads)
    padded_grad = spatial_rims(grad_act, channels)
    grad_local = depthwise(padded_grad, depth_weight, True, x_cells, channels)
    grad_features = (grad_local + spectral_grad.reshape(planes, y_cells, merged)).astype(
        jnp.bfloat16
    )
    return (output, grad_features, grad_spec)


def solution(mesh):
    placed = (P("gz", "gy", "gx"), P(), P(), P(), P(), P(), P("gz", "gy", "gx"))
    return jax.shard_map(
        per_device,
        mesh=mesh,
        in_specs=placed,
        out_specs=(P("gz", "gy", "gx"), P("gz", "gy", "gx"), P(None, "gx", None, None)),
        check_vma=False,
    )
```

```python
import functools
import math

import jax
import jax.numpy as jnp
from jax import lax
from jax.experimental import pallas as pl
from jax.experimental.pallas import tpu as pltpu
from jax.sharding import PartitionSpec as P


def padded_2(value, sides, width, wrap):
    for axis, dim in sides:
        size, length = (lax.axis_size(axis), value.shape[dim])
        last = lax.slice_in_dim(value, length - width, length, axis=dim)
        leading = lax.slice_in_dim(value, 0, width, axis=dim)
        if size == 2 and not wrap:
            first = lax.axis_index(axis) == 0
            swapped = lax.ppermute(jnp.where(first, last, leading), axis, [(0, 1), (1, 0)])
            zeros = jnp.zeros_like(swapped)
            before = jnp.where(first, zeros, swapped)
            after = jnp.where(first, swapped, zeros)
        else:
            up = [(i, (i + 1) % size) for i in range(size if wrap else size - 1)]
            down = [(j, i) for i, j in up]
            before = lax.ppermute(last, axis, up)
            after = lax.ppermute(leading, axis, down)
        value = jnp.concatenate([before, value, after], axis=dim)
    return value


def gelu_parts(values):
    normal_cdf = 0.5 * (1.0 + jax.scipy.special.erf(values * (1.0 / math.sqrt(2.0))))
    density = jnp.exp(-0.5 * values * values) * (1.0 / math.sqrt(2.0 * math.pi))
    return (values * normal_cdf, normal_cdf + values * density)


def dft_tables(offset, cells, x_length, frequency):
    position = offset + jnp.arange(cells, dtype=jnp.int32)
    phase_int = position[:, None] * frequency[None, :] % x_length
    angles = phase_int.astype(jnp.float32) * (2.0 * math.pi / x_length)
    return (jnp.cos(angles).astype(jnp.bfloat16), (-jnp.sin(angles)).astype(jnp.bfloat16))


def scaled_table(table, frequency, x_length):
    mode_scale = jnp.where(frequency == 0, 1.0, 2.0).astype(jnp.float32) / x_length
    return (table.astype(jnp.float32) * mode_scale[None, :]).astype(jnp.bfloat16)


def gathered_order(axis, share_size):
    size = lax.axis_size(axis)
    shifts = jnp.arange(size, dtype=jnp.int32)
    me = lax.axis_index(axis)
    if size & (size - 1):
        sources = (me - shifts) % size
    else:
        sources = jnp.bitwise_xor(me, shifts)
    local = jnp.arange(share_size, dtype=jnp.int32)
    return (sources[:, None] * share_size + local[None, :]).reshape(-1)


def ring_gather(block, axis):
    size = lax.axis_size(axis)
    if size & (size - 1) == 0:
        step = 1
        while step < size:
            block = jnp.concatenate(
                [block, lax.ppermute(block, axis, [(i, i ^ step) for i in range(size)])], axis=0
            )
            step *= 2
        return block
    pieces = [block]
    for shift in range(1, size):
        pieces.append(lax.ppermute(block, axis, [(i, (i + shift) % size) for i in range(size)]))
    return jnp.concatenate(pieces, axis=0)


def ring_reduce_scatter(value, axis):
    size = lax.axis_size(axis)
    share = value.shape[0] // size
    me = lax.axis_index(axis)
    if size & (size - 1) == 0:
        step = size // 2
        count = size
        while step >= 1:
            count //= 2
            upper = jnp.bitwise_and(me, step) != 0
            keep = lax.dynamic_slice_in_dim(value, jnp.where(upper, count, 0) * share, count * share, 0)
            send = lax.dynamic_slice_in_dim(value, jnp.where(upper, 0, count) * share, count * share, 0)
            value = keep + lax.ppermute(send, axis, [(i, i ^ step) for i in range(size)])
            step //= 2
        return value
    total = lax.dynamic_slice_in_dim(value, me * share, share, 0)
    for shift in range(1, size):
        piece = lax.dynamic_slice_in_dim(value, ((me + shift) % size) * share, share, 0)
        total = total + lax.ppermute(piece, axis, [(i, (i + shift) % size) for i in range(size)])
    return total


def butterfly_sum(value, axis):
    size = lax.axis_size(axis)
    if size & (size - 1):
        return lax.psum(value, axis)
    step = 1
    while step < size:
        value = value.astype(jnp.bfloat16)
        value = value.astype(jnp.float32) + lax.ppermute(
            value, axis, [(i, i ^ step) for i in range(size)]
        ).astype(jnp.float32)
        step *= 2
    return value


def block_weights(spec_real, spec_imag):
    upper_row = jnp.concatenate([spec_real, spec_imag], axis=2)
    lower_row = jnp.concatenate([-spec_imag, spec_real], axis=2)
    return jnp.concatenate([upper_row, lower_row], axis=1)


def spatial_rims(field_block, channels):
    x_wide = padded_2(field_block, (("gx", 2),), 2 * channels, True)
    inner = padded_2(x_wide, (("gy", 1),), 1, False)
    size = lax.axis_size("gz")
    up = [(i, i + 1) for i in range(size - 1)]
    down = [(j, i) for i, j in up]
    below = lax.ppermute(inner[-1:], "gz", up)
    above = lax.ppermute(inner[:1], "gz", down)
    return (inner, below, above)


def stencil_kernel(chunk, x_pad, y_cells, rows, plan, sources, has_acc, *refs):
    src_refs = refs[:sources]
    acc_ref = refs[sources] if has_acc else None
    w_ref, o_ref = refs[sources + has_acc :]
    width = chunk + 2 * x_pad
    count = o_ref.shape[2] // chunk
    shift = chunk + x_pad - x_pad // 2
    side = (chunk + x_pad) // 128

    def body(index, carry):
        base = pl.multiple_of(index * chunk, chunk)
        for plane, terms in enumerate(plan):
            for row in range(0, y_cells, rows):
                left = jnp.zeros((rows, chunk + x_pad), jnp.float32)
                centre = jnp.zeros((rows, chunk), jnp.float32)
                right = jnp.zeros((rows, chunk + x_pad), jnp.float32)
                for source, source_plane, step_z in terms:
                    for step_y in range(3):
                        window = src_refs[source][
                            source_plane, pl.ds(row + step_y, rows), pl.ds(base, width)
                        ].astype(jnp.float32)
                        tap = 9 * step_z + 3 * step_y
                        gain_l = jnp.concatenate([w_ref[tap]] * side, axis=1)
                        gain_c = jnp.concatenate([w_ref[tap + 1]] * (side - 1), axis=1)
                        gain_r = jnp.concatenate([w_ref[tap + 2]] * side, axis=1)
                        left = left + window[:, : chunk + x_pad] * gain_l
                        centre = centre + window[:, x_pad : x_pad + chunk] * gain_c
                        right = right + window[:, x_pad:] * gain_r
                total = (
                    centre
                    + pltpu.roll(left, shift, 1)[:, :chunk]
                    + pltpu.roll(right, shift, 1)[:, :chunk]
                )
                if has_acc:
                    total = total + acc_ref[plane, pl.ds(row, rows), pl.ds(base, chunk)]
                o_ref[plane, pl.ds(row, rows), pl.ds(base, chunk)] = total.astype(o_ref.dtype)
        return carry

    lax.fori_loop(0, count, body, 0)


def stencil_call(plan, inputs, acc, gains, y_cells, lanes, channels, out_dtype):
    chunk = min(1024, lanes)
    rows = 8 if y_cells % 8 == 0 else y_cells
    kernel = functools.partial(
        stencil_kernel, chunk, 2 * channels, y_cells, rows, plan, len(inputs), acc is not None
    )
    operands = list(inputs) + ([acc] if acc is not None else []) + [gains]
    return pl.pallas_call(
        kernel,
        out_shape=jax.ShapeDtypeStruct((len(plan), y_cells, lanes), out_dtype),
    )(*operands)


def depthwise(rims, taps, flipped, x_cells, channels, out_dtype=jnp.float32):
    inner, below, above = rims
    planes = inner.shape[0]
    y_cells = inner.shape[1] - 2
    lanes = x_cells * channels
    rows = 8 if y_cells % 8 == 0 else y_cells
    if flipped:
        taps = taps[::-1]
    gains = jnp.tile(taps.astype(jnp.float32), (1, 128 // channels))
    gains = jnp.broadcast_to(gains[:, None, :], (gains.shape[0], rows, 128))
    local_plan = tuple(
        tuple((0, plane + step_z - 1, step_z) for step_z in range(3) if 0 <= plane + step_z - 1 < planes)
        for plane in range(planes)
    )
    local = stencil_call(local_plan, (inner,), None, gains, y_cells, lanes, channels, jnp.float32)
    rim_plan = tuple(
        ((((0, 0, 0),) if plane == 0 else ()) + (((1, 0, 2),) if plane == planes - 1 else ()))
        for plane in range(planes)
    )
    return stencil_call(rim_plan, (below, above), local, gains, y_cells, lanes, channels, out_dtype)


def share_terms(field3, cos_table, sin_table):
    real_part = jnp.einsum("rxc,xk->krc", field3, cos_table, preferred_element_type=jnp.float32)
    imag_part = jnp.einsum("rxc,xk->krc", field3, sin_table, preferred_element_type=jnp.float32)
    return ring_reduce_scatter(jnp.concatenate([real_part, imag_part], axis=2), "gx")


def share_inverse(modes_share, cos_table, sin_table, channels):
    segment = ring_gather(modes_share, "gx")
    running = jnp.einsum(
        "krc,xk->rxc", segment[:, :, :channels], cos_table, preferred_element_type=jnp.float32
    )
    return running + jnp.einsum(
        "krc,xk->rxc", segment[:, :, channels:], sin_table, preferred_element_type=jnp.float32
    )


def split_gradients(dblock, channels):
    grad_real = dblock[:, :channels, :channels] + dblock[:, channels:, channels:]
    grad_imag = dblock[:, :channels, channels:] - dblock[:, channels:, :channels]
    return jnp.stack([grad_real, grad_imag])


def sum_gradients(local_grads):
    flat = local_grads.reshape(-1, 1024)
    return butterfly_sum(butterfly_sum(flat, "gy"), "gz").reshape(local_grads.shape)


def per_device(
    features, depth_weight, expand_weight, project_weight, spec_real, spec_imag, cotangent
):
    planes, y_cells, merged = features.shape
    channels = depth_weight.shape[1]
    x_cells = merged // channels
    row_count = planes * y_cells
    mode_count = spec_real.shape[0]
    group_size = lax.axis_size("gx")
    x_length = x_cells * group_size
    x_start = lax.axis_index("gx") * x_cells
    share_size = mode_count // group_size
    cos_part, sin_part = dft_tables(
        x_start, x_cells, x_length, jnp.arange(mode_count, dtype=jnp.int32)
    )
    order = gathered_order("gx", share_size)
    cos_order, sin_order = dft_tables(x_start, x_cells, x_length, order)
    cos_scaled = scaled_table(cos_order, order, x_length)
    sin_scaled = scaled_table(sin_order, order, x_length)
    cos_fwd_scaled = scaled_table(cos_part, jnp.arange(mode_count, dtype=jnp.int32), x_length)
    sin_fwd_scaled = scaled_table(sin_part, jnp.arange(mode_count, dtype=jnp.int32), x_length)
    blocks = block_weights(spec_real, spec_imag)
    padded = spatial_rims(features, channels)
    activation = depthwise(padded, depth_weight, False, x_cells, channels, jnp.bfloat16)
    field3 = features.reshape(row_count, x_cells, channels)
    owned_blocks = lax.dynamic_slice_in_dim(
        blocks, lax.axis_index("gx") * share_size, share_size, 0
    )
    coeffs = share_terms(field3, cos_part, sin_part).astype(jnp.bfloat16)
    mixed_modes = jnp.einsum(
        "krc,kco->kro", coeffs, owned_blocks, preferred_element_type=jnp.float32
    ).astype(jnp.bfloat16)
    mixed_modes, activation = lax.optimization_barrier((mixed_modes, activation))
    activation = activation.reshape(row_count * x_cells, channels)
    hidden_pre = jnp.dot(activation, expand_weight, preferred_element_type=jnp.float32)
    hidden, hidden_slope = gelu_parts(hidden_pre)
    local_branch = jnp.dot(
        hidden.astype(jnp.bfloat16), project_weight, preferred_element_type=jnp.float32
    )
    local_branch = local_branch.reshape(row_count, x_cells, channels)
    spectral = share_inverse(mixed_modes, cos_scaled, sin_scaled, channels)
    result, slopes = gelu_parts(local_branch + spectral)
    output = result.astype(jnp.bfloat16).reshape(planes, y_cells, merged)
    grad_pre = (
        lax.optimization_barrier(cotangent.reshape(row_count, x_cells, channels)).astype(jnp.float32)
        * slopes
    ).astype(jnp.bfloat16)
    hidden_grad = jnp.dot(
        grad_pre.reshape(row_count * x_cells, channels),
        project_weight.T,
        preferred_element_type=jnp.float32,
    )
    grad_hidden = (hidden_grad * hidden_slope).astype(jnp.bfloat16)
    grad_act = jnp.dot(grad_hidden, expand_weight.T, preferred_element_type=jnp.float32).astype(
        jnp.bfloat16
    )
    grad_act = grad_act.reshape(planes, y_cells, merged)
    dcoef = share_terms(grad_pre, cos_fwd_scaled, sin_fwd_scaled).astype(jnp.bfloat16)
    dmode = jnp.einsum(
        "kro,kco->krc", dcoef, owned_blocks, preferred_element_type=jnp.float32
    ).astype(jnp.bfloat16)
    dblock = jnp.einsum("krc,kro->kco", coeffs, dcoef, preferred_element_type=jnp.float32)
    local_grads = split_gradients(dblock, channels)
    spectral_grad = share_inverse(dmode, cos_order, sin_order, channels)
    grad_spec = sum_gradients(local_grads)
    padded_grad = spatial_rims(grad_act, channels)
    grad_local = depthwise(padded_grad, depth_weight, True, x_cells, channels)
    grad_features = (grad_local + spectral_grad.reshape(planes, y_cells, merged)).astype(
        jnp.bfloat16
    )
    return (output, grad_features, grad_spec)


def solution(mesh):
    placed = (P("gz", "gy", "gx"), P(), P(), P(), P(), P(), P("gz", "gy", "gx"))
    return jax.shard_map(
        per_device,
        mesh=mesh,
        in_specs=placed,
        out_specs=(P("gz", "gy", "gx"), P("gz", "gy", "gx"), P(None, "gx", None, None)),
        check_vma=False,
    )
```

```python
import functools
import math

import jax
import jax.numpy as jnp
from jax import lax
from jax.experimental import pallas as pl
from jax.experimental.pallas import tpu as pltpu
from jax.sharding import PartitionSpec as P


def padded_2(value, sides, width, wrap):
    for axis, dim in sides:
        size, length = (lax.axis_size(axis), value.shape[dim])
        last = lax.slice_in_dim(value, length - width, length, axis=dim)
        leading = lax.slice_in_dim(value, 0, width, axis=dim)
        if size == 2 and not wrap:
            first = lax.axis_index(axis) == 0
            swapped = lax.ppermute(jnp.where(first, last, leading), axis, [(0, 1), (1, 0)])
            zeros = jnp.zeros_like(swapped)
            before = jnp.where(first, zeros, swapped)
            after = jnp.where(first, swapped, zeros)
        else:
            up = [(i, (i + 1) % size) for i in range(size if wrap else size - 1)]
            down = [(j, i) for i, j in up]
            before = lax.ppermute(last, axis, up)
            after = lax.ppermute(leading, axis, down)
        value = jnp.concatenate([before, value, after], axis=dim)
    return value


def gelu_parts(values):
    normal_cdf = 0.5 * (1.0 + jax.scipy.special.erf(values * (1.0 / math.sqrt(2.0))))
    density = jnp.exp(-0.5 * values * values) * (1.0 / math.sqrt(2.0 * math.pi))
    return (values * normal_cdf, normal_cdf + values * density)


def dft_tables(offset, cells, x_length, frequency):
    position = offset + jnp.arange(cells, dtype=jnp.int32)
    phase_int = position[:, None] * frequency[None, :] % x_length
    angles = phase_int.astype(jnp.float32) * (2.0 * math.pi / x_length)
    return (jnp.cos(angles).astype(jnp.bfloat16), (-jnp.sin(angles)).astype(jnp.bfloat16))


def scaled_table(table, frequency, x_length):
    mode_scale = jnp.where(frequency == 0, 1.0, 2.0).astype(jnp.float32) / x_length
    return (table.astype(jnp.float32) * mode_scale[None, :]).astype(jnp.bfloat16)


def gathered_order(axis, share_size):
    size = lax.axis_size(axis)
    shifts = jnp.arange(size, dtype=jnp.int32)
    me = lax.axis_index(axis)
    if size & (size - 1):
        sources = (me - shifts) % size
    else:
        sources = jnp.bitwise_xor(me, shifts)
    local = jnp.arange(share_size, dtype=jnp.int32)
    return (sources[:, None] * share_size + local[None, :]).reshape(-1)


def ring_gather(block, axis):
    size = lax.axis_size(axis)
    if size & (size - 1) == 0:
        step = 1
        while step < size:
            block = jnp.concatenate(
                [block, lax.ppermute(block, axis, [(i, i ^ step) for i in range(size)])], axis=0
            )
            step *= 2
        return block
    pieces = [block]
    for shift in range(1, size):
        pieces.append(lax.ppermute(block, axis, [(i, (i + shift) % size) for i in range(size)]))
    return jnp.concatenate(pieces, axis=0)


def ring_reduce_scatter(value, axis):
    size = lax.axis_size(axis)
    share = value.shape[0] // size
    me = lax.axis_index(axis)
    if size & (size - 1) == 0:
        step = size // 2
        count = size
        while step >= 1:
            count //= 2
            upper = jnp.bitwise_and(me, step) != 0
            keep = lax.dynamic_slice_in_dim(value, jnp.where(upper, count, 0) * share, count * share, 0)
            send = lax.dynamic_slice_in_dim(value, jnp.where(upper, 0, count) * share, count * share, 0)
            value = keep + lax.ppermute(send, axis, [(i, i ^ step) for i in range(size)])
            step //= 2
        return value
    total = lax.dynamic_slice_in_dim(value, me * share, share, 0)
    for shift in range(1, size):
        piece = lax.dynamic_slice_in_dim(value, ((me + shift) % size) * share, share, 0)
        total = total + lax.ppermute(piece, axis, [(i, (i + shift) % size) for i in range(size)])
    return total


def butterfly_sum(value, axis):
    size = lax.axis_size(axis)
    if size & (size - 1):
        return lax.psum(value, axis)
    step = 1
    while step < size:
        value = value.astype(jnp.bfloat16)
        value = value.astype(jnp.float32) + lax.ppermute(
            value, axis, [(i, i ^ step) for i in range(size)]
        ).astype(jnp.float32)
        step *= 2
    return value


def block_weights(spec_real, spec_imag):
    upper_row = jnp.concatenate([spec_real, spec_imag], axis=2)
    lower_row = jnp.concatenate([-spec_imag, spec_real], axis=2)
    return jnp.concatenate([upper_row, lower_row], axis=1)


def spatial_rims(field_block, channels):
    x_wide = padded_2(field_block, (("gx", 2),), 2 * channels, True)
    inner = padded_2(x_wide, (("gy", 1),), 1, False)
    size = lax.axis_size("gz")
    up = [(i, i + 1) for i in range(size - 1)]
    down = [(j, i) for i, j in up]
    below = lax.ppermute(inner[-1:], "gz", up)
    above = lax.ppermute(inner[:1], "gz", down)
    return (inner, below, above)


def stencil_kernel(chunk, x_pad, y_cells, rows, plan, sources, has_acc, *refs):
    src_refs = refs[:sources]
    acc_ref = refs[sources] if has_acc else None
    w_ref, o_ref = refs[sources + has_acc :]
    width = chunk + 2 * x_pad
    count = o_ref.shape[2] // chunk
    shift = chunk + x_pad - x_pad // 2
    side = (chunk + x_pad) // 128

    def body(index, carry):
        base = pl.multiple_of(index * chunk, chunk)
        for plane, terms in enumerate(plan):
            for row in range(0, y_cells, rows):
                left = jnp.zeros((rows, chunk + x_pad), jnp.float32)
                centre = jnp.zeros((rows, chunk), jnp.float32)
                right = jnp.zeros((rows, chunk + x_pad), jnp.float32)
                for source, source_plane, step_z in terms:
                    for step_y in range(3):
                        window = src_refs[source][
                            source_plane, pl.ds(row + step_y, rows), pl.ds(base, width)
                        ].astype(jnp.float32)
                        tap = 9 * step_z + 3 * step_y
                        gain_l = jnp.concatenate([w_ref[tap]] * side, axis=1)
                        gain_c = jnp.concatenate([w_ref[tap + 1]] * (side - 1), axis=1)
                        gain_r = jnp.concatenate([w_ref[tap + 2]] * side, axis=1)
                        left = left + window[:, : chunk + x_pad] * gain_l
                        centre = centre + window[:, x_pad : x_pad + chunk] * gain_c
                        right = right + window[:, x_pad:] * gain_r
                total = (
                    centre
                    + pltpu.roll(left, shift, 1)[:, :chunk]
                    + pltpu.roll(right, shift, 1)[:, :chunk]
                )
                if has_acc:
                    total = total + acc_ref[plane, pl.ds(row, rows), pl.ds(base, chunk)]
                o_ref[plane, pl.ds(row, rows), pl.ds(base, chunk)] = total.astype(o_ref.dtype)
        return carry

    lax.fori_loop(0, count, body, 0)


def stencil_call(plan, inputs, acc, gains, y_cells, lanes, channels, out_dtype):
    chunk = min(1024, lanes)
    rows = 8 if y_cells % 8 == 0 else y_cells
    kernel = functools.partial(
        stencil_kernel, chunk, 2 * channels, y_cells, rows, plan, len(inputs), acc is not None
    )
    operands = list(inputs) + ([acc] if acc is not None else []) + [gains]
    return pl.pallas_call(
        kernel,
        out_shape=jax.ShapeDtypeStruct((len(plan), y_cells, lanes), out_dtype),
    )(*operands)


def depthwise(rims, taps, flipped, x_cells, channels, out_dtype=jnp.float32):
    inner, below, above = rims
    planes = inner.shape[0]
    y_cells = inner.shape[1] - 2
    lanes = x_cells * channels
    rows = 8 if y_cells % 8 == 0 else y_cells
    if flipped:
        taps = taps[::-1]
    gains = jnp.tile(taps.astype(jnp.float32), (1, 128 // channels))
    gains = jnp.broadcast_to(gains[:, None, :], (gains.shape[0], rows, 128))
    local_plan = tuple(
        tuple((0, plane + step_z - 1, step_z) for step_z in range(3) if 0 <= plane + step_z - 1 < planes)
        for plane in range(planes)
    )
    local = stencil_call(local_plan, (inner,), None, gains, y_cells, lanes, channels, jnp.float32)
    rim_plan = tuple(
        ((((0, 0, 0),) if plane == 0 else ()) + (((1, 0, 2),) if plane == planes - 1 else ()))
        for plane in range(planes)
    )
    return stencil_call(rim_plan, (below, above), local, gains, y_cells, lanes, channels, out_dtype)


def share_terms(field3, cos_table, sin_table):
    real_part = jnp.einsum("rxc,xk->krc", field3, cos_table, preferred_element_type=jnp.float32)
    imag_part = jnp.einsum("rxc,xk->krc", field3, sin_table, preferred_element_type=jnp.float32)
    return ring_reduce_scatter(jnp.concatenate([real_part, imag_part], axis=2), "gx")


def share_inverse(modes_share, cos_table, sin_table, channels):
    segment = ring_gather(modes_share, "gx")
    running = jnp.einsum(
        "krc,xk->rxc", segment[:, :, :channels], cos_table, preferred_element_type=jnp.float32
    )
    return running + jnp.einsum(
        "krc,xk->rxc", segment[:, :, channels:], sin_table, preferred_element_type=jnp.float32
    )


def split_gradients(dblock, channels):
    grad_real = dblock[:, :channels, :channels] + dblock[:, channels:, channels:]
    grad_imag = dblock[:, :channels, channels:] - dblock[:, channels:, :channels]
    return jnp.stack([grad_real, grad_imag])


def sum_gradients(local_grads):
    flat = local_grads.reshape(-1, 1024)
    return butterfly_sum(butterfly_sum(flat, "gy"), "gz").reshape(local_grads.shape)


def per_device(
    features, depth_weight, expand_weight, project_weight, spec_real, spec_imag, cotangent
):
    planes, y_cells, merged = features.shape
    channels = depth_weight.shape[1]
    x_cells = merged // channels
    row_count = planes * y_cells
    mode_count = spec_real.shape[0]
    group_size = lax.axis_size("gx")
    x_length = x_cells * group_size
    x_start = lax.axis_index("gx") * x_cells
    share_size = mode_count // group_size
    cos_part, sin_part = dft_tables(
        x_start, x_cells, x_length, jnp.arange(mode_count, dtype=jnp.int32)
    )
    order = gathered_order("gx", share_size)
    cos_order, sin_order = dft_tables(x_start, x_cells, x_length, order)
    cos_scaled = scaled_table(cos_order, order, x_length)
    sin_scaled = scaled_table(sin_order, order, x_length)
    cos_fwd_scaled = scaled_table(cos_part, jnp.arange(mode_count, dtype=jnp.int32), x_length)
    sin_fwd_scaled = scaled_table(sin_part, jnp.arange(mode_count, dtype=jnp.int32), x_length)
    blocks = block_weights(spec_real, spec_imag)
    padded = spatial_rims(features, channels)
    activation = depthwise(padded, depth_weight, False, x_cells, channels, jnp.bfloat16)
    field3 = features.reshape(row_count, x_cells, channels)
    owned_blocks = lax.dynamic_slice_in_dim(
        blocks, lax.axis_index("gx") * share_size, share_size, 0
    )
    coeffs = share_terms(field3, cos_part, sin_part).astype(jnp.bfloat16)
    mixed_modes = jnp.einsum(
        "krc,kco->kro", coeffs, owned_blocks, preferred_element_type=jnp.float32
    ).astype(jnp.bfloat16)
    activation = activation.reshape(row_count * x_cells, channels)
    hidden_pre = jnp.dot(activation, expand_weight, preferred_element_type=jnp.float32)
    hidden, hidden_slope = gelu_parts(hidden_pre)
    local_branch = jnp.dot(
        hidden.astype(jnp.bfloat16), project_weight, preferred_element_type=jnp.float32
    )
    local_branch = local_branch.reshape(row_count, x_cells, channels)
    spectral = share_inverse(mixed_modes, cos_scaled, sin_scaled, channels)
    result, slopes = gelu_parts(local_branch + spectral)
    output = result.astype(jnp.bfloat16).reshape(planes, y_cells, merged)
    grad_pre = (
        lax.optimization_barrier(cotangent.reshape(row_count, x_cells, channels)).astype(jnp.float32)
        * slopes
    ).astype(jnp.bfloat16)
    hidden_grad = jnp.dot(
        grad_pre.reshape(row_count * x_cells, channels),
        project_weight.T,
        preferred_element_type=jnp.float32,
    )
    grad_hidden = (hidden_grad * hidden_slope).astype(jnp.bfloat16)
    grad_act = jnp.dot(grad_hidden, expand_weight.T, preferred_element_type=jnp.float32).astype(
        jnp.bfloat16
    )
    grad_act = grad_act.reshape(planes, y_cells, merged)
    dcoef = share_terms(grad_pre, cos_fwd_scaled, sin_fwd_scaled).astype(jnp.bfloat16)
    dmode = jnp.einsum(
        "kro,kco->krc", dcoef, owned_blocks, preferred_element_type=jnp.float32
    ).astype(jnp.bfloat16)
    dblock = jnp.einsum("krc,kro->kco", coeffs, dcoef, preferred_element_type=jnp.float32)
    local_grads = split_gradients(dblock, channels)
    dmode, local_grads, grad_act = lax.optimization_barrier((dmode, local_grads, grad_act))
    spectral_grad = share_inverse(dmode, cos_order, sin_order, channels)
    grad_spec = sum_gradients(local_grads)
    padded_grad = spatial_rims(grad_act, channels)
    grad_local = depthwise(padded_grad, depth_weight, True, x_cells, channels)
    grad_features = (grad_local + spectral_grad.reshape(planes, y_cells, merged)).astype(
        jnp.bfloat16
    )
    return (output, grad_features, grad_spec)


def solution(mesh):
    placed = (P("gz", "gy", "gx"), P(), P(), P(), P(), P(), P("gz", "gy", "gx"))
    return jax.shard_map(
        per_device,
        mesh=mesh,
        in_specs=placed,
        out_specs=(P("gz", "gy", "gx"), P("gz", "gy", "gx"), P(None, "gx", None, None)),
        check_vma=False,
    )
```

```python
import functools
import math

import jax
import jax.numpy as jnp
from jax import lax
from jax.experimental import pallas as pl
from jax.experimental.pallas import tpu as pltpu
from jax.sharding import PartitionSpec as P


def padded_2(value, sides, width, wrap):
    for axis, dim in sides:
        size, length = (lax.axis_size(axis), value.shape[dim])
        last = lax.slice_in_dim(value, length - width, length, axis=dim)
        leading = lax.slice_in_dim(value, 0, width, axis=dim)
        if size == 2 and not wrap:
            first = lax.axis_index(axis) == 0
            swapped = lax.ppermute(jnp.where(first, last, leading), axis, [(0, 1), (1, 0)])
            zeros = jnp.zeros_like(swapped)
            before = jnp.where(first, zeros, swapped)
            after = jnp.where(first, swapped, zeros)
        else:
            up = [(i, (i + 1) % size) for i in range(size if wrap else size - 1)]
            down = [(j, i) for i, j in up]
            before = lax.ppermute(last, axis, up)
            after = lax.ppermute(leading, axis, down)
        value = jnp.concatenate([before, value, after], axis=dim)
    return value


def gelu_parts(values):
    normal_cdf = 0.5 * (1.0 + jax.scipy.special.erf(values * (1.0 / math.sqrt(2.0))))
    density = jnp.exp(-0.5 * values * values) * (1.0 / math.sqrt(2.0 * math.pi))
    return (values * normal_cdf, normal_cdf + values * density)


def dft_tables(offset, cells, x_length, frequency):
    position = offset + jnp.arange(cells, dtype=jnp.int32)
    phase_int = position[:, None] * frequency[None, :] % x_length
    angles = phase_int.astype(jnp.float32) * (2.0 * math.pi / x_length)
    return (jnp.cos(angles).astype(jnp.bfloat16), (-jnp.sin(angles)).astype(jnp.bfloat16))


def scaled_table(table, frequency, x_length):
    mode_scale = jnp.where(frequency == 0, 1.0, 2.0).astype(jnp.float32) / x_length
    return (table.astype(jnp.float32) * mode_scale[None, :]).astype(jnp.bfloat16)


def gathered_order(axis, share_size):
    size = lax.axis_size(axis)
    shifts = jnp.arange(size, dtype=jnp.int32)
    me = lax.axis_index(axis)
    if size & (size - 1):
        sources = (me - shifts) % size
    else:
        sources = jnp.bitwise_xor(me, shifts)
    local = jnp.arange(share_size, dtype=jnp.int32)
    return (sources[:, None] * share_size + local[None, :]).reshape(-1)


def ring_gather(block, axis):
    size = lax.axis_size(axis)
    if size & (size - 1) == 0:
        step = 1
        while step < size:
            block = jnp.concatenate(
                [block, lax.ppermute(block, axis, [(i, i ^ step) for i in range(size)])], axis=0
            )
            step *= 2
        return block
    pieces = [block]
    for shift in range(1, size):
        pieces.append(lax.ppermute(block, axis, [(i, (i + shift) % size) for i in range(size)]))
    return jnp.concatenate(pieces, axis=0)


def ring_reduce_scatter(value, axis):
    size = lax.axis_size(axis)
    share = value.shape[0] // size
    me = lax.axis_index(axis)
    if size & (size - 1) == 0:
        step = size // 2
        count = size
        while step >= 1:
            count //= 2
            upper = jnp.bitwise_and(me, step) != 0
            keep = lax.dynamic_slice_in_dim(value, jnp.where(upper, count, 0) * share, count * share, 0)
            send = lax.dynamic_slice_in_dim(value, jnp.where(upper, 0, count) * share, count * share, 0)
            value = keep + lax.ppermute(send, axis, [(i, i ^ step) for i in range(size)])
            step //= 2
        return value
    total = lax.dynamic_slice_in_dim(value, me * share, share, 0)
    for shift in range(1, size):
        piece = lax.dynamic_slice_in_dim(value, ((me + shift) % size) * share, share, 0)
        total = total + lax.ppermute(piece, axis, [(i, (i + shift) % size) for i in range(size)])
    return total


def butterfly_sum(value, axis):
    size = lax.axis_size(axis)
    if size & (size - 1):
        return lax.psum(value, axis)
    step = 1
    while step < size:
        value = value.astype(jnp.bfloat16)
        value = value.astype(jnp.float32) + lax.ppermute(
            value, axis, [(i, i ^ step) for i in range(size)]
        ).astype(jnp.float32)
        step *= 2
    return value


def block_weights(spec_real, spec_imag):
    upper_row = jnp.concatenate([spec_real, spec_imag], axis=2)
    lower_row = jnp.concatenate([-spec_imag, spec_real], axis=2)
    return jnp.concatenate([upper_row, lower_row], axis=1)


def spatial_rims(field_block, channels):
    x_wide = padded_2(field_block, (("gx", 2),), 2 * channels, True)
    inner = padded_2(x_wide, (("gy", 1),), 1, False)
    size = lax.axis_size("gz")
    up = [(i, i + 1) for i in range(size - 1)]
    down = [(j, i) for i, j in up]
    below = lax.ppermute(inner[-1:], "gz", up)
    above = lax.ppermute(inner[:1], "gz", down)
    return (inner, below, above)


def stencil_kernel(chunk, x_pad, y_cells, rows, plan, sources, has_acc, *refs):
    src_refs = refs[:sources]
    acc_refs = refs[sources : sources + has_acc]
    w_ref, o_ref = refs[sources + has_acc :]
    width = chunk + 2 * x_pad
    count = o_ref.shape[2] // chunk
    shift = chunk + x_pad - x_pad // 2
    side = (chunk + x_pad) // 128

    def body(index, carry):
        base = pl.multiple_of(index * chunk, chunk)
        for plane, terms in enumerate(plan):
            for row in range(0, y_cells, rows):
                left = jnp.zeros((rows, chunk + x_pad), jnp.float32)
                centre = jnp.zeros((rows, chunk), jnp.float32)
                right = jnp.zeros((rows, chunk + x_pad), jnp.float32)
                for source, source_plane, step_z in terms:
                    for step_y in range(3):
                        window = src_refs[source][
                            source_plane, pl.ds(row + step_y, rows), pl.ds(base, width)
                        ].astype(jnp.float32)
                        tap = 9 * step_z + 3 * step_y
                        gain_l = jnp.concatenate([w_ref[tap]] * side, axis=1)
                        gain_c = jnp.concatenate([w_ref[tap + 1]] * (side - 1), axis=1)
                        gain_r = jnp.concatenate([w_ref[tap + 2]] * side, axis=1)
                        left = left + window[:, : chunk + x_pad] * gain_l
                        centre = centre + window[:, x_pad : x_pad + chunk] * gain_c
                        right = right + window[:, x_pad:] * gain_r
                total = (
                    centre
                    + pltpu.roll(left, shift, 1)[:, :chunk]
                    + pltpu.roll(right, shift, 1)[:, :chunk]
                )
                for acc_ref in acc_refs:
                    total = total + acc_ref[plane, pl.ds(row, rows), pl.ds(base, chunk)]
                o_ref[plane, pl.ds(row, rows), pl.ds(base, chunk)] = total.astype(o_ref.dtype)
        return carry

    lax.fori_loop(0, count, body, 0)


def stencil_call(plan, inputs, accs, gains, y_cells, lanes, channels, out_dtype):
    chunk = min(1024, lanes)
    rows = 8 if y_cells % 8 == 0 else y_cells
    kernel = functools.partial(
        stencil_kernel, chunk, 2 * channels, y_cells, rows, plan, len(inputs), len(accs)
    )
    operands = list(inputs) + list(accs) + [gains]
    return pl.pallas_call(
        kernel,
        out_shape=jax.ShapeDtypeStruct((len(plan), y_cells, lanes), out_dtype),
    )(*operands)


def depthwise(rims, taps, flipped, x_cells, channels, out_dtype=jnp.float32, extra=()):
    inner, below, above = rims
    planes = inner.shape[0]
    y_cells = inner.shape[1] - 2
    lanes = x_cells * channels
    rows = 8 if y_cells % 8 == 0 else y_cells
    if flipped:
        taps = taps[::-1]
    gains = jnp.tile(taps.astype(jnp.float32), (1, 128 // channels))
    gains = jnp.broadcast_to(gains[:, None, :], (gains.shape[0], rows, 128))
    local_plan = tuple(
        tuple((0, plane + step_z - 1, step_z) for step_z in range(3) if 0 <= plane + step_z - 1 < planes)
        for plane in range(planes)
    )
    local = stencil_call(local_plan, (inner,), (), gains, y_cells, lanes, channels, jnp.float32)
    rim_plan = tuple(
        ((((0, 0, 0),) if plane == 0 else ()) + (((1, 0, 2),) if plane == planes - 1 else ()))
        for plane in range(planes)
    )
    accs = (local,) + tuple(extra)
    return stencil_call(rim_plan, (below, above), accs, gains, y_cells, lanes, channels, out_dtype)


def share_terms(field3, cos_table, sin_table):
    real_part = jnp.einsum("rxc,xk->krc", field3, cos_table, preferred_element_type=jnp.float32)
    imag_part = jnp.einsum("rxc,xk->krc", field3, sin_table, preferred_element_type=jnp.float32)
    return ring_reduce_scatter(jnp.concatenate([real_part, imag_part], axis=2), "gx")


def share_inverse(modes_share, cos_table, sin_table, channels):
    segment = ring_gather(modes_share, "gx")
    running = jnp.einsum(
        "krc,xk->rxc", segment[:, :, :channels], cos_table, preferred_element_type=jnp.float32
    )
    return running + jnp.einsum(
        "krc,xk->rxc", segment[:, :, channels:], sin_table, preferred_element_type=jnp.float32
    )


def split_gradients(dblock, channels):
    grad_real = dblock[:, :channels, :channels] + dblock[:, channels:, channels:]
    grad_imag = dblock[:, :channels, channels:] - dblock[:, channels:, :channels]
    return jnp.stack([grad_real, grad_imag])


def sum_gradients(local_grads):
    flat = local_grads.reshape(-1, 1024)
    return butterfly_sum(butterfly_sum(flat, "gy"), "gz").reshape(local_grads.shape)


def per_device(
    features, depth_weight, expand_weight, project_weight, spec_real, spec_imag, cotangent
):
    planes, y_cells, merged = features.shape
    channels = depth_weight.shape[1]
    x_cells = merged // channels
    row_count = planes * y_cells
    mode_count = spec_real.shape[0]
    group_size = lax.axis_size("gx")
    x_length = x_cells * group_size
    x_start = lax.axis_index("gx") * x_cells
    share_size = mode_count // group_size
    cos_part, sin_part = dft_tables(
        x_start, x_cells, x_length, jnp.arange(mode_count, dtype=jnp.int32)
    )
    order = gathered_order("gx", share_size)
    cos_order, sin_order = dft_tables(x_start, x_cells, x_length, order)
    cos_scaled = scaled_table(cos_order, order, x_length)
    sin_scaled = scaled_table(sin_order, order, x_length)
    cos_fwd_scaled = scaled_table(cos_part, jnp.arange(mode_count, dtype=jnp.int32), x_length)
    sin_fwd_scaled = scaled_table(sin_part, jnp.arange(mode_count, dtype=jnp.int32), x_length)
    blocks = block_weights(spec_real, spec_imag)
    padded = spatial_rims(features, channels)
    activation = depthwise(padded, depth_weight, False, x_cells, channels, jnp.bfloat16)
    field3 = features.reshape(row_count, x_cells, channels)
    owned_blocks = lax.dynamic_slice_in_dim(
        blocks, lax.axis_index("gx") * share_size, share_size, 0
    )
    coeffs = share_terms(field3, cos_part, sin_part).astype(jnp.bfloat16)
    mixed_modes = jnp.einsum(
        "krc,kco->kro", coeffs, owned_blocks, preferred_element_type=jnp.float32
    ).astype(jnp.bfloat16)
    mixed_modes, activation = lax.optimization_barrier((mixed_modes, activation))
    activation = activation.reshape(row_count * x_cells, channels)
    hidden_pre = jnp.dot(activation, expand_weight, preferred_element_type=jnp.float32)
    hidden, hidden_slope = gelu_parts(hidden_pre)
    local_branch = jnp.dot(
        hidden.astype(jnp.bfloat16), project_weight, preferred_element_type=jnp.float32
    )
    local_branch = local_branch.reshape(row_count, x_cells, channels)
    spectral = share_inverse(mixed_modes, cos_scaled, sin_scaled, channels)
    result, slopes = gelu_parts(local_branch + spectral)
    output = result.astype(jnp.bfloat16).reshape(planes, y_cells, merged)
    grad_pre = (
        lax.optimization_barrier(cotangent.reshape(row_count, x_cells, channels)).astype(jnp.float32)
        * slopes
    ).astype(jnp.bfloat16)
    hidden_grad = jnp.dot(
        grad_pre.reshape(row_count * x_cells, channels),
        project_weight.T,
        preferred_element_type=jnp.float32,
    )
    grad_hidden = (hidden_grad * hidden_slope).astype(jnp.bfloat16)
    grad_act = jnp.dot(grad_hidden, expand_weight.T, preferred_element_type=jnp.float32).astype(
        jnp.bfloat16
    )
    grad_act = grad_act.reshape(planes, y_cells, merged)
    dcoef = share_terms(grad_pre, cos_fwd_scaled, sin_fwd_scaled).astype(jnp.bfloat16)
    dmode = jnp.einsum(
        "kro,kco->krc", dcoef, owned_blocks, preferred_element_type=jnp.float32
    ).astype(jnp.bfloat16)
    dblock = jnp.einsum("krc,kro->kco", coeffs, dcoef, preferred_element_type=jnp.float32)
    local_grads = split_gradients(dblock, channels)
    dmode, local_grads, grad_act = lax.optimization_barrier((dmode, local_grads, grad_act))
    spectral_grad = share_inverse(dmode, cos_order, sin_order, channels)
    grad_spec = sum_gradients(local_grads)
    padded_grad = spatial_rims(grad_act, channels)
    grad_features = depthwise(
        padded_grad,
        depth_weight,
        True,
        x_cells,
        channels,
        jnp.bfloat16,
        (spectral_grad.reshape(planes, y_cells, merged),),
    )
    return (output, grad_features, grad_spec)


def solution(mesh):
    placed = (P("gz", "gy", "gx"), P(), P(), P(), P(), P(), P("gz", "gy", "gx"))
    return jax.shard_map(
        per_device,
        mesh=mesh,
        in_specs=placed,
        out_specs=(P("gz", "gy", "gx"), P("gz", "gy", "gx"), P(None, "gx", None, None)),
        check_vma=False,
    )
```

```python
import functools
import math

import jax
import jax.numpy as jnp
from jax import lax
from jax.experimental import pallas as pl
from jax.experimental.pallas import tpu as pltpu
from jax.sharding import PartitionSpec as P


def padded_2(value, sides, width, wrap):
    for axis, dim in sides:
        size, length = (lax.axis_size(axis), value.shape[dim])
        last = lax.slice_in_dim(value, length - width, length, axis=dim)
        leading = lax.slice_in_dim(value, 0, width, axis=dim)
        if size == 2 and not wrap:
            first = lax.axis_index(axis) == 0
            swapped = lax.ppermute(jnp.where(first, last, leading), axis, [(0, 1), (1, 0)])
            zeros = jnp.zeros_like(swapped)
            before = jnp.where(first, zeros, swapped)
            after = jnp.where(first, swapped, zeros)
        else:
            up = [(i, (i + 1) % size) for i in range(size if wrap else size - 1)]
            down = [(j, i) for i, j in up]
            before = lax.ppermute(last, axis, up)
            after = lax.ppermute(leading, axis, down)
        value = jnp.concatenate([before, value, after], axis=dim)
    return value


def gelu_parts(values):
    normal_cdf = 0.5 * (1.0 + jax.scipy.special.erf(values * (1.0 / math.sqrt(2.0))))
    density = jnp.exp(-0.5 * values * values) * (1.0 / math.sqrt(2.0 * math.pi))
    return (values * normal_cdf, normal_cdf + values * density)


def dft_tables(offset, cells, x_length, frequency):
    position = offset + jnp.arange(cells, dtype=jnp.int32)
    phase_int = position[:, None] * frequency[None, :] % x_length
    angles = phase_int.astype(jnp.float32) * (2.0 * math.pi / x_length)
    return (jnp.cos(angles).astype(jnp.bfloat16), (-jnp.sin(angles)).astype(jnp.bfloat16))


def scaled_table(table, frequency, x_length):
    mode_scale = jnp.where(frequency == 0, 1.0, 2.0).astype(jnp.float32) / x_length
    return (table.astype(jnp.float32) * mode_scale[None, :]).astype(jnp.bfloat16)


def gathered_order(axis, share_size):
    size = lax.axis_size(axis)
    shifts = jnp.arange(size, dtype=jnp.int32)
    me = lax.axis_index(axis)
    if size & (size - 1):
        sources = (me - shifts) % size
    else:
        sources = jnp.bitwise_xor(me, shifts)
    local = jnp.arange(share_size, dtype=jnp.int32)
    return (sources[:, None] * share_size + local[None, :]).reshape(-1)


def ring_gather(block, axis):
    size = lax.axis_size(axis)
    if size & (size - 1) == 0:
        step = 1
        while step < size:
            block = jnp.concatenate(
                [block, lax.ppermute(block, axis, [(i, i ^ step) for i in range(size)])], axis=0
            )
            step *= 2
        return block
    pieces = [block]
    for shift in range(1, size):
        pieces.append(lax.ppermute(block, axis, [(i, (i + shift) % size) for i in range(size)]))
    return jnp.concatenate(pieces, axis=0)


def ring_reduce_scatter(value, axis):
    size = lax.axis_size(axis)
    share = value.shape[0] // size
    me = lax.axis_index(axis)
    if size & (size - 1) == 0:
        step = size // 2
        count = size
        while step >= 1:
            count //= 2
            upper = jnp.bitwise_and(me, step) != 0
            keep = lax.dynamic_slice_in_dim(value, jnp.where(upper, count, 0) * share, count * share, 0)
            send = lax.dynamic_slice_in_dim(value, jnp.where(upper, 0, count) * share, count * share, 0)
            value = keep + lax.ppermute(send, axis, [(i, i ^ step) for i in range(size)])
            step //= 2
        return value
    total = lax.dynamic_slice_in_dim(value, me * share, share, 0)
    for shift in range(1, size):
        piece = lax.dynamic_slice_in_dim(value, ((me + shift) % size) * share, share, 0)
        total = total + lax.ppermute(piece, axis, [(i, (i + shift) % size) for i in range(size)])
    return total


def butterfly_sum(value, axis):
    size = lax.axis_size(axis)
    if size & (size - 1):
        return lax.psum(value, axis)
    step = 1
    while step < size:
        value = value.astype(jnp.bfloat16)
        value = value.astype(jnp.float32) + lax.ppermute(
            value, axis, [(i, i ^ step) for i in range(size)]
        ).astype(jnp.float32)
        step *= 2
    return value


def block_weights(spec_real, spec_imag):
    upper_row = jnp.concatenate([spec_real, spec_imag], axis=2)
    lower_row = jnp.concatenate([-spec_imag, spec_real], axis=2)
    return jnp.concatenate([upper_row, lower_row], axis=1)


def spatial_rims(field_block, channels):
    x_wide = padded_2(field_block, (("gx", 2),), 2 * channels, True)
    inner = padded_2(x_wide, (("gy", 1),), 1, False)
    size = lax.axis_size("gz")
    up = [(i, i + 1) for i in range(size - 1)]
    down = [(j, i) for i, j in up]
    below = lax.ppermute(inner[-1:], "gz", up)
    above = lax.ppermute(inner[:1], "gz", down)
    return (inner, below, above)


def stencil_kernel(chunk, x_pad, y_cells, rows, plan, sources, has_acc, *refs):
    src_refs = refs[:sources]
    acc_refs = refs[sources : sources + has_acc]
    w_ref, o_ref = refs[sources + has_acc :]
    width = chunk + 2 * x_pad
    count = o_ref.shape[2] // chunk
    shift = chunk + x_pad - x_pad // 2
    side = (chunk + x_pad) // 128

    def body(index, carry):
        base = pl.multiple_of(index * chunk, chunk)
        for plane, terms in enumerate(plan):
            for row in range(0, y_cells, rows):
                left = jnp.zeros((rows, chunk + x_pad), jnp.float32)
                centre = jnp.zeros((rows, chunk), jnp.float32)
                right = jnp.zeros((rows, chunk + x_pad), jnp.float32)
                for source, source_plane, step_z in terms:
                    for step_y in range(3):
                        window = src_refs[source][
                            source_plane, pl.ds(row + step_y, rows), pl.ds(base, width)
                        ].astype(jnp.float32)
                        tap = 9 * step_z + 3 * step_y
                        gain_l = jnp.concatenate([w_ref[tap]] * side, axis=1)
                        gain_c = jnp.concatenate([w_ref[tap + 1]] * (side - 1), axis=1)
                        gain_r = jnp.concatenate([w_ref[tap + 2]] * side, axis=1)
                        left = left + window[:, : chunk + x_pad] * gain_l
                        centre = centre + window[:, x_pad : x_pad + chunk] * gain_c
                        right = right + window[:, x_pad:] * gain_r
                total = (
                    centre
                    + pltpu.roll(left, shift, 1)[:, :chunk]
                    + pltpu.roll(right, shift, 1)[:, :chunk]
                )
                for acc_ref in acc_refs:
                    total = total + acc_ref[plane, pl.ds(row, rows), pl.ds(base, chunk)].astype(
                        jnp.float32
                    )
                o_ref[plane, pl.ds(row, rows), pl.ds(base, chunk)] = total.astype(o_ref.dtype)
        return carry

    lax.fori_loop(0, count, body, 0)


def stencil_call(plan, inputs, accs, gains, y_cells, lanes, channels, out_dtype):
    chunk = min(1024, lanes)
    rows = 8 if y_cells % 8 == 0 else y_cells
    kernel = functools.partial(
        stencil_kernel, chunk, 2 * channels, y_cells, rows, plan, len(inputs), len(accs)
    )
    operands = list(inputs) + list(accs) + [gains]
    return pl.pallas_call(
        kernel,
        out_shape=jax.ShapeDtypeStruct((len(plan), y_cells, lanes), out_dtype),
    )(*operands)


def depthwise(rims, taps, flipped, x_cells, channels, out_dtype=jnp.float32, extra=()):
    inner, below, above = rims
    planes = inner.shape[0]
    y_cells = inner.shape[1] - 2
    lanes = x_cells * channels
    rows = 8 if y_cells % 8 == 0 else y_cells
    if flipped:
        taps = taps[::-1]
    gains = jnp.tile(taps.astype(jnp.float32), (1, 128 // channels))
    gains = jnp.broadcast_to(gains[:, None, :], (gains.shape[0], rows, 128))
    local_plan = tuple(
        tuple((0, plane + step_z - 1, step_z) for step_z in range(3) if 0 <= plane + step_z - 1 < planes)
        for plane in range(planes)
    )
    local = stencil_call(local_plan, (inner,), (), gains, y_cells, lanes, channels, jnp.float32)
    rim_plan = tuple(
        ((((0, 0, 0),) if plane == 0 else ()) + (((1, 0, 2),) if plane == planes - 1 else ()))
        for plane in range(planes)
    )
    accs = (local,) + tuple(extra)
    return stencil_call(rim_plan, (below, above), accs, gains, y_cells, lanes, channels, out_dtype)


def share_terms(field3, cos_table, sin_table):
    real_part = jnp.einsum("rxc,xk->krc", field3, cos_table, preferred_element_type=jnp.float32)
    imag_part = jnp.einsum("rxc,xk->krc", field3, sin_table, preferred_element_type=jnp.float32)
    return ring_reduce_scatter(jnp.concatenate([real_part, imag_part], axis=2), "gx")


def share_inverse(modes_share, cos_table, sin_table, channels):
    segment = ring_gather(modes_share, "gx")
    running = jnp.einsum(
        "krc,xk->rxc", segment[:, :, :channels], cos_table, preferred_element_type=jnp.float32
    )
    return running + jnp.einsum(
        "krc,xk->rxc", segment[:, :, channels:], sin_table, preferred_element_type=jnp.float32
    )


def split_gradients(dblock, channels):
    grad_real = dblock[:, :channels, :channels] + dblock[:, channels:, channels:]
    grad_imag = dblock[:, :channels, channels:] - dblock[:, channels:, :channels]
    return jnp.stack([grad_real, grad_imag])


def sum_gradients(local_grads):
    flat = local_grads.reshape(-1, 1024)
    return butterfly_sum(butterfly_sum(flat, "gy"), "gz").reshape(local_grads.shape)


def per_device(
    features, depth_weight, expand_weight, project_weight, spec_real, spec_imag, cotangent
):
    planes, y_cells, merged = features.shape
    channels = depth_weight.shape[1]
    x_cells = merged // channels
    row_count = planes * y_cells
    mode_count = spec_real.shape[0]
    group_size = lax.axis_size("gx")
    x_length = x_cells * group_size
    x_start = lax.axis_index("gx") * x_cells
    share_size = mode_count // group_size
    cos_part, sin_part = dft_tables(
        x_start, x_cells, x_length, jnp.arange(mode_count, dtype=jnp.int32)
    )
    order = gathered_order("gx", share_size)
    cos_order, sin_order = dft_tables(x_start, x_cells, x_length, order)
    cos_scaled = scaled_table(cos_order, order, x_length)
    sin_scaled = scaled_table(sin_order, order, x_length)
    cos_fwd_scaled = scaled_table(cos_part, jnp.arange(mode_count, dtype=jnp.int32), x_length)
    sin_fwd_scaled = scaled_table(sin_part, jnp.arange(mode_count, dtype=jnp.int32), x_length)
    blocks = block_weights(spec_real, spec_imag)
    padded = spatial_rims(features, channels)
    activation = depthwise(padded, depth_weight, False, x_cells, channels, jnp.bfloat16)
    field3 = features.reshape(row_count, x_cells, channels)
    owned_blocks = lax.dynamic_slice_in_dim(
        blocks, lax.axis_index("gx") * share_size, share_size, 0
    )
    coeffs = share_terms(field3, cos_part, sin_part).astype(jnp.bfloat16)
    mixed_modes = jnp.einsum(
        "krc,kco->kro", coeffs, owned_blocks, preferred_element_type=jnp.float32
    ).astype(jnp.bfloat16)
    mixed_modes, activation = lax.optimization_barrier((mixed_modes, activation))
    activation = activation.reshape(row_count * x_cells, channels)
    hidden_pre = jnp.dot(activation, expand_weight, preferred_element_type=jnp.float32)
    hidden, hidden_slope = gelu_parts(hidden_pre)
    local_branch = jnp.dot(
        hidden.astype(jnp.bfloat16), project_weight, preferred_element_type=jnp.float32
    )
    local_branch = local_branch.reshape(row_count, x_cells, channels)
    spectral = share_inverse(mixed_modes, cos_scaled, sin_scaled, channels)
    result, slopes = gelu_parts(local_branch + spectral)
    output = result.astype(jnp.bfloat16).reshape(planes, y_cells, merged)
    grad_pre = (
        lax.optimization_barrier(cotangent.reshape(row_count, x_cells, channels)).astype(jnp.float32)
        * slopes
    ).astype(jnp.bfloat16)
    hidden_grad = jnp.dot(
        grad_pre.reshape(row_count * x_cells, channels),
        project_weight.T,
        preferred_element_type=jnp.float32,
    )
    grad_hidden = (hidden_grad * hidden_slope).astype(jnp.bfloat16)
    grad_act = jnp.dot(grad_hidden, expand_weight.T, preferred_element_type=jnp.float32).astype(
        jnp.bfloat16
    )
    grad_act = grad_act.reshape(planes, y_cells, merged)
    dcoef = share_terms(grad_pre, cos_fwd_scaled, sin_fwd_scaled).astype(jnp.bfloat16)
    dmode = jnp.einsum(
        "kro,kco->krc", dcoef, owned_blocks, preferred_element_type=jnp.float32
    ).astype(jnp.bfloat16)
    dblock = jnp.einsum("krc,kro->kco", coeffs, dcoef, preferred_element_type=jnp.float32)
    local_grads = split_gradients(dblock, channels)
    dmode, local_grads, grad_act = lax.optimization_barrier((dmode, local_grads, grad_act))
    spectral_grad = share_inverse(dmode, cos_order, sin_order, channels)
    grad_spec = sum_gradients(local_grads)
    padded_grad = spatial_rims(grad_act, channels)
    grad_features = depthwise(
        padded_grad,
        depth_weight,
        True,
        x_cells,
        channels,
        jnp.bfloat16,
        (spectral_grad.astype(jnp.bfloat16).reshape(planes, y_cells, merged),),
    )
    return (output, grad_features, grad_spec)


def solution(mesh):
    placed = (P("gz", "gy", "gx"), P(), P(), P(), P(), P(), P("gz", "gy", "gx"))
    return jax.shard_map(
        per_device,
        mesh=mesh,
        in_specs=placed,
        out_specs=(P("gz", "gy", "gx"), P("gz", "gy", "gx"), P(None, "gx", None, None)),
        check_vma=False,
    )
```

```python
import functools
import math

import jax
import jax.numpy as jnp
from jax import lax
from jax.experimental import pallas as pl
from jax.experimental.pallas import tpu as pltpu
from jax.sharding import PartitionSpec as P


def padded_2(value, sides, width, wrap):
    for axis, dim in sides:
        size, length = (lax.axis_size(axis), value.shape[dim])
        last = lax.slice_in_dim(value, length - width, length, axis=dim)
        leading = lax.slice_in_dim(value, 0, width, axis=dim)
        if size == 2 and not wrap:
            first = lax.axis_index(axis) == 0
            swapped = lax.ppermute(jnp.where(first, last, leading), axis, [(0, 1), (1, 0)])
            zeros = jnp.zeros_like(swapped)
            before = jnp.where(first, zeros, swapped)
            after = jnp.where(first, swapped, zeros)
        else:
            up = [(i, (i + 1) % size) for i in range(size if wrap else size - 1)]
            down = [(j, i) for i, j in up]
            before = lax.ppermute(last, axis, up)
            after = lax.ppermute(leading, axis, down)
        value = jnp.concatenate([before, value, after], axis=dim)
    return value


def gelu_parts(values):
    normal_cdf = 0.5 * (1.0 + jax.scipy.special.erf(values * (1.0 / math.sqrt(2.0))))
    density = jnp.exp(-0.5 * values * values) * (1.0 / math.sqrt(2.0 * math.pi))
    return (values * normal_cdf, normal_cdf + values * density)


def dft_tables(offset, cells, x_length, frequency):
    position = offset + jnp.arange(cells, dtype=jnp.int32)
    phase_int = position[:, None] * frequency[None, :] % x_length
    angles = phase_int.astype(jnp.float32) * (2.0 * math.pi / x_length)
    return (jnp.cos(angles).astype(jnp.bfloat16), (-jnp.sin(angles)).astype(jnp.bfloat16))


def scaled_table(table, frequency, x_length):
    mode_scale = jnp.where(frequency == 0, 1.0, 2.0).astype(jnp.float32) / x_length
    return (table.astype(jnp.float32) * mode_scale[None, :]).astype(jnp.bfloat16)


def gathered_order(axis, share_size):
    size = lax.axis_size(axis)
    shifts = jnp.arange(size, dtype=jnp.int32)
    me = lax.axis_index(axis)
    if size & (size - 1):
        sources = (me - shifts) % size
    else:
        sources = jnp.bitwise_xor(me, shifts)
    local = jnp.arange(share_size, dtype=jnp.int32)
    return (sources[:, None] * share_size + local[None, :]).reshape(-1)


def ring_gather(block, axis):
    size = lax.axis_size(axis)
    if size & (size - 1) == 0:
        step = 1
        while step < size:
            block = jnp.concatenate(
                [block, lax.ppermute(block, axis, [(i, i ^ step) for i in range(size)])], axis=0
            )
            step *= 2
        return block
    pieces = [block]
    for shift in range(1, size):
        pieces.append(lax.ppermute(block, axis, [(i, (i + shift) % size) for i in range(size)]))
    return jnp.concatenate(pieces, axis=0)


def ring_reduce_scatter(value, axis):
    size = lax.axis_size(axis)
    share = value.shape[0] // size
    me = lax.axis_index(axis)
    if size & (size - 1) == 0:
        step = size // 2
        count = size
        while step >= 1:
            count //= 2
            upper = jnp.bitwise_and(me, step) != 0
            keep = lax.dynamic_slice_in_dim(value, jnp.where(upper, count, 0) * share, count * share, 0)
            send = lax.dynamic_slice_in_dim(value, jnp.where(upper, 0, count) * share, count * share, 0)
            value = keep + lax.ppermute(send, axis, [(i, i ^ step) for i in range(size)])
            step //= 2
        return value
    total = lax.dynamic_slice_in_dim(value, me * share, share, 0)
    for shift in range(1, size):
        piece = lax.dynamic_slice_in_dim(value, ((me + shift) % size) * share, share, 0)
        total = total + lax.ppermute(piece, axis, [(i, (i + shift) % size) for i in range(size)])
    return total


def butterfly_sum(value, axis):
    size = lax.axis_size(axis)
    if size & (size - 1):
        return lax.psum(value, axis)
    step = 1
    while step < size:
        value = value.astype(jnp.bfloat16)
        value = value.astype(jnp.float32) + lax.ppermute(
            value, axis, [(i, i ^ step) for i in range(size)]
        ).astype(jnp.float32)
        step *= 2
    return value


def block_weights(spec_real, spec_imag):
    upper_row = jnp.concatenate([spec_real, spec_imag], axis=2)
    lower_row = jnp.concatenate([-spec_imag, spec_real], axis=2)
    return jnp.concatenate([upper_row, lower_row], axis=1)


def spatial_rims(field_block, channels):
    x_wide = padded_2(field_block, (("gx", 2),), 2 * channels, True)
    inner = padded_2(x_wide, (("gy", 1),), 1, False)
    size = lax.axis_size("gz")
    up = [(i, i + 1) for i in range(size - 1)]
    down = [(j, i) for i, j in up]
    below = lax.ppermute(inner[-1:], "gz", up)
    above = lax.ppermute(inner[:1], "gz", down)
    return (inner, below, above)


def stencil_kernel(chunk, x_pad, y_cells, rows, plan, sources, has_acc, *refs):
    src_refs = refs[:sources]
    acc_refs = refs[sources : sources + has_acc]
    w_ref, o_ref = refs[sources + has_acc :]
    width = chunk + 2 * x_pad
    count = o_ref.shape[2] // chunk
    shift = chunk + x_pad - x_pad // 2
    side = (chunk + x_pad) // 128

    def body(index, carry):
        base = pl.multiple_of(index * chunk, chunk)
        for plane, terms in enumerate(plan):
            for row in range(0, y_cells, rows):
                left = jnp.zeros((rows, chunk + x_pad), jnp.float32)
                centre = jnp.zeros((rows, chunk), jnp.float32)
                right = jnp.zeros((rows, chunk + x_pad), jnp.float32)
                for source, source_plane, step_z in terms:
                    for step_y in range(3):
                        window = src_refs[source][
                            source_plane, pl.ds(row + step_y, rows), pl.ds(base, width)
                        ].astype(jnp.float32)
                        tap = 9 * step_z + 3 * step_y
                        gain_l = jnp.concatenate([w_ref[tap]] * side, axis=1)
                        gain_c = jnp.concatenate([w_ref[tap + 1]] * (side - 1), axis=1)
                        gain_r = jnp.concatenate([w_ref[tap + 2]] * side, axis=1)
                        left = left + window[:, : chunk + x_pad] * gain_l
                        centre = centre + window[:, x_pad : x_pad + chunk] * gain_c
                        right = right + window[:, x_pad:] * gain_r
                total = (
                    centre
                    + pltpu.roll(left, shift, 1)[:, :chunk]
                    + pltpu.roll(right, shift, 1)[:, :chunk]
                )
                for acc_ref in acc_refs:
                    total = total + acc_ref[plane, pl.ds(row, rows), pl.ds(base, chunk)].astype(
                        jnp.float32
                    )
                o_ref[plane, pl.ds(row, rows), pl.ds(base, chunk)] = total.astype(o_ref.dtype)
        return carry

    lax.fori_loop(0, count, body, 0)


def stencil_call(plan, inputs, accs, gains, y_cells, lanes, channels, out_dtype):
    chunk = min(1024, lanes)
    rows = 8 if y_cells % 8 == 0 else y_cells
    kernel = functools.partial(
        stencil_kernel, chunk, 2 * channels, y_cells, rows, plan, len(inputs), len(accs)
    )
    operands = list(inputs) + list(accs) + [gains]
    return pl.pallas_call(
        kernel,
        out_shape=jax.ShapeDtypeStruct((len(plan), y_cells, lanes), out_dtype),
    )(*operands)


def depthwise(rims, taps, flipped, x_cells, channels, out_dtype=jnp.float32, extra=()):
    inner, below, above = rims
    planes = inner.shape[0]
    y_cells = inner.shape[1] - 2
    lanes = x_cells * channels
    rows = 8 if y_cells % 8 == 0 else y_cells
    if flipped:
        taps = taps[::-1]
    gains = jnp.tile(taps.astype(jnp.float32), (1, 128 // channels))
    gains = jnp.broadcast_to(gains[:, None, :], (gains.shape[0], rows, 128))
    local_plan = tuple(
        tuple((0, plane + step_z - 1, step_z) for step_z in range(3) if 0 <= plane + step_z - 1 < planes)
        for plane in range(planes)
    )
    local = stencil_call(local_plan, (inner,), (), gains, y_cells, lanes, channels, jnp.bfloat16)
    rim_plan = tuple(
        ((((0, 0, 0),) if plane == 0 else ()) + (((1, 0, 2),) if plane == planes - 1 else ()))
        for plane in range(planes)
    )
    accs = (local,) + tuple(extra)
    return stencil_call(rim_plan, (below, above), accs, gains, y_cells, lanes, channels, out_dtype)


def share_terms(field3, cos_table, sin_table):
    real_part = jnp.einsum("rxc,xk->krc", field3, cos_table, preferred_element_type=jnp.float32)
    imag_part = jnp.einsum("rxc,xk->krc", field3, sin_table, preferred_element_type=jnp.float32)
    return ring_reduce_scatter(jnp.concatenate([real_part, imag_part], axis=2), "gx")


def share_inverse(modes_share, cos_table, sin_table, channels):
    segment = ring_gather(modes_share, "gx")
    running = jnp.einsum(
        "krc,xk->rxc", segment[:, :, :channels], cos_table, preferred_element_type=jnp.float32
    )
    return running + jnp.einsum(
        "krc,xk->rxc", segment[:, :, channels:], sin_table, preferred_element_type=jnp.float32
    )


def split_gradients(dblock, channels):
    grad_real = dblock[:, :channels, :channels] + dblock[:, channels:, channels:]
    grad_imag = dblock[:, :channels, channels:] - dblock[:, channels:, :channels]
    return jnp.stack([grad_real, grad_imag])


def sum_gradients(local_grads):
    flat = local_grads.reshape(-1, 1024)
    return butterfly_sum(butterfly_sum(flat, "gy"), "gz").reshape(local_grads.shape)


def per_device(
    features, depth_weight, expand_weight, project_weight, spec_real, spec_imag, cotangent
):
    planes, y_cells, merged = features.shape
    channels = depth_weight.shape[1]
    x_cells = merged // channels
    row_count = planes * y_cells
    mode_count = spec_real.shape[0]
    group_size = lax.axis_size("gx")
    x_length = x_cells * group_size
    x_start = lax.axis_index("gx") * x_cells
    share_size = mode_count // group_size
    cos_part, sin_part = dft_tables(
        x_start, x_cells, x_length, jnp.arange(mode_count, dtype=jnp.int32)
    )
    order = gathered_order("gx", share_size)
    cos_order, sin_order = dft_tables(x_start, x_cells, x_length, order)
    cos_scaled = scaled_table(cos_order, order, x_length)
    sin_scaled = scaled_table(sin_order, order, x_length)
    cos_fwd_scaled = scaled_table(cos_part, jnp.arange(mode_count, dtype=jnp.int32), x_length)
    sin_fwd_scaled = scaled_table(sin_part, jnp.arange(mode_count, dtype=jnp.int32), x_length)
    blocks = block_weights(spec_real, spec_imag)
    padded = spatial_rims(features, channels)
    activation = depthwise(padded, depth_weight, False, x_cells, channels, jnp.bfloat16)
    field3 = features.reshape(row_count, x_cells, channels)
    owned_blocks = lax.dynamic_slice_in_dim(
        blocks, lax.axis_index("gx") * share_size, share_size, 0
    )
    coeffs = share_terms(field3, cos_part, sin_part).astype(jnp.bfloat16)
    mixed_modes = jnp.einsum(
        "krc,kco->kro", coeffs, owned_blocks, preferred_element_type=jnp.float32
    ).astype(jnp.bfloat16)
    mixed_modes, activation = lax.optimization_barrier((mixed_modes, activation))
    activation = activation.reshape(row_count * x_cells, channels)
    hidden_pre = jnp.dot(activation, expand_weight, preferred_element_type=jnp.float32)
    hidden, hidden_slope = gelu_parts(hidden_pre)
    local_branch = jnp.dot(
        hidden.astype(jnp.bfloat16), project_weight, preferred_element_type=jnp.float32
    )
    local_branch = local_branch.reshape(row_count, x_cells, channels)
    spectral = share_inverse(mixed_modes, cos_scaled, sin_scaled, channels)
    result, slopes = gelu_parts(local_branch + spectral)
    output = result.astype(jnp.bfloat16).reshape(planes, y_cells, merged)
    grad_pre = (
        lax.optimization_barrier(cotangent.reshape(row_count, x_cells, channels)).astype(jnp.float32)
        * slopes
    ).astype(jnp.bfloat16)
    hidden_grad = jnp.dot(
        grad_pre.reshape(row_count * x_cells, channels),
        project_weight.T,
        preferred_element_type=jnp.float32,
    )
    grad_hidden = (hidden_grad * hidden_slope).astype(jnp.bfloat16)
    grad_act = jnp.dot(grad_hidden, expand_weight.T, preferred_element_type=jnp.float32).astype(
        jnp.bfloat16
    )
    grad_act = grad_act.reshape(planes, y_cells, merged)
    dcoef = share_terms(grad_pre, cos_fwd_scaled, sin_fwd_scaled).astype(jnp.bfloat16)
    dmode = jnp.einsum(
        "kro,kco->krc", dcoef, owned_blocks, preferred_element_type=jnp.float32
    ).astype(jnp.bfloat16)
    dblock = jnp.einsum("krc,kro->kco", coeffs, dcoef, preferred_element_type=jnp.float32)
    local_grads = split_gradients(dblock, channels)
    dmode, local_grads, grad_act = lax.optimization_barrier((dmode, local_grads, grad_act))
    spectral_grad = share_inverse(dmode, cos_order, sin_order, channels)
    grad_spec = sum_gradients(local_grads)
    padded_grad = spatial_rims(grad_act, channels)
    grad_features = depthwise(
        padded_grad,
        depth_weight,
        True,
        x_cells,
        channels,
        jnp.bfloat16,
        (spectral_grad.astype(jnp.bfloat16).reshape(planes, y_cells, merged),),
    )
    return (output, grad_features, grad_spec)


def solution(mesh):
    placed = (P("gz", "gy", "gx"), P(), P(), P(), P(), P(), P("gz", "gy", "gx"))
    return jax.shard_map(
        per_device,
        mesh=mesh,
        in_specs=placed,
        out_specs=(P("gz", "gy", "gx"), P("gz", "gy", "gx"), P(None, "gx", None, None)),
        check_vma=False,
    )
```

```python
import functools
import math

import jax
import jax.numpy as jnp
from jax import lax
from jax.experimental import pallas as pl
from jax.experimental.pallas import tpu as pltpu
from jax.sharding import PartitionSpec as P


def padded_2(value, sides, width, wrap):
    for axis, dim in sides:
        size, length = (lax.axis_size(axis), value.shape[dim])
        last = lax.slice_in_dim(value, length - width, length, axis=dim)
        leading = lax.slice_in_dim(value, 0, width, axis=dim)
        if size == 2 and not wrap:
            first = lax.axis_index(axis) == 0
            swapped = lax.ppermute(jnp.where(first, last, leading), axis, [(0, 1), (1, 0)])
            zeros = jnp.zeros_like(swapped)
            before = jnp.where(first, zeros, swapped)
            after = jnp.where(first, swapped, zeros)
        else:
            up = [(i, (i + 1) % size) for i in range(size if wrap else size - 1)]
            down = [(j, i) for i, j in up]
            before = lax.ppermute(last, axis, up)
            after = lax.ppermute(leading, axis, down)
        value = jnp.concatenate([before, value, after], axis=dim)
    return value


def gelu_parts(values):
    normal_cdf = 0.5 * (1.0 + jax.scipy.special.erf(values * (1.0 / math.sqrt(2.0))))
    density = jnp.exp(-0.5 * values * values) * (1.0 / math.sqrt(2.0 * math.pi))
    return (values * normal_cdf, normal_cdf + values * density)


def dft_tables(offset, cells, x_length, frequency):
    position = offset + jnp.arange(cells, dtype=jnp.int32)
    phase_int = position[:, None] * frequency[None, :] % x_length
    angles = phase_int.astype(jnp.float32) * (2.0 * math.pi / x_length)
    return (jnp.cos(angles).astype(jnp.bfloat16), (-jnp.sin(angles)).astype(jnp.bfloat16))


def scaled_table(table, frequency, x_length):
    mode_scale = jnp.where(frequency == 0, 1.0, 2.0).astype(jnp.float32) / x_length
    return (table.astype(jnp.float32) * mode_scale[None, :]).astype(jnp.bfloat16)


def gathered_order(axis, share_size):
    size = lax.axis_size(axis)
    shifts = jnp.arange(size, dtype=jnp.int32)
    me = lax.axis_index(axis)
    if size & (size - 1):
        sources = (me - shifts) % size
    else:
        sources = jnp.bitwise_xor(me, shifts)
    local = jnp.arange(share_size, dtype=jnp.int32)
    return (sources[:, None] * share_size + local[None, :]).reshape(-1)


def ring_gather(block, axis):
    size = lax.axis_size(axis)
    if size & (size - 1) == 0:
        step = 1
        while step < size:
            block = jnp.concatenate(
                [block, lax.ppermute(block, axis, [(i, i ^ step) for i in range(size)])], axis=0
            )
            step *= 2
        return block
    pieces = [block]
    for shift in range(1, size):
        pieces.append(lax.ppermute(block, axis, [(i, (i + shift) % size) for i in range(size)]))
    return jnp.concatenate(pieces, axis=0)


def ring_reduce_scatter(value, axis):
    size = lax.axis_size(axis)
    share = value.shape[0] // size
    me = lax.axis_index(axis)
    if size & (size - 1) == 0:
        step = size // 2
        count = size
        while step >= 1:
            count //= 2
            upper = jnp.bitwise_and(me, step) != 0
            keep = lax.dynamic_slice_in_dim(value, jnp.where(upper, count, 0) * share, count * share, 0)
            send = lax.dynamic_slice_in_dim(value, jnp.where(upper, 0, count) * share, count * share, 0)
            value = keep + lax.ppermute(send, axis, [(i, i ^ step) for i in range(size)])
            step //= 2
        return value
    total = lax.dynamic_slice_in_dim(value, me * share, share, 0)
    for shift in range(1, size):
        piece = lax.dynamic_slice_in_dim(value, ((me + shift) % size) * share, share, 0)
        total = total + lax.ppermute(piece, axis, [(i, (i + shift) % size) for i in range(size)])
    return total


def butterfly_sum(value, axis):
    size = lax.axis_size(axis)
    if size & (size - 1):
        return lax.psum(value, axis)
    step = 1
    while step < size:
        value = value.astype(jnp.bfloat16)
        value = value.astype(jnp.float32) + lax.ppermute(
            value, axis, [(i, i ^ step) for i in range(size)]
        ).astype(jnp.float32)
        step *= 2
    return value


def block_weights(spec_real, spec_imag):
    upper_row = jnp.concatenate([spec_real, spec_imag], axis=2)
    lower_row = jnp.concatenate([-spec_imag, spec_real], axis=2)
    return jnp.concatenate([upper_row, lower_row], axis=1)


def spatial_rims(field_block, channels):
    x_wide = padded_2(field_block, (("gx", 2),), 2 * channels, True)
    inner = padded_2(x_wide, (("gy", 1),), 1, False)
    size = lax.axis_size("gz")
    up = [(i, i + 1) for i in range(size - 1)]
    down = [(j, i) for i, j in up]
    below = lax.ppermute(inner[-1:], "gz", up)
    above = lax.ppermute(inner[:1], "gz", down)
    return (inner, below, above)


def stencil_kernel(chunk, x_pad, y_cells, rows, plan, sources, has_acc, *refs):
    src_refs = refs[:sources]
    acc_refs = refs[sources : sources + has_acc]
    w_ref, o_ref = refs[sources + has_acc :]
    width = chunk + 2 * x_pad
    count = o_ref.shape[2] // chunk
    shift = chunk + x_pad - x_pad // 2
    side = (chunk + x_pad) // 128

    def body(index, carry):
        base = pl.multiple_of(index * chunk, chunk)
        for plane, terms in enumerate(plan):
            for row in range(0, y_cells, rows):
                left = jnp.zeros((rows, chunk + x_pad), jnp.float32)
                centre = jnp.zeros((rows, chunk), jnp.float32)
                right = jnp.zeros((rows, chunk + x_pad), jnp.float32)
                for source, source_plane, step_z in terms:
                    for step_y in range(3):
                        window = src_refs[source][
                            source_plane, pl.ds(row + step_y, rows), pl.ds(base, width)
                        ].astype(jnp.float32)
                        tap = 9 * step_z + 3 * step_y
                        gain_l = jnp.concatenate([w_ref[tap]] * side, axis=1)
                        gain_c = jnp.concatenate([w_ref[tap + 1]] * (side - 1), axis=1)
                        gain_r = jnp.concatenate([w_ref[tap + 2]] * side, axis=1)
                        left = left + window[:, : chunk + x_pad] * gain_l
                        centre = centre + window[:, x_pad : x_pad + chunk] * gain_c
                        right = right + window[:, x_pad:] * gain_r
                total = (
                    centre
                    + pltpu.roll(left, shift, 1)[:, :chunk]
                    + pltpu.roll(right, shift, 1)[:, :chunk]
                )
                for acc_ref in acc_refs:
                    total = total + acc_ref[plane, pl.ds(row, rows), pl.ds(base, chunk)].astype(
                        jnp.float32
                    )
                o_ref[plane, pl.ds(row, rows), pl.ds(base, chunk)] = total.astype(o_ref.dtype)
        return carry

    lax.fori_loop(0, count, body, 0)


def stencil_call(plan, inputs, accs, gains, y_cells, lanes, channels, out_dtype):
    chunk = min(1024, lanes)
    rows = 8 if y_cells % 8 == 0 else y_cells
    kernel = functools.partial(
        stencil_kernel, chunk, 2 * channels, y_cells, rows, plan, len(inputs), len(accs)
    )
    operands = list(inputs) + list(accs) + [gains]
    return pl.pallas_call(
        kernel,
        out_shape=jax.ShapeDtypeStruct((len(plan), y_cells, lanes), out_dtype),
    )(*operands)


def depthwise(rims, taps, flipped, x_cells, channels, out_dtype=jnp.float32, extra=()):
    inner, below, above = rims
    planes = inner.shape[0]
    y_cells = inner.shape[1] - 2
    lanes = x_cells * channels
    rows = 8 if y_cells % 8 == 0 else y_cells
    if flipped:
        taps = taps[::-1]
    gains = jnp.tile(taps.astype(jnp.float32), (1, 128 // channels))
    gains = jnp.broadcast_to(gains[:, None, :], (gains.shape[0], rows, 128))
    local_plan = tuple(
        tuple((0, plane + step_z - 1, step_z) for step_z in range(3) if 0 <= plane + step_z - 1 < planes)
        for plane in range(planes)
    )
    local = stencil_call(local_plan, (inner,), (), gains, y_cells, lanes, channels, jnp.float32)
    rim_plan = tuple(
        ((((0, 0, 0),) if plane == 0 else ()) + (((1, 0, 2),) if plane == planes - 1 else ()))
        for plane in range(planes)
    )
    accs = (local,) + tuple(extra)
    return stencil_call(rim_plan, (below, above), accs, gains, y_cells, lanes, channels, out_dtype)


def share_terms(field3, cos_table, sin_table):
    real_part = jnp.einsum("rxc,xk->krc", field3, cos_table, preferred_element_type=jnp.float32)
    imag_part = jnp.einsum("rxc,xk->krc", field3, sin_table, preferred_element_type=jnp.float32)
    return ring_reduce_scatter(jnp.concatenate([real_part, imag_part], axis=2), "gx")


def share_inverse(modes_share, cos_table, sin_table, channels):
    segment = ring_gather(modes_share, "gx")
    running = jnp.einsum(
        "krc,xk->rxc", segment[:, :, :channels], cos_table, preferred_element_type=jnp.float32
    )
    return running + jnp.einsum(
        "krc,xk->rxc", segment[:, :, channels:], sin_table, preferred_element_type=jnp.float32
    )


def split_gradients(dblock, channels):
    grad_real = dblock[:, :channels, :channels] + dblock[:, channels:, channels:]
    grad_imag = dblock[:, :channels, channels:] - dblock[:, channels:, :channels]
    return jnp.stack([grad_real, grad_imag])


def sum_gradients(local_grads):
    flat = local_grads.reshape(-1, 1024)
    return butterfly_sum(butterfly_sum(flat, "gy"), "gz").reshape(local_grads.shape)


def per_device(
    features, depth_weight, expand_weight, project_weight, spec_real, spec_imag, cotangent
):
    planes, y_cells, merged = features.shape
    channels = depth_weight.shape[1]
    x_cells = merged // channels
    row_count = planes * y_cells
    mode_count = spec_real.shape[0]
    group_size = lax.axis_size("gx")
    x_length = x_cells * group_size
    x_start = lax.axis_index("gx") * x_cells
    share_size = mode_count // group_size
    cos_part, sin_part = dft_tables(
        x_start, x_cells, x_length, jnp.arange(mode_count, dtype=jnp.int32)
    )
    order = gathered_order("gx", share_size)
    cos_order, sin_order = dft_tables(x_start, x_cells, x_length, order)
    cos_scaled = scaled_table(cos_order, order, x_length)
    sin_scaled = scaled_table(sin_order, order, x_length)
    cos_fwd_scaled = scaled_table(cos_part, jnp.arange(mode_count, dtype=jnp.int32), x_length)
    sin_fwd_scaled = scaled_table(sin_part, jnp.arange(mode_count, dtype=jnp.int32), x_length)
    blocks = block_weights(spec_real, spec_imag)
    padded = spatial_rims(features, channels)
    activation = depthwise(padded, depth_weight, False, x_cells, channels, jnp.bfloat16)
    field3 = features.reshape(row_count, x_cells, channels)
    owned_blocks = lax.dynamic_slice_in_dim(
        blocks, lax.axis_index("gx") * share_size, share_size, 0
    )
    coeffs = share_terms(field3, cos_part, sin_part).astype(jnp.bfloat16)
    mixed_modes = jnp.einsum(
        "krc,kco->kro", coeffs, owned_blocks, preferred_element_type=jnp.float32
    ).astype(jnp.bfloat16)
    mixed_modes, activation = lax.optimization_barrier((mixed_modes, activation))
    activation = activation.reshape(row_count * x_cells, channels)
    hidden_pre = jnp.dot(activation, expand_weight, preferred_element_type=jnp.float32)
    hidden, hidden_slope = gelu_parts(hidden_pre)
    local_branch = jnp.dot(
        hidden.astype(jnp.bfloat16), project_weight, preferred_element_type=jnp.float32
    )
    local_branch = local_branch.reshape(row_count, x_cells, channels)
    spectral = share_inverse(mixed_modes, cos_scaled, sin_scaled, channels)
    result, slopes = gelu_parts(local_branch + spectral)
    out_points = result.astype(jnp.bfloat16)
    grad_pre = (
        lax.optimization_barrier(cotangent.reshape(row_count, x_cells, channels)).astype(jnp.float32)
        * slopes
    ).astype(jnp.bfloat16)
    hidden_grad = jnp.dot(
        grad_pre.reshape(row_count * x_cells, channels),
        project_weight.T,
        preferred_element_type=jnp.float32,
    )
    grad_hidden = (hidden_grad * hidden_slope).astype(jnp.bfloat16)
    grad_act = jnp.dot(grad_hidden, expand_weight.T, preferred_element_type=jnp.float32).astype(
        jnp.bfloat16
    )
    grad_act = grad_act.reshape(planes, y_cells, merged)
    dcoef = share_terms(grad_pre, cos_fwd_scaled, sin_fwd_scaled).astype(jnp.bfloat16)
    dmode = jnp.einsum(
        "kro,kco->krc", dcoef, owned_blocks, preferred_element_type=jnp.float32
    ).astype(jnp.bfloat16)
    dblock = jnp.einsum("krc,kro->kco", coeffs, dcoef, preferred_element_type=jnp.float32)
    local_grads = split_gradients(dblock, channels)
    dmode, local_grads, grad_act = lax.optimization_barrier((dmode, local_grads, grad_act))
    spectral_grad = share_inverse(dmode, cos_order, sin_order, channels)
    grad_spec = sum_gradients(local_grads)
    padded_grad = spatial_rims(grad_act, channels)
    out_points, inner_grad = lax.optimization_barrier((out_points, padded_grad[0]))
    padded_grad = (inner_grad,) + padded_grad[1:]
    output = out_points.reshape(planes, y_cells, merged)
    grad_features = depthwise(
        padded_grad,
        depth_weight,
        True,
        x_cells,
        channels,
        jnp.bfloat16,
        (spectral_grad.astype(jnp.bfloat16).reshape(planes, y_cells, merged),),
    )
    return (output, grad_features, grad_spec)


def solution(mesh):
    placed = (P("gz", "gy", "gx"), P(), P(), P(), P(), P(), P("gz", "gy", "gx"))
    return jax.shard_map(
        per_device,
        mesh=mesh,
        in_specs=placed,
        out_specs=(P("gz", "gy", "gx"), P("gz", "gy", "gx"), P(None, "gx", None, None)),
        check_vma=False,
    )
```

```python
import functools
import math

import jax
import jax.numpy as jnp
from jax import lax
from jax.experimental import pallas as pl
from jax.experimental.pallas import tpu as pltpu
from jax.sharding import PartitionSpec as P


def padded_2(value, sides, width, wrap):
    for axis, dim in sides:
        size, length = (lax.axis_size(axis), value.shape[dim])
        last = lax.slice_in_dim(value, length - width, length, axis=dim)
        leading = lax.slice_in_dim(value, 0, width, axis=dim)
        if size == 2 and not wrap:
            first = lax.axis_index(axis) == 0
            swapped = lax.ppermute(jnp.where(first, last, leading), axis, [(0, 1), (1, 0)])
            zeros = jnp.zeros_like(swapped)
            before = jnp.where(first, zeros, swapped)
            after = jnp.where(first, swapped, zeros)
        else:
            up = [(i, (i + 1) % size) for i in range(size if wrap else size - 1)]
            down = [(j, i) for i, j in up]
            before = lax.ppermute(last, axis, up)
            after = lax.ppermute(leading, axis, down)
        value = jnp.concatenate([before, value, after], axis=dim)
    return value


def gelu_parts(values):
    normal_cdf = 0.5 * (1.0 + jax.scipy.special.erf(values * (1.0 / math.sqrt(2.0))))
    density = jnp.exp(-0.5 * values * values) * (1.0 / math.sqrt(2.0 * math.pi))
    return (values * normal_cdf, normal_cdf + values * density)


def dft_tables(offset, cells, x_length, frequency):
    position = offset + jnp.arange(cells, dtype=jnp.int32)
    phase_int = position[:, None] * frequency[None, :] % x_length
    angles = phase_int.astype(jnp.float32) * (2.0 * math.pi / x_length)
    return (jnp.cos(angles).astype(jnp.bfloat16), (-jnp.sin(angles)).astype(jnp.bfloat16))


def scaled_table(table, frequency, x_length):
    mode_scale = jnp.where(frequency == 0, 1.0, 2.0).astype(jnp.float32) / x_length
    return (table.astype(jnp.float32) * mode_scale[None, :]).astype(jnp.bfloat16)


def gathered_order(axis, share_size):
    size = lax.axis_size(axis)
    shifts = jnp.arange(size, dtype=jnp.int32)
    me = lax.axis_index(axis)
    if size & (size - 1):
        sources = (me - shifts) % size
    else:
        sources = jnp.bitwise_xor(me, shifts)
    local = jnp.arange(share_size, dtype=jnp.int32)
    return (sources[:, None] * share_size + local[None, :]).reshape(-1)


def ring_gather(block, axis):
    size = lax.axis_size(axis)
    if size & (size - 1) == 0:
        step = 1
        while step < size:
            block = jnp.concatenate(
                [block, lax.ppermute(block, axis, [(i, i ^ step) for i in range(size)])], axis=0
            )
            step *= 2
        return block
    pieces = [block]
    for shift in range(1, size):
        pieces.append(lax.ppermute(block, axis, [(i, (i + shift) % size) for i in range(size)]))
    return jnp.concatenate(pieces, axis=0)


def ring_reduce_scatter(value, axis):
    size = lax.axis_size(axis)
    share = value.shape[0] // size
    me = lax.axis_index(axis)
    if size & (size - 1) == 0:
        step = size // 2
        count = size
        while step >= 1:
            count //= 2
            upper = jnp.bitwise_and(me, step) != 0
            keep = lax.dynamic_slice_in_dim(value, jnp.where(upper, count, 0) * share, count * share, 0)
            send = lax.dynamic_slice_in_dim(value, jnp.where(upper, 0, count) * share, count * share, 0)
            value = keep + lax.ppermute(send, axis, [(i, i ^ step) for i in range(size)])
            step //= 2
        return value
    total = lax.dynamic_slice_in_dim(value, me * share, share, 0)
    for shift in range(1, size):
        piece = lax.dynamic_slice_in_dim(value, ((me + shift) % size) * share, share, 0)
        total = total + lax.ppermute(piece, axis, [(i, (i + shift) % size) for i in range(size)])
    return total


def butterfly_sum(value, axis):
    size = lax.axis_size(axis)
    if size & (size - 1):
        return lax.psum(value, axis)
    step = 1
    while step < size:
        value = value.astype(jnp.bfloat16)
        value = value.astype(jnp.float32) + lax.ppermute(
            value, axis, [(i, i ^ step) for i in range(size)]
        ).astype(jnp.float32)
        step *= 2
    return value


def block_weights(spec_real, spec_imag):
    upper_row = jnp.concatenate([spec_real, spec_imag], axis=2)
    lower_row = jnp.concatenate([-spec_imag, spec_real], axis=2)
    return jnp.concatenate([upper_row, lower_row], axis=1)


def spatial_rims(field_block, channels):
    x_wide = padded_2(field_block, (("gx", 2),), 2 * channels, True)
    inner = padded_2(x_wide, (("gy", 1),), 1, False)
    size = lax.axis_size("gz")
    up = [(i, i + 1) for i in range(size - 1)]
    down = [(j, i) for i, j in up]
    below = lax.ppermute(inner[-1:], "gz", up)
    above = lax.ppermute(inner[:1], "gz", down)
    return (inner, below, above)


def stencil_kernel(chunk, x_pad, y_cells, rows, plan, sources, has_acc, *refs):
    src_refs = refs[:sources]
    acc_refs = refs[sources : sources + has_acc]
    w_ref, o_ref = refs[sources + has_acc :]
    width = chunk + 2 * x_pad
    count = o_ref.shape[2] // chunk
    shift = chunk + x_pad - x_pad // 2
    side = (chunk + x_pad) // 128

    def body(index, carry):
        base = pl.multiple_of(index * chunk, chunk)
        for plane, terms in enumerate(plan):
            for row in range(0, y_cells, rows):
                left = jnp.zeros((rows, chunk + x_pad), jnp.float32)
                centre = jnp.zeros((rows, chunk), jnp.float32)
                right = jnp.zeros((rows, chunk + x_pad), jnp.float32)
                for source, source_plane, step_z in terms:
                    for step_y in range(3):
                        window = src_refs[source][
                            source_plane, pl.ds(row + step_y, rows), pl.ds(base, width)
                        ].astype(jnp.float32)
                        tap = 9 * step_z + 3 * step_y
                        gain_l = jnp.concatenate([w_ref[tap]] * side, axis=1)
                        gain_c = jnp.concatenate([w_ref[tap + 1]] * (side - 1), axis=1)
                        gain_r = jnp.concatenate([w_ref[tap + 2]] * side, axis=1)
                        left = left + window[:, : chunk + x_pad] * gain_l
                        centre = centre + window[:, x_pad : x_pad + chunk] * gain_c
                        right = right + window[:, x_pad:] * gain_r
                total = (
                    centre
                    + pltpu.roll(left, shift, 1)[:, :chunk]
                    + pltpu.roll(right, shift, 1)[:, :chunk]
                )
                for acc_ref in acc_refs:
                    total = total + acc_ref[plane, pl.ds(row, rows), pl.ds(base, chunk)].astype(
                        jnp.float32
                    )
                o_ref[plane, pl.ds(row, rows), pl.ds(base, chunk)] = total.astype(o_ref.dtype)
        return carry

    lax.fori_loop(0, count, body, 0)


def stencil_call(plan, inputs, accs, gains, y_cells, lanes, channels, out_dtype):
    chunk = min(512, lanes)
    rows = 16 if y_cells % 16 == 0 else y_cells
    kernel = functools.partial(
        stencil_kernel, chunk, 2 * channels, y_cells, rows, plan, len(inputs), len(accs)
    )
    operands = list(inputs) + list(accs) + [gains]
    return pl.pallas_call(
        kernel,
        out_shape=jax.ShapeDtypeStruct((len(plan), y_cells, lanes), out_dtype),
    )(*operands)


def depthwise(rims, taps, flipped, x_cells, channels, out_dtype=jnp.float32, extra=()):
    inner, below, above = rims
    planes = inner.shape[0]
    y_cells = inner.shape[1] - 2
    lanes = x_cells * channels
    rows = 16 if y_cells % 16 == 0 else y_cells
    if flipped:
        taps = taps[::-1]
    gains = jnp.tile(taps.astype(jnp.float32), (1, 128 // channels))
    gains = jnp.broadcast_to(gains[:, None, :], (gains.shape[0], rows, 128))
    local_plan = tuple(
        tuple((0, plane + step_z - 1, step_z) for step_z in range(3) if 0 <= plane + step_z - 1 < planes)
        for plane in range(planes)
    )
    local = stencil_call(local_plan, (inner,), (), gains, y_cells, lanes, channels, jnp.float32)
    rim_plan = tuple(
        ((((0, 0, 0),) if plane == 0 else ()) + (((1, 0, 2),) if plane == planes - 1 else ()))
        for plane in range(planes)
    )
    accs = (local,) + tuple(extra)
    return stencil_call(rim_plan, (below, above), accs, gains, y_cells, lanes, channels, out_dtype)


def share_terms(field3, cos_table, sin_table):
    real_part = jnp.einsum("rxc,xk->krc", field3, cos_table, preferred_element_type=jnp.float32)
    imag_part = jnp.einsum("rxc,xk->krc", field3, sin_table, preferred_element_type=jnp.float32)
    return ring_reduce_scatter(jnp.concatenate([real_part, imag_part], axis=2), "gx")


def share_inverse(modes_share, cos_table, sin_table, channels):
    segment = ring_gather(modes_share, "gx")
    running = jnp.einsum(
        "krc,xk->rxc", segment[:, :, :channels], cos_table, preferred_element_type=jnp.float32
    )
    return running + jnp.einsum(
        "krc,xk->rxc", segment[:, :, channels:], sin_table, preferred_element_type=jnp.float32
    )


def split_gradients(dblock, channels):
    grad_real = dblock[:, :channels, :channels] + dblock[:, channels:, channels:]
    grad_imag = dblock[:, :channels, channels:] - dblock[:, channels:, :channels]
    return jnp.stack([grad_real, grad_imag])


def sum_gradients(local_grads):
    flat = local_grads.reshape(-1, 1024)
    return butterfly_sum(butterfly_sum(flat, "gy"), "gz").reshape(local_grads.shape)


def per_device(
    features, depth_weight, expand_weight, project_weight, spec_real, spec_imag, cotangent
):
    planes, y_cells, merged = features.shape
    channels = depth_weight.shape[1]
    x_cells = merged // channels
    row_count = planes * y_cells
    mode_count = spec_real.shape[0]
    group_size = lax.axis_size("gx")
    x_length = x_cells * group_size
    x_start = lax.axis_index("gx") * x_cells
    share_size = mode_count // group_size
    cos_part, sin_part = dft_tables(
        x_start, x_cells, x_length, jnp.arange(mode_count, dtype=jnp.int32)
    )
    order = gathered_order("gx", share_size)
    cos_order, sin_order = dft_tables(x_start, x_cells, x_length, order)
    cos_scaled = scaled_table(cos_order, order, x_length)
    sin_scaled = scaled_table(sin_order, order, x_length)
    cos_fwd_scaled = scaled_table(cos_part, jnp.arange(mode_count, dtype=jnp.int32), x_length)
    sin_fwd_scaled = scaled_table(sin_part, jnp.arange(mode_count, dtype=jnp.int32), x_length)
    blocks = block_weights(spec_real, spec_imag)
    padded = spatial_rims(features, channels)
    activation = depthwise(padded, depth_weight, False, x_cells, channels, jnp.bfloat16)
    field3 = features.reshape(row_count, x_cells, channels)
    owned_blocks = lax.dynamic_slice_in_dim(
        blocks, lax.axis_index("gx") * share_size, share_size, 0
    )
    coeffs = share_terms(field3, cos_part, sin_part).astype(jnp.bfloat16)
    mixed_modes = jnp.einsum(
        "krc,kco->kro", coeffs, owned_blocks, preferred_element_type=jnp.float32
    ).astype(jnp.bfloat16)
    mixed_modes, activation = lax.optimization_barrier((mixed_modes, activation))
    activation = activation.reshape(row_count * x_cells, channels)
    hidden_pre = jnp.dot(activation, expand_weight, preferred_element_type=jnp.float32)
    hidden, hidden_slope = gelu_parts(hidden_pre)
    local_branch = jnp.dot(
        hidden.astype(jnp.bfloat16), project_weight, preferred_element_type=jnp.float32
    )
    local_branch = local_branch.reshape(row_count, x_cells, channels)
    spectral = share_inverse(mixed_modes, cos_scaled, sin_scaled, channels)
    result, slopes = gelu_parts(local_branch + spectral)
    output = result.astype(jnp.bfloat16).reshape(planes, y_cells, merged)
    grad_pre = (
        lax.optimization_barrier(cotangent.reshape(row_count, x_cells, channels)).astype(jnp.float32)
        * slopes
    ).astype(jnp.bfloat16)
    hidden_grad = jnp.dot(
        grad_pre.reshape(row_count * x_cells, channels),
        project_weight.T,
        preferred_element_type=jnp.float32,
    )
    grad_hidden = (hidden_grad * hidden_slope).astype(jnp.bfloat16)
    grad_act = jnp.dot(grad_hidden, expand_weight.T, preferred_element_type=jnp.float32).astype(
        jnp.bfloat16
    )
    grad_act = grad_act.reshape(planes, y_cells, merged)
    dcoef = share_terms(grad_pre, cos_fwd_scaled, sin_fwd_scaled).astype(jnp.bfloat16)
    dmode = jnp.einsum(
        "kro,kco->krc", dcoef, owned_blocks, preferred_element_type=jnp.float32
    ).astype(jnp.bfloat16)
    dblock = jnp.einsum("krc,kro->kco", coeffs, dcoef, preferred_element_type=jnp.float32)
    local_grads = split_gradients(dblock, channels)
    dmode, local_grads, grad_act = lax.optimization_barrier((dmode, local_grads, grad_act))
    spectral_grad = share_inverse(dmode, cos_order, sin_order, channels)
    grad_spec = sum_gradients(local_grads)
    padded_grad = spatial_rims(grad_act, channels)
    grad_features = depthwise(
        padded_grad,
        depth_weight,
        True,
        x_cells,
        channels,
        jnp.bfloat16,
        (spectral_grad.astype(jnp.bfloat16).reshape(planes, y_cells, merged),),
    )
    return (output, grad_features, grad_spec)


def solution(mesh):
    placed = (P("gz", "gy", "gx"), P(), P(), P(), P(), P(), P("gz", "gy", "gx"))
    return jax.shard_map(
        per_device,
        mesh=mesh,
        in_specs=placed,
        out_specs=(P("gz", "gy", "gx"), P("gz", "gy", "gx"), P(None, "gx", None, None)),
        check_vma=False,
    )
```

```python
import functools
import math

import jax
import jax.numpy as jnp
from jax import lax
from jax.experimental import pallas as pl
from jax.experimental.pallas import tpu as pltpu
from jax.sharding import PartitionSpec as P


def padded_2(value, sides, width, wrap):
    for axis, dim in sides:
        size, length = (lax.axis_size(axis), value.shape[dim])
        last = lax.slice_in_dim(value, length - width, length, axis=dim)
        leading = lax.slice_in_dim(value, 0, width, axis=dim)
        if size == 2 and not wrap:
            first = lax.axis_index(axis) == 0
            swapped = lax.ppermute(jnp.where(first, last, leading), axis, [(0, 1), (1, 0)])
            zeros = jnp.zeros_like(swapped)
            before = jnp.where(first, zeros, swapped)
            after = jnp.where(first, swapped, zeros)
        else:
            up = [(i, (i + 1) % size) for i in range(size if wrap else size - 1)]
            down = [(j, i) for i, j in up]
            before = lax.ppermute(last, axis, up)
            after = lax.ppermute(leading, axis, down)
        value = jnp.concatenate([before, value, after], axis=dim)
    return value


def gelu_parts(values):
    normal_cdf = 0.5 * (1.0 + jax.scipy.special.erf(values * (1.0 / math.sqrt(2.0))))
    density = jnp.exp(-0.5 * values * values) * (1.0 / math.sqrt(2.0 * math.pi))
    return (values * normal_cdf, normal_cdf + values * density)


def dft_tables(offset, cells, x_length, frequency):
    position = offset + jnp.arange(cells, dtype=jnp.int32)
    phase_int = position[:, None] * frequency[None, :] % x_length
    angles = phase_int.astype(jnp.float32) * (2.0 * math.pi / x_length)
    return (jnp.cos(angles).astype(jnp.bfloat16), (-jnp.sin(angles)).astype(jnp.bfloat16))


def scaled_table(table, frequency, x_length):
    mode_scale = jnp.where(frequency == 0, 1.0, 2.0).astype(jnp.float32) / x_length
    return (table.astype(jnp.float32) * mode_scale[None, :]).astype(jnp.bfloat16)


def gathered_order(axis, share_size):
    size = lax.axis_size(axis)
    shifts = jnp.arange(size, dtype=jnp.int32)
    me = lax.axis_index(axis)
    if size & (size - 1):
        sources = (me - shifts) % size
    else:
        sources = jnp.bitwise_xor(me, shifts)
    local = jnp.arange(share_size, dtype=jnp.int32)
    return (sources[:, None] * share_size + local[None, :]).reshape(-1)


def ring_gather(block, axis):
    size = lax.axis_size(axis)
    if size & (size - 1) == 0:
        step = 1
        while step < size:
            block = jnp.concatenate(
                [block, lax.ppermute(block, axis, [(i, i ^ step) for i in range(size)])], axis=0
            )
            step *= 2
        return block
    pieces = [block]
    for shift in range(1, size):
        pieces.append(lax.ppermute(block, axis, [(i, (i + shift) % size) for i in range(size)]))
    return jnp.concatenate(pieces, axis=0)


def ring_reduce_scatter(value, axis):
    size = lax.axis_size(axis)
    share = value.shape[0] // size
    me = lax.axis_index(axis)
    if size & (size - 1) == 0:
        step = size // 2
        count = size
        while step >= 1:
            count //= 2
            upper = jnp.bitwise_and(me, step) != 0
            keep = lax.dynamic_slice_in_dim(value, jnp.where(upper, count, 0) * share, count * share, 0)
            send = lax.dynamic_slice_in_dim(value, jnp.where(upper, 0, count) * share, count * share, 0)
            value = keep + lax.ppermute(send, axis, [(i, i ^ step) for i in range(size)])
            step //= 2
        return value
    total = lax.dynamic_slice_in_dim(value, me * share, share, 0)
    for shift in range(1, size):
        piece = lax.dynamic_slice_in_dim(value, ((me + shift) % size) * share, share, 0)
        total = total + lax.ppermute(piece, axis, [(i, (i + shift) % size) for i in range(size)])
    return total


def butterfly_sum(value, axis):
    size = lax.axis_size(axis)
    if size & (size - 1):
        return lax.psum(value, axis)
    step = 1
    while step < size:
        value = value.astype(jnp.bfloat16)
        value = value.astype(jnp.float32) + lax.ppermute(
            value, axis, [(i, i ^ step) for i in range(size)]
        ).astype(jnp.float32)
        step *= 2
    return value


def block_weights(spec_real, spec_imag):
    upper_row = jnp.concatenate([spec_real, spec_imag], axis=2)
    lower_row = jnp.concatenate([-spec_imag, spec_real], axis=2)
    return jnp.concatenate([upper_row, lower_row], axis=1)


def spatial_rims(field_block, channels):
    x_wide = padded_2(field_block, (("gx", 2),), 2 * channels, True)
    inner = padded_2(x_wide, (("gy", 1),), 1, False)
    size = lax.axis_size("gz")
    up = [(i, i + 1) for i in range(size - 1)]
    down = [(j, i) for i, j in up]
    below = lax.ppermute(inner[-1:], "gz", up)
    above = lax.ppermute(inner[:1], "gz", down)
    return (inner, below, above)


def stencil_kernel(chunk, x_pad, y_cells, rows, plan, sources, has_acc, *refs):
    src_refs = refs[:sources]
    acc_refs = refs[sources : sources + has_acc]
    w_ref, o_ref = refs[sources + has_acc :]
    width = chunk + 2 * x_pad
    count = o_ref.shape[2] // chunk
    shift = chunk + x_pad - x_pad // 2
    side = (chunk + x_pad) // 128

    def body(index, carry):
        base = pl.multiple_of(index * chunk, chunk)
        for plane, terms in enumerate(plan):
            for row in range(0, y_cells, rows):
                left = jnp.zeros((rows, chunk + x_pad), jnp.float32)
                centre = jnp.zeros((rows, chunk), jnp.float32)
                right = jnp.zeros((rows, chunk + x_pad), jnp.float32)
                for source, source_plane, step_z in terms:
                    for step_y in range(3):
                        window = src_refs[source][
                            source_plane, pl.ds(row + step_y, rows), pl.ds(base, width)
                        ].astype(jnp.float32)
                        tap = 9 * step_z + 3 * step_y
                        gain_l = jnp.concatenate([w_ref[tap]] * side, axis=1)
                        gain_c = jnp.concatenate([w_ref[tap + 1]] * (side - 1), axis=1)
                        gain_r = jnp.concatenate([w_ref[tap + 2]] * side, axis=1)
                        left = left + window[:, : chunk + x_pad] * gain_l
                        centre = centre + window[:, x_pad : x_pad + chunk] * gain_c
                        right = right + window[:, x_pad:] * gain_r
                total = (
                    centre
                    + pltpu.roll(left, shift, 1)[:, :chunk]
                    + pltpu.roll(right, shift, 1)[:, :chunk]
                )
                for acc_ref in acc_refs:
                    total = total + acc_ref[plane, pl.ds(row, rows), pl.ds(base, chunk)].astype(
                        jnp.float32
                    )
                o_ref[plane, pl.ds(row, rows), pl.ds(base, chunk)] = total.astype(o_ref.dtype)
        return carry

    lax.fori_loop(0, count, body, 0)


def stencil_call(plan, inputs, accs, gains, y_cells, lanes, channels, out_dtype):
    chunk = min(2048, lanes)
    rows = 8 if y_cells % 8 == 0 else y_cells
    kernel = functools.partial(
        stencil_kernel, chunk, 2 * channels, y_cells, rows, plan, len(inputs), len(accs)
    )
    operands = list(inputs) + list(accs) + [gains]
    return pl.pallas_call(
        kernel,
        out_shape=jax.ShapeDtypeStruct((len(plan), y_cells, lanes), out_dtype),
    )(*operands)


def depthwise(rims, taps, flipped, x_cells, channels, out_dtype=jnp.float32, extra=()):
    inner, below, above = rims
    planes = inner.shape[0]
    y_cells = inner.shape[1] - 2
    lanes = x_cells * channels
    rows = 8 if y_cells % 8 == 0 else y_cells
    if flipped:
        taps = taps[::-1]
    gains = jnp.tile(taps.astype(jnp.float32), (1, 128 // channels))
    gains = jnp.broadcast_to(gains[:, None, :], (gains.shape[0], rows, 128))
    local_plan = tuple(
        tuple((0, plane + step_z - 1, step_z) for step_z in range(3) if 0 <= plane + step_z - 1 < planes)
        for plane in range(planes)
    )
    local = stencil_call(local_plan, (inner,), (), gains, y_cells, lanes, channels, jnp.float32)
    rim_plan = tuple(
        ((((0, 0, 0),) if plane == 0 else ()) + (((1, 0, 2),) if plane == planes - 1 else ()))
        for plane in range(planes)
    )
    accs = (local,) + tuple(extra)
    return stencil_call(rim_plan, (below, above), accs, gains, y_cells, lanes, channels, out_dtype)


def share_terms(field3, cos_table, sin_table):
    real_part = jnp.einsum("rxc,xk->krc", field3, cos_table, preferred_element_type=jnp.float32)
    imag_part = jnp.einsum("rxc,xk->krc", field3, sin_table, preferred_element_type=jnp.float32)
    return ring_reduce_scatter(jnp.concatenate([real_part, imag_part], axis=2), "gx")


def share_inverse(modes_share, cos_table, sin_table, channels):
    segment = ring_gather(modes_share, "gx")
    running = jnp.einsum(
        "krc,xk->rxc", segment[:, :, :channels], cos_table, preferred_element_type=jnp.float32
    )
    return running + jnp.einsum(
        "krc,xk->rxc", segment[:, :, channels:], sin_table, preferred_element_type=jnp.float32
    )


def split_gradients(dblock, channels):
    grad_real = dblock[:, :channels, :channels] + dblock[:, channels:, channels:]
    grad_imag = dblock[:, :channels, channels:] - dblock[:, channels:, :channels]
    return jnp.stack([grad_real, grad_imag])


def sum_gradients(local_grads):
    flat = local_grads.reshape(-1, 1024)
    return butterfly_sum(butterfly_sum(flat, "gy"), "gz").reshape(local_grads.shape)


def per_device(
    features, depth_weight, expand_weight, project_weight, spec_real, spec_imag, cotangent
):
    planes, y_cells, merged = features.shape
    channels = depth_weight.shape[1]
    x_cells = merged // channels
    row_count = planes * y_cells
    mode_count = spec_real.shape[0]
    group_size = lax.axis_size("gx")
    x_length = x_cells * group_size
    x_start = lax.axis_index("gx") * x_cells
    share_size = mode_count // group_size
    cos_part, sin_part = dft_tables(
        x_start, x_cells, x_length, jnp.arange(mode_count, dtype=jnp.int32)
    )
    order = gathered_order("gx", share_size)
    cos_order, sin_order = dft_tables(x_start, x_cells, x_length, order)
    cos_scaled = scaled_table(cos_order, order, x_length)
    sin_scaled = scaled_table(sin_order, order, x_length)
    cos_fwd_scaled = scaled_table(cos_part, jnp.arange(mode_count, dtype=jnp.int32), x_length)
    sin_fwd_scaled = scaled_table(sin_part, jnp.arange(mode_count, dtype=jnp.int32), x_length)
    blocks = block_weights(spec_real, spec_imag)
    padded = spatial_rims(features, channels)
    activation = depthwise(padded, depth_weight, False, x_cells, channels, jnp.bfloat16)
    field3 = features.reshape(row_count, x_cells, channels)
    owned_blocks = lax.dynamic_slice_in_dim(
        blocks, lax.axis_index("gx") * share_size, share_size, 0
    )
    coeffs = share_terms(field3, cos_part, sin_part).astype(jnp.bfloat16)
    mixed_modes = jnp.einsum(
        "krc,kco->kro", coeffs, owned_blocks, preferred_element_type=jnp.float32
    ).astype(jnp.bfloat16)
    mixed_modes, activation = lax.optimization_barrier((mixed_modes, activation))
    activation = activation.reshape(row_count * x_cells, channels)
    hidden_pre = jnp.dot(activation, expand_weight, preferred_element_type=jnp.float32)
    hidden, hidden_slope = gelu_parts(hidden_pre)
    local_branch = jnp.dot(
        hidden.astype(jnp.bfloat16), project_weight, preferred_element_type=jnp.float32
    )
    local_branch = local_branch.reshape(row_count, x_cells, channels)
    spectral = share_inverse(mixed_modes, cos_scaled, sin_scaled, channels)
    result, slopes = gelu_parts(local_branch + spectral)
    output = result.astype(jnp.bfloat16).reshape(planes, y_cells, merged)
    grad_pre = (
        lax.optimization_barrier(cotangent.reshape(row_count, x_cells, channels)).astype(jnp.float32)
        * slopes
    ).astype(jnp.bfloat16)
    hidden_grad = jnp.dot(
        grad_pre.reshape(row_count * x_cells, channels),
        project_weight.T,
        preferred_element_type=jnp.float32,
    )
    grad_hidden = (hidden_grad * hidden_slope).astype(jnp.bfloat16)
    grad_act = jnp.dot(grad_hidden, expand_weight.T, preferred_element_type=jnp.float32).astype(
        jnp.bfloat16
    )
    grad_act = grad_act.reshape(planes, y_cells, merged)
    dcoef = share_terms(grad_pre, cos_fwd_scaled, sin_fwd_scaled).astype(jnp.bfloat16)
    dmode = jnp.einsum(
        "kro,kco->krc", dcoef, owned_blocks, preferred_element_type=jnp.float32
    ).astype(jnp.bfloat16)
    dblock = jnp.einsum("krc,kro->kco", coeffs, dcoef, preferred_element_type=jnp.float32)
    local_grads = split_gradients(dblock, channels)
    dmode, local_grads, grad_act = lax.optimization_barrier((dmode, local_grads, grad_act))
    spectral_grad = share_inverse(dmode, cos_order, sin_order, channels)
    grad_spec = sum_gradients(local_grads)
    padded_grad = spatial_rims(grad_act, channels)
    grad_features = depthwise(
        padded_grad,
        depth_weight,
        True,
        x_cells,
        channels,
        jnp.bfloat16,
        (spectral_grad.astype(jnp.bfloat16).reshape(planes, y_cells, merged),),
    )
    return (output, grad_features, grad_spec)


def solution(mesh):
    placed = (P("gz", "gy", "gx"), P(), P(), P(), P(), P(), P("gz", "gy", "gx"))
    return jax.shard_map(
        per_device,
        mesh=mesh,
        in_specs=placed,
        out_specs=(P("gz", "gy", "gx"), P("gz", "gy", "gx"), P(None, "gx", None, None)),
        check_vma=False,
    )
```

```python
import functools
import math

import jax
import jax.numpy as jnp
from jax import lax
from jax.experimental import pallas as pl
from jax.experimental.pallas import tpu as pltpu
from jax.sharding import PartitionSpec as P


def padded_2(value, sides, width, wrap):
    for axis, dim in sides:
        size, length = (lax.axis_size(axis), value.shape[dim])
        last = lax.slice_in_dim(value, length - width, length, axis=dim)
        leading = lax.slice_in_dim(value, 0, width, axis=dim)
        if size == 2 and not wrap:
            first = lax.axis_index(axis) == 0
            swapped = lax.ppermute(jnp.where(first, last, leading), axis, [(0, 1), (1, 0)])
            zeros = jnp.zeros_like(swapped)
            before = jnp.where(first, zeros, swapped)
            after = jnp.where(first, swapped, zeros)
        else:
            up = [(i, (i + 1) % size) for i in range(size if wrap else size - 1)]
            down = [(j, i) for i, j in up]
            before = lax.ppermute(last, axis, up)
            after = lax.ppermute(leading, axis, down)
        value = jnp.concatenate([before, value, after], axis=dim)
    return value


def gelu_parts(values):
    normal_cdf = 0.5 * (1.0 + jax.scipy.special.erf(values * (1.0 / math.sqrt(2.0))))
    density = jnp.exp(-0.5 * values * values) * (1.0 / math.sqrt(2.0 * math.pi))
    return (values * normal_cdf, normal_cdf + values * density)


def dft_tables(offset, cells, x_length, frequency):
    position = offset + jnp.arange(cells, dtype=jnp.int32)
    phase_int = position[:, None] * frequency[None, :] % x_length
    angles = phase_int.astype(jnp.float32) * (2.0 * math.pi / x_length)
    return (jnp.cos(angles).astype(jnp.bfloat16), (-jnp.sin(angles)).astype(jnp.bfloat16))


def scaled_table(table, frequency, x_length):
    mode_scale = jnp.where(frequency == 0, 1.0, 2.0).astype(jnp.float32) / x_length
    return (table.astype(jnp.float32) * mode_scale[None, :]).astype(jnp.bfloat16)


def gathered_order(axis, share_size):
    size = lax.axis_size(axis)
    shifts = jnp.arange(size, dtype=jnp.int32)
    me = lax.axis_index(axis)
    if size & (size - 1):
        sources = (me - shifts) % size
    else:
        sources = jnp.bitwise_xor(me, shifts)
    local = jnp.arange(share_size, dtype=jnp.int32)
    return (sources[:, None] * share_size + local[None, :]).reshape(-1)


def ring_gather(block, axis):
    size = lax.axis_size(axis)
    if size & (size - 1) == 0:
        step = 1
        while step < size:
            block = jnp.concatenate(
                [block, lax.ppermute(block, axis, [(i, i ^ step) for i in range(size)])], axis=0
            )
            step *= 2
        return block
    pieces = [block]
    for shift in range(1, size):
        pieces.append(lax.ppermute(block, axis, [(i, (i + shift) % size) for i in range(size)]))
    return jnp.concatenate(pieces, axis=0)


def ring_reduce_scatter(value, axis):
    size = lax.axis_size(axis)
    share = value.shape[0] // size
    me = lax.axis_index(axis)
    if size & (size - 1) == 0:
        step = size // 2
        count = size
        while step >= 1:
            count //= 2
            upper = jnp.bitwise_and(me, step) != 0
            keep = lax.dynamic_slice_in_dim(value, jnp.where(upper, count, 0) * share, count * share, 0)
            send = lax.dynamic_slice_in_dim(value, jnp.where(upper, 0, count) * share, count * share, 0)
            value = keep + lax.ppermute(send, axis, [(i, i ^ step) for i in range(size)])
            step //= 2
        return value
    total = lax.dynamic_slice_in_dim(value, me * share, share, 0)
    for shift in range(1, size):
        piece = lax.dynamic_slice_in_dim(value, ((me + shift) % size) * share, share, 0)
        total = total + lax.ppermute(piece, axis, [(i, (i + shift) % size) for i in range(size)])
    return total


def butterfly_sum(value, axis):
    size = lax.axis_size(axis)
    if size & (size - 1):
        return lax.psum(value, axis)
    step = 1
    while step < size:
        value = value.astype(jnp.bfloat16)
        value = value.astype(jnp.float32) + lax.ppermute(
            value, axis, [(i, i ^ step) for i in range(size)]
        ).astype(jnp.float32)
        step *= 2
    return value


def block_weights(spec_real, spec_imag):
    upper_row = jnp.concatenate([spec_real, spec_imag], axis=2)
    lower_row = jnp.concatenate([-spec_imag, spec_real], axis=2)
    return jnp.concatenate([upper_row, lower_row], axis=1)


def spatial_rims(field_block, channels):
    x_wide = padded_2(field_block, (("gx", 2),), 2 * channels, True)
    inner = padded_2(x_wide, (("gy", 1),), 1, False)
    size = lax.axis_size("gz")
    up = [(i, i + 1) for i in range(size - 1)]
    down = [(j, i) for i, j in up]
    below = lax.ppermute(inner[-1:], "gz", up)
    above = lax.ppermute(inner[:1], "gz", down)
    return (inner, below, above)


def stencil_kernel(chunk, x_pad, y_cells, rows, plan, sources, has_acc, *refs):
    src_refs = refs[:sources]
    acc_refs = refs[sources : sources + has_acc]
    w_ref, o_ref = refs[sources + has_acc :]
    width = chunk + 2 * x_pad
    count = o_ref.shape[2] // chunk
    shift = chunk + x_pad - x_pad // 2
    side = (chunk + x_pad) // 128

    def body(index, carry):
        base = pl.multiple_of(index * chunk, chunk)
        for plane, terms in enumerate(plan):
            for row in range(0, y_cells, rows):
                left = jnp.zeros((rows, chunk + x_pad), jnp.float32)
                centre = jnp.zeros((rows, chunk), jnp.float32)
                right = jnp.zeros((rows, chunk + x_pad), jnp.float32)
                for source, source_plane, step_z in terms:
                    for step_y in range(3):
                        window = src_refs[source][
                            source_plane, pl.ds(row + step_y, rows), pl.ds(base, width)
                        ].astype(jnp.float32)
                        tap = 9 * step_z + 3 * step_y
                        gain_l = jnp.concatenate([w_ref[tap]] * side, axis=1)
                        gain_c = jnp.concatenate([w_ref[tap + 1]] * (side - 1), axis=1)
                        gain_r = jnp.concatenate([w_ref[tap + 2]] * side, axis=1)
                        left = left + window[:, : chunk + x_pad] * gain_l
                        centre = centre + window[:, x_pad : x_pad + chunk] * gain_c
                        right = right + window[:, x_pad:] * gain_r
                total = (
                    centre
                    + pltpu.roll(left, shift, 1)[:, :chunk]
                    + pltpu.roll(right, shift, 1)[:, :chunk]
                )
                for acc_ref in acc_refs:
                    total = total + acc_ref[plane, pl.ds(row, rows), pl.ds(base, chunk)].astype(
                        jnp.float32
                    )
                o_ref[plane, pl.ds(row, rows), pl.ds(base, chunk)] = total.astype(o_ref.dtype)
        return carry

    lax.fori_loop(0, count, body, 0)


def stencil_call(plan, inputs, accs, gains, y_cells, lanes, channels, out_dtype):
    chunk = min(1024, lanes)
    rows = 8 if y_cells % 8 == 0 else y_cells
    kernel = functools.partial(
        stencil_kernel, chunk, 2 * channels, y_cells, rows, plan, len(inputs), len(accs)
    )
    operands = list(inputs) + list(accs) + [gains]
    return pl.pallas_call(
        kernel,
        out_shape=jax.ShapeDtypeStruct((len(plan), y_cells, lanes), out_dtype),
    )(*operands)


def depthwise(rims, taps, flipped, x_cells, channels, out_dtype=jnp.float32, extra=()):
    inner, below, above = rims
    planes = inner.shape[0]
    y_cells = inner.shape[1] - 2
    lanes = x_cells * channels
    rows = 8 if y_cells % 8 == 0 else y_cells
    if flipped:
        taps = taps[::-1]
    gains = jnp.tile(taps.astype(jnp.float32), (1, 128 // channels))
    gains = jnp.broadcast_to(gains[:, None, :], (gains.shape[0], rows, 128))
    local_plan = tuple(
        tuple((0, plane + step_z - 1, step_z) for step_z in range(3) if 0 <= plane + step_z - 1 < planes)
        for plane in range(planes)
    )
    local_dtype = jnp.bfloat16 if flipped else jnp.float32
    local = stencil_call(local_plan, (inner,), (), gains, y_cells, lanes, channels, local_dtype)
    rim_plan = tuple(
        ((((0, 0, 0),) if plane == 0 else ()) + (((1, 0, 2),) if plane == planes - 1 else ()))
        for plane in range(planes)
    )
    accs = (local,) + tuple(extra)
    return stencil_call(rim_plan, (below, above), accs, gains, y_cells, lanes, channels, out_dtype)


def share_terms(field3, cos_table, sin_table):
    real_part = jnp.einsum("rxc,xk->krc", field3, cos_table, preferred_element_type=jnp.float32)
    imag_part = jnp.einsum("rxc,xk->krc", field3, sin_table, preferred_element_type=jnp.float32)
    return ring_reduce_scatter(jnp.concatenate([real_part, imag_part], axis=2), "gx")


def share_inverse(modes_share, cos_table, sin_table, channels):
    segment = ring_gather(modes_share, "gx")
    running = jnp.einsum(
        "krc,xk->rxc", segment[:, :, :channels], cos_table, preferred_element_type=jnp.float32
    )
    return running + jnp.einsum(
        "krc,xk->rxc", segment[:, :, channels:], sin_table, preferred_element_type=jnp.float32
    )


def split_gradients(dblock, channels):
    grad_real = dblock[:, :channels, :channels] + dblock[:, channels:, channels:]
    grad_imag = dblock[:, :channels, channels:] - dblock[:, channels:, :channels]
    return jnp.stack([grad_real, grad_imag])


def sum_gradients(local_grads):
    flat = local_grads.reshape(-1, 1024)
    return butterfly_sum(butterfly_sum(flat, "gy"), "gz").reshape(local_grads.shape)


def per_device(
    features, depth_weight, expand_weight, project_weight, spec_real, spec_imag, cotangent
):
    planes, y_cells, merged = features.shape
    channels = depth_weight.shape[1]
    x_cells = merged // channels
    row_count = planes * y_cells
    mode_count = spec_real.shape[0]
    group_size = lax.axis_size("gx")
    x_length = x_cells * group_size
    x_start = lax.axis_index("gx") * x_cells
    share_size = mode_count // group_size
    cos_part, sin_part = dft_tables(
        x_start, x_cells, x_length, jnp.arange(mode_count, dtype=jnp.int32)
    )
    order = gathered_order("gx", share_size)
    cos_order, sin_order = dft_tables(x_start, x_cells, x_length, order)
    cos_scaled = scaled_table(cos_order, order, x_length)
    sin_scaled = scaled_table(sin_order, order, x_length)
    cos_fwd_scaled = scaled_table(cos_part, jnp.arange(mode_count, dtype=jnp.int32), x_length)
    sin_fwd_scaled = scaled_table(sin_part, jnp.arange(mode_count, dtype=jnp.int32), x_length)
    blocks = block_weights(spec_real, spec_imag)
    padded = spatial_rims(features, channels)
    activation = depthwise(padded, depth_weight, False, x_cells, channels, jnp.bfloat16)
    field3 = features.reshape(row_count, x_cells, channels)
    owned_blocks = lax.dynamic_slice_in_dim(
        blocks, lax.axis_index("gx") * share_size, share_size, 0
    )
    coeffs = share_terms(field3, cos_part, sin_part).astype(jnp.bfloat16)
    mixed_modes = jnp.einsum(
        "krc,kco->kro", coeffs, owned_blocks, preferred_element_type=jnp.float32
    ).astype(jnp.bfloat16)
    mixed_modes, activation = lax.optimization_barrier((mixed_modes, activation))
    activation = activation.reshape(row_count * x_cells, channels)
    hidden_pre = jnp.dot(activation, expand_weight, preferred_element_type=jnp.float32)
    hidden, hidden_slope = gelu_parts(hidden_pre)
    local_branch = jnp.dot(
        hidden.astype(jnp.bfloat16), project_weight, preferred_element_type=jnp.float32
    )
    local_branch = local_branch.reshape(row_count, x_cells, channels)
    spectral = share_inverse(mixed_modes, cos_scaled, sin_scaled, channels)
    result, slopes = gelu_parts(local_branch + spectral)
    output = result.astype(jnp.bfloat16).reshape(planes, y_cells, merged)
    grad_pre = (
        lax.optimization_barrier(cotangent.reshape(row_count, x_cells, channels)).astype(jnp.float32)
        * slopes
    ).astype(jnp.bfloat16)
    hidden_grad = jnp.dot(
        grad_pre.reshape(row_count * x_cells, channels),
        project_weight.T,
        preferred_element_type=jnp.float32,
    )
    grad_hidden = (hidden_grad * hidden_slope).astype(jnp.bfloat16)
    grad_act = jnp.dot(grad_hidden, expand_weight.T, preferred_element_type=jnp.float32).astype(
        jnp.bfloat16
    )
    grad_act = grad_act.reshape(planes, y_cells, merged)
    dcoef = share_terms(grad_pre, cos_fwd_scaled, sin_fwd_scaled).astype(jnp.bfloat16)
    dmode = jnp.einsum(
        "kro,kco->krc", dcoef, owned_blocks, preferred_element_type=jnp.float32
    ).astype(jnp.bfloat16)
    dblock = jnp.einsum("krc,kro->kco", coeffs, dcoef, preferred_element_type=jnp.float32)
    local_grads = split_gradients(dblock, channels)
    dmode, local_grads, grad_act = lax.optimization_barrier((dmode, local_grads, grad_act))
    spectral_grad = share_inverse(dmode, cos_order, sin_order, channels)
    grad_spec = sum_gradients(local_grads)
    padded_grad = spatial_rims(grad_act, channels)
    grad_features = depthwise(
        padded_grad,
        depth_weight,
        True,
        x_cells,
        channels,
        jnp.bfloat16,
        (spectral_grad.astype(jnp.bfloat16).reshape(planes, y_cells, merged),),
    )
    return (output, grad_features, grad_spec)


def solution(mesh):
    placed = (P("gz", "gy", "gx"), P(), P(), P(), P(), P(), P("gz", "gy", "gx"))
    return jax.shard_map(
        per_device,
        mesh=mesh,
        in_specs=placed,
        out_specs=(P("gz", "gy", "gx"), P("gz", "gy", "gx"), P(None, "gx", None, None)),
        check_vma=False,
    )
```

```python
import functools
import math

import jax
import jax.numpy as jnp
from jax import lax
from jax.experimental import pallas as pl
from jax.experimental.pallas import tpu as pltpu
from jax.sharding import PartitionSpec as P


def padded_2(value, sides, width, wrap):
    for axis, dim in sides:
        size, length = (lax.axis_size(axis), value.shape[dim])
        last = lax.slice_in_dim(value, length - width, length, axis=dim)
        leading = lax.slice_in_dim(value, 0, width, axis=dim)
        if size == 2 and not wrap:
            first = lax.axis_index(axis) == 0
            swapped = lax.ppermute(jnp.where(first, last, leading), axis, [(0, 1), (1, 0)])
            zeros = jnp.zeros_like(swapped)
            before = jnp.where(first, zeros, swapped)
            after = jnp.where(first, swapped, zeros)
        else:
            up = [(i, (i + 1) % size) for i in range(size if wrap else size - 1)]
            down = [(j, i) for i, j in up]
            before = lax.ppermute(last, axis, up)
            after = lax.ppermute(leading, axis, down)
        value = jnp.concatenate([before, value, after], axis=dim)
    return value


def gelu_parts(values):
    normal_cdf = 0.5 * (1.0 + jax.scipy.special.erf(values * (1.0 / math.sqrt(2.0))))
    density = jnp.exp(-0.5 * values * values) * (1.0 / math.sqrt(2.0 * math.pi))
    return (values * normal_cdf, normal_cdf + values * density)


def dft_tables(offset, cells, x_length, frequency):
    position = offset + jnp.arange(cells, dtype=jnp.int32)
    phase_int = position[:, None] * frequency[None, :] % x_length
    angles = phase_int.astype(jnp.float32) * (2.0 * math.pi / x_length)
    return (jnp.cos(angles).astype(jnp.bfloat16), (-jnp.sin(angles)).astype(jnp.bfloat16))


def scaled_table(table, frequency, x_length):
    mode_scale = jnp.where(frequency == 0, 1.0, 2.0).astype(jnp.float32) / x_length
    return (table.astype(jnp.float32) * mode_scale[None, :]).astype(jnp.bfloat16)


def gathered_order(axis, share_size):
    size = lax.axis_size(axis)
    shifts = jnp.arange(size, dtype=jnp.int32)
    me = lax.axis_index(axis)
    if size & (size - 1):
        sources = (me - shifts) % size
    else:
        sources = jnp.bitwise_xor(me, shifts)
    local = jnp.arange(share_size, dtype=jnp.int32)
    return (sources[:, None] * share_size + local[None, :]).reshape(-1)


def ring_gather(block, axis):
    size = lax.axis_size(axis)
    if size & (size - 1) == 0:
        step = 1
        while step < size:
            block = jnp.concatenate(
                [block, lax.ppermute(block, axis, [(i, i ^ step) for i in range(size)])], axis=0
            )
            step *= 2
        return block
    pieces = [block]
    for shift in range(1, size):
        pieces.append(lax.ppermute(block, axis, [(i, (i + shift) % size) for i in range(size)]))
    return jnp.concatenate(pieces, axis=0)


def ring_reduce_scatter(value, axis):
    size = lax.axis_size(axis)
    share = value.shape[0] // size
    me = lax.axis_index(axis)
    if size & (size - 1) == 0:
        step = size // 2
        count = size
        while step >= 1:
            count //= 2
            upper = jnp.bitwise_and(me, step) != 0
            keep = lax.dynamic_slice_in_dim(value, jnp.where(upper, count, 0) * share, count * share, 0)
            send = lax.dynamic_slice_in_dim(value, jnp.where(upper, 0, count) * share, count * share, 0)
            value = keep + lax.ppermute(send, axis, [(i, i ^ step) for i in range(size)])
            step //= 2
        return value
    total = lax.dynamic_slice_in_dim(value, me * share, share, 0)
    for shift in range(1, size):
        piece = lax.dynamic_slice_in_dim(value, ((me + shift) % size) * share, share, 0)
        total = total + lax.ppermute(piece, axis, [(i, (i + shift) % size) for i in range(size)])
    return total


def butterfly_sum(value, axis):
    size = lax.axis_size(axis)
    if size & (size - 1):
        return lax.psum(value, axis)
    step = 1
    while step < size:
        value = value.astype(jnp.bfloat16)
        value = value.astype(jnp.float32) + lax.ppermute(
            value, axis, [(i, i ^ step) for i in range(size)]
        ).astype(jnp.float32)
        step *= 2
    return value


def block_weights(spec_real, spec_imag):
    upper_row = jnp.concatenate([spec_real, spec_imag], axis=2)
    lower_row = jnp.concatenate([-spec_imag, spec_real], axis=2)
    return jnp.concatenate([upper_row, lower_row], axis=1)


def spatial_rims(field_block, channels):
    x_wide = padded_2(field_block, (("gx", 2),), 2 * channels, True)
    inner = padded_2(x_wide, (("gy", 1),), 1, False)
    size = lax.axis_size("gz")
    up = [(i, i + 1) for i in range(size - 1)]
    down = [(j, i) for i, j in up]
    below = lax.ppermute(inner[-1:], "gz", up)
    above = lax.ppermute(inner[:1], "gz", down)
    return (inner, below, above)


def stencil_kernel(chunk, x_pad, y_cells, rows, plan, sources, has_acc, *refs):
    src_refs = refs[:sources]
    acc_refs = refs[sources : sources + has_acc]
    w_ref, o_ref = refs[sources + has_acc :]
    width = chunk + 2 * x_pad
    count = o_ref.shape[2] // chunk
    shift = chunk + x_pad - x_pad // 2
    side = (chunk + x_pad) // 128

    def body(index, carry):
        base = pl.multiple_of(index * chunk, chunk)
        for plane, terms in enumerate(plan):
            for row in range(0, y_cells, rows):
                left = jnp.zeros((rows, chunk + x_pad), jnp.float32)
                centre = jnp.zeros((rows, chunk), jnp.float32)
                right = jnp.zeros((rows, chunk + x_pad), jnp.float32)
                for source, source_plane, step_z in terms:
                    for step_y in range(3):
                        window = src_refs[source][
                            source_plane, pl.ds(row + step_y, rows), pl.ds(base, width)
                        ].astype(jnp.float32)
                        tap = 9 * step_z + 3 * step_y
                        gain_l = jnp.concatenate([w_ref[tap]] * side, axis=1)
                        gain_c = jnp.concatenate([w_ref[tap + 1]] * (side - 1), axis=1)
                        gain_r = jnp.concatenate([w_ref[tap + 2]] * side, axis=1)
                        left = left + window[:, : chunk + x_pad] * gain_l
                        centre = centre + window[:, x_pad : x_pad + chunk] * gain_c
                        right = right + window[:, x_pad:] * gain_r
                total = (
                    centre
                    + pltpu.roll(left, shift, 1)[:, :chunk]
                    + pltpu.roll(right, shift, 1)[:, :chunk]
                )
                for acc_ref in acc_refs:
                    total = total + acc_ref[plane, pl.ds(row, rows), pl.ds(base, chunk)].astype(
                        jnp.float32
                    )
                o_ref[plane, pl.ds(row, rows), pl.ds(base, chunk)] = total.astype(o_ref.dtype)
        return carry

    lax.fori_loop(0, count, body, 0)


def stencil_call(plan, inputs, accs, gains, y_cells, lanes, channels, out_dtype):
    chunk = min(2048, lanes)
    rows = 8 if y_cells % 8 == 0 else y_cells
    kernel = functools.partial(
        stencil_kernel, chunk, 2 * channels, y_cells, rows, plan, len(inputs), len(accs)
    )
    operands = list(inputs) + list(accs) + [gains]
    return pl.pallas_call(
        kernel,
        out_shape=jax.ShapeDtypeStruct((len(plan), y_cells, lanes), out_dtype),
    )(*operands)


def depthwise(rims, taps, flipped, x_cells, channels, out_dtype=jnp.float32, extra=()):
    inner, below, above = rims
    planes = inner.shape[0]
    y_cells = inner.shape[1] - 2
    lanes = x_cells * channels
    rows = 8 if y_cells % 8 == 0 else y_cells
    if flipped:
        taps = taps[::-1]
    gains = jnp.tile(taps.astype(jnp.float32), (1, 128 // channels))
    gains = jnp.broadcast_to(gains[:, None, :], (gains.shape[0], rows, 128))
    local_plan = tuple(
        tuple((0, plane + step_z - 1, step_z) for step_z in range(3) if 0 <= plane + step_z - 1 < planes)
        for plane in range(planes)
    )
    local_dtype = jnp.bfloat16 if flipped else jnp.float32
    local = stencil_call(local_plan, (inner,), (), gains, y_cells, lanes, channels, local_dtype)
    rim_plan = tuple(
        ((((0, 0, 0),) if plane == 0 else ()) + (((1, 0, 2),) if plane == planes - 1 else ()))
        for plane in range(planes)
    )
    accs = (local,) + tuple(extra)
    return stencil_call(rim_plan, (below, above), accs, gains, y_cells, lanes, channels, out_dtype)


def share_terms(field3, cos_table, sin_table):
    real_part = jnp.einsum("rxc,xk->krc", field3, cos_table, preferred_element_type=jnp.float32)
    imag_part = jnp.einsum("rxc,xk->krc", field3, sin_table, preferred_element_type=jnp.float32)
    return ring_reduce_scatter(jnp.concatenate([real_part, imag_part], axis=2), "gx")


def share_inverse(modes_share, cos_table, sin_table, channels):
    segment = ring_gather(modes_share, "gx")
    running = jnp.einsum(
        "krc,xk->rxc", segment[:, :, :channels], cos_table, preferred_element_type=jnp.float32
    )
    return running + jnp.einsum(
        "krc,xk->rxc", segment[:, :, channels:], sin_table, preferred_element_type=jnp.float32
    )


def split_gradients(dblock, channels):
    grad_real = dblock[:, :channels, :channels] + dblock[:, channels:, channels:]
    grad_imag = dblock[:, :channels, channels:] - dblock[:, channels:, :channels]
    return jnp.stack([grad_real, grad_imag])


def sum_gradients(local_grads):
    flat = local_grads.reshape(-1, 1024)
    return butterfly_sum(butterfly_sum(flat, "gy"), "gz").reshape(local_grads.shape)


def per_device(
    features, depth_weight, expand_weight, project_weight, spec_real, spec_imag, cotangent
):
    planes, y_cells, merged = features.shape
    channels = depth_weight.shape[1]
    x_cells = merged // channels
    row_count = planes * y_cells
    mode_count = spec_real.shape[0]
    group_size = lax.axis_size("gx")
    x_length = x_cells * group_size
    x_start = lax.axis_index("gx") * x_cells
    share_size = mode_count // group_size
    cos_part, sin_part = dft_tables(
        x_start, x_cells, x_length, jnp.arange(mode_count, dtype=jnp.int32)
    )
    order = gathered_order("gx", share_size)
    cos_order, sin_order = dft_tables(x_start, x_cells, x_length, order)
    cos_scaled = scaled_table(cos_order, order, x_length)
    sin_scaled = scaled_table(sin_order, order, x_length)
    cos_fwd_scaled = scaled_table(cos_part, jnp.arange(mode_count, dtype=jnp.int32), x_length)
    sin_fwd_scaled = scaled_table(sin_part, jnp.arange(mode_count, dtype=jnp.int32), x_length)
    blocks = block_weights(spec_real, spec_imag)
    padded = spatial_rims(features, channels)
    activation = depthwise(padded, depth_weight, False, x_cells, channels, jnp.bfloat16)
    field3 = features.reshape(row_count, x_cells, channels)
    owned_blocks = lax.dynamic_slice_in_dim(
        blocks, lax.axis_index("gx") * share_size, share_size, 0
    )
    coeffs = share_terms(field3, cos_part, sin_part).astype(jnp.bfloat16)
    mixed_modes = jnp.einsum(
        "krc,kco->kro", coeffs, owned_blocks, preferred_element_type=jnp.float32
    ).astype(jnp.bfloat16)
    mixed_modes, activation = lax.optimization_barrier((mixed_modes, activation))
    activation = activation.reshape(row_count * x_cells, channels)
    hidden_pre = jnp.dot(activation, expand_weight, preferred_element_type=jnp.float32)
    hidden, hidden_slope = gelu_parts(hidden_pre)
    local_branch = jnp.dot(
        hidden.astype(jnp.bfloat16), project_weight, preferred_element_type=jnp.float32
    )
    local_branch = local_branch.reshape(row_count, x_cells, channels)
    spectral = share_inverse(mixed_modes, cos_scaled, sin_scaled, channels)
    result, slopes = gelu_parts(local_branch + spectral)
    output = result.astype(jnp.bfloat16).reshape(planes, y_cells, merged)
    grad_pre = (
        lax.optimization_barrier(cotangent.reshape(row_count, x_cells, channels)).astype(jnp.float32)
        * slopes
    ).astype(jnp.bfloat16)
    hidden_grad = jnp.dot(
        grad_pre.reshape(row_count * x_cells, channels),
        project_weight.T,
        preferred_element_type=jnp.float32,
    )
    grad_hidden = (hidden_grad * hidden_slope).astype(jnp.bfloat16)
    grad_act = jnp.dot(grad_hidden, expand_weight.T, preferred_element_type=jnp.float32).astype(
        jnp.bfloat16
    )
    grad_act = grad_act.reshape(planes, y_cells, merged)
    dcoef = share_terms(grad_pre, cos_fwd_scaled, sin_fwd_scaled).astype(jnp.bfloat16)
    dmode = jnp.einsum(
        "kro,kco->krc", dcoef, owned_blocks, preferred_element_type=jnp.float32
    ).astype(jnp.bfloat16)
    dblock = jnp.einsum("krc,kro->kco", coeffs, dcoef, preferred_element_type=jnp.float32)
    local_grads = split_gradients(dblock, channels)
    dmode, local_grads, grad_act = lax.optimization_barrier((dmode, local_grads, grad_act))
    spectral_grad = share_inverse(dmode, cos_order, sin_order, channels)
    grad_spec = sum_gradients(local_grads)
    padded_grad = spatial_rims(grad_act, channels)
    grad_features = depthwise(
        padded_grad,
        depth_weight,
        True,
        x_cells,
        channels,
        jnp.bfloat16,
        (spectral_grad.astype(jnp.bfloat16).reshape(planes, y_cells, merged),),
    )
    return (output, grad_features, grad_spec)


def solution(mesh):
    placed = (P("gz", "gy", "gx"), P(), P(), P(), P(), P(), P("gz", "gy", "gx"))
    return jax.shard_map(
        per_device,
        mesh=mesh,
        in_specs=placed,
        out_specs=(P("gz", "gy", "gx"), P("gz", "gy", "gx"), P(None, "gx", None, None)),
        check_vma=False,
    )
```
